128 devices in a mesh: px: 8 (over z, core), py: 16 (over x, y).
Axes of the slice: x: 4, y: 4, z: 4, core: 2. Of those that a mesh axis runs over, the one named last changes fastest.
Arguments:
- nodes: bfloat16 [8, 16, 2048, 256], P('px', 'py'), may hold values from -6 to 80
- tile_src: int32 [8, 16, 16, 4], P('px', 'py'), may hold values from 0 to 79
- tile_mask: int32 [8, 16, 16, 4, 128, 128], P('px', 'py'), may hold values 0 or 1
- tokens: bfloat16 [128, 2048, 256], P(('px', 'py')), may hold values from -6 to 16
- tok_count: int32 [128, 128], P(None, ('px', 'py')), may hold values from 1 to 16, as said below
- w_e1: bfloat16 [256, 256], replicated, may hold values from -0.375 to 0.375
- w_e2: bfloat16 [256, 256], replicated, may hold values from -0.375 to 0.375
- w_n1: bfloat16 [512, 256], replicated, may hold values from -0.25 to 0.25
- w_n2: bfloat16 [256, 256], replicated, may hold values from -0.375 to 0.375
- w_q: bfloat16 [256, 256], replicated
- w_kv: bfloat16 [256, 512], replicated
- w_o: bfloat16 [256, 256], replicated, may hold values from -0.375 to 0.375
- cotangent: bfloat16 [8, 16, 2048, 256], P('px', 'py'), may hold values from -6 to 6
Outputs:
- grad_nodes: bfloat16 [8, 16, 2048, 256], P('px', 'py')
- grad_tokens: bfloat16 [128, 2048, 256], P(('px', 'py'))
The draws below stay inside these ranges and needn't reach their ends.
Inputs may be any that keep to these rules, and one draw needn't show every extreme that they name: tok_count[s, e] slots of the 16 that device s holds for partition e are live, the first ones; every device's own slots for its own partition are all live.
All inputs are finite; a program needn't handle non-finite values. No bound on the sum of `tile_mask` on one device may be relied on, other than what follows from the above.
Results may differ from the reference program's by a relative error of at most 0.025.
Values may be sent and summed in bfloat16 or wider, within the bound.
No kernel may reach another device: no remote copies, remote signals or barrier semaphores. Data moves between devices by JAX's collectives and lax.ppermute only.
A program may use at most 128 MiB of HBM per device.

```python
import math
import jax
import jax.numpy as jnp
from jax import lax

L = 256
HID = 256
BLK = 128
KT = 4
NBD = 16
TS = 16
DEV = 128
NN = 2048
NK = 2048
N_PX = 8
N_PY = 16


def draw_tok_count(key, part):
    drawn = jax.random.randint(key, (DEV, DEV), 1, TS + 1)
    diagonal = jnp.eye(DEV, dtype=jnp.int32)
    return jnp.where(diagonal > 0, TS, drawn).astype(jnp.int32)


def drawn_normal(key, extent):
    return jax.random.truncated_normal(key, -6.0, 6.0, extent, jnp.float32)


def draw_nodes(key, part):
    extent = (N_PX, N_PY, NN, L)
    own_key = jax.random.fold_in(key, 21)
    values = drawn_normal(own_key, extent)
    return values.astype(jnp.bfloat16)


def draw_tokens(key, part):
    extent = (DEV, NK, L)
    own_key = jax.random.fold_in(key, 23)
    values = drawn_normal(own_key, extent)
    return values.astype(jnp.bfloat16)


def draw_w_q(key, part):
    extent = (L, L)
    own_key = jax.random.fold_in(key, 11)
    values = drawn_normal(own_key, extent) / math.sqrt(L)
    return values.astype(jnp.bfloat16)


def draw_w_kv(key, part):
    extent = (L, 2 * L)
    own_key = jax.random.fold_in(key, 13)
    values = drawn_normal(own_key, extent) / math.sqrt(L)
    return values.astype(jnp.bfloat16)


def place_ends(result, stream_key, least, largest):
    index_at = [jax.random.randint(jax.random.fold_in(stream_key, axis), (), 0, length) for axis, length in enumerate(result.shape)]
    main_axis = result.shape.index(max(result.shape))
    beside = index_at[:main_axis] + [(index_at[main_axis] + 1) % result.shape[main_axis]] + index_at[main_axis + 1:]
    return result.at[tuple(index_at)].set(least).at[tuple(beside)].set(largest)


def block_scale(rng, shape, split, least, high):
    def one(dim, shards_of):
        steps = jax.random.uniform(jax.random.fold_in(jax.random.fold_in(rng, 6), dim), (shards_of,), jnp.float32, least / len(split), high / len(split))
        return jnp.repeat(jnp.exp(steps), shape[dim] // shards_of).reshape((-1,) + (1,) * (len(shape) - dim - 1))

    factor_of = one(*split[0])
    for cut in split[1:]:
        factor_of = factor_of * one(*cut)
    return factor_of


def centred(rng, shape, deviation, most, pieces=(), kind=jnp.bfloat16):
    loudness = block_scale(rng, shape, pieces, -0.22, 0.18) if pieces else 1.0
    entries = jax.random.normal(rng, shape, jnp.float32) * deviation * loudness
    return jnp.minimum(jnp.maximum(entries, -most), most).astype(kind)


def setup_inputs(seed: int = 0) -> dict:
    streams_of = jax.random.split(jax.random.key(seed), 14)
    nodes = draw_nodes(jax.random.fold_in(streams_of[13], 71), 0)
    tile_src = place_ends(jax.random.randint(streams_of[1], (N_PX, N_PY, NBD, KT), 0, 5 * NBD), jax.random.fold_in(streams_of[1], 1), 0, (5 * NBD) - 1).astype(jnp.int32)
    tile_mask = place_ends((jax.random.randint(streams_of[2], (N_PX, N_PY, NBD, KT, BLK, BLK), 0, BLK) < 3).astype(jnp.int32), jax.random.fold_in(streams_of[2], 1), 0, 1)
    tokens = draw_tokens(jax.random.fold_in(streams_of[13], 71), 0)
    tok_count = draw_tok_count(jax.random.fold_in(streams_of[13], 71), 0)
    w_e1 = centred(streams_of[5], (L, HID), L ** -0.5, 0.375)
    w_e2 = centred(streams_of[6], (HID, L), HID ** -0.5, 0.375)
    w_n1 = centred(streams_of[7], (2 * L, HID), (2 * L) ** -0.5, 0.25)
    w_n2 = centred(streams_of[8], (HID, L), HID ** -0.5, 0.375)
    w_q = draw_w_q(jax.random.fold_in(streams_of[13], 71), 0)
    w_kv = draw_w_kv(jax.random.fold_in(streams_of[13], 71), 0)
    w_o = centred(streams_of[11], (L, L), L ** -0.5, 0.375)
    cotangent = centred(streams_of[12], (N_PX, N_PY, NN, L), 1.0, 6.0, ((0, 8), (1, 16)))
    return dict(nodes=nodes, tile_src=tile_src, tile_mask=tile_mask, tokens=tokens, tok_count=tok_count, w_e1=w_e1, w_e2=w_e2, w_n1=w_n1, w_n2=w_n2, w_q=w_q, w_kv=w_kv, w_o=w_o, cotangent=cotangent)


def dense(left, right):
    return jnp.dot(left, right, preferred_element_type=jnp.float32)

def silu_slope(values):
    sigma = jax.nn.sigmoid(values)
    return sigma * (1.0 + values * (1.0 - sigma))

def reference(nodes, tile_src, tile_mask, tokens, tok_count, w_e1, w_e2, w_n1, w_n2, w_q, w_kv, w_o, cotangent):
    flat_nodes = nodes.reshape(DEV, NN, L)
    flat_cot = cotangent.reshape(DEV, NN, L)
    flat_src = tile_src.reshape(DEV, NBD, KT)
    flat_mask = tile_mask.reshape(DEV, NBD, KT, BLK, BLK)
    score_scale = 1.0 / math.sqrt(L)

    def edge_front(latent):
        activation = jax.nn.silu(dense(latent, w_e1)).astype(jnp.bfloat16)
        return dense(activation, w_e2).astype(jnp.bfloat16)
    message = lax.map(edge_front, flat_nodes).reshape(N_PX, N_PY, NN, L)
    padded = jnp.pad(message, ((1, 1), (1, 1), (0, 0), (0, 0)))
    sources = jnp.stack([padded[1:-1, 1:-1], padded[:-2, 1:-1], padded[2:, 1:-1], padded[1:-1, :-2], padded[1:-1, 2:]], axis=2).reshape(DEV, 5 * NBD, BLK, L)

    def node_front(inputs):
        latent, source, picked_ids, tile_bits = inputs
        picked = source[picked_ids].astype(jnp.float32)
        gathered = jnp.einsum('bkij,bkjl->bil', tile_bits.astype(jnp.float32), picked, precision=lax.Precision.HIGHEST)
        gathered = gathered.reshape(NN, L).astype(jnp.bfloat16)
        zvalue = dense(latent, w_n1[:L]) + dense(gathered, w_n1[L:])
        hidden = jax.nn.silu(zvalue).astype(jnp.bfloat16)
        updated = (latent.astype(jnp.float32) + dense(hidden, w_n2)).astype(jnp.bfloat16)
        return (dense(updated, w_q).astype(jnp.bfloat16), zvalue)
    queries, zvalues = lax.map(node_front, (flat_nodes, sources, flat_src, flat_mask))
    keyvals = dense(tokens.reshape(-1, L), w_kv).astype(jnp.bfloat16).reshape(DEV, DEV, TS, 2 * L)
    arrived = jnp.transpose(keyvals, (1, 0, 2, 3)).reshape(DEV, NK, 2 * L)
    counts_in = jnp.transpose(tok_count)

    def attend_back(inputs):
        query_rows, cot_rows, kv_rows, counts = inputs
        key_rows = kv_rows[:, :L]
        value_rows = kv_rows[:, L:]
        live_keys = (jnp.arange(TS)[None, :] < counts[:, None]).reshape(-1)
        scores = dense(query_rows, key_rows.T) * score_scale
        scores = jnp.where(live_keys[None, :], scores, -jnp.inf)
        highest = lax.optimization_barrier(jnp.max(scores, axis=1, keepdims=True))
        expo_terms = jnp.exp(scores - highest)
        probability = expo_terms / lax.optimization_barrier(jnp.sum(expo_terms, axis=1, keepdims=True))
        prob_low = probability.astype(jnp.bfloat16)
        grad_out = dense(cot_rows, w_o.T).astype(jnp.bfloat16)
        grad_prob = dense(grad_out, value_rows.T)
        grad_vals = dense(prob_low.T, grad_out)
        spread = lax.optimization_barrier(jnp.sum(probability * grad_prob, axis=1, keepdims=True))
        grad_score = (probability * (grad_prob - spread) * score_scale).astype(jnp.bfloat16)
        grad_query = dense(grad_score, key_rows).astype(jnp.bfloat16)
        grad_keys = dense(grad_score.T, query_rows)
        grad_kv = jnp.concatenate([grad_keys, grad_vals], axis=1).astype(jnp.bfloat16)
        return (grad_query, grad_kv)
    grad_queries, grad_kvs = lax.map(attend_back, (queries, flat_cot, arrived, counts_in))
    returned = jnp.transpose(grad_kvs.reshape(DEV, DEV, TS, 2 * L), (1, 0, 2, 3)).reshape(-1, 2 * L)
    grad_tokens = dense(returned, w_kv.T).astype(jnp.bfloat16).reshape(DEV, NK, L)

    def node_back(inputs):
        zvalue, cot_rows, grad_query = inputs
        grad_update = cot_rows.astype(jnp.float32) + dense(grad_query, w_q.T)
        update_low = grad_update.astype(jnp.bfloat16)
        grad_z = (dense(update_low, w_n2.T) * silu_slope(zvalue)).astype(jnp.bfloat16)
        grad_agg = dense(grad_z, w_n1[L:].T).astype(jnp.bfloat16)
        grad_node = grad_update + dense(grad_z, w_n1[:L].T)
        return (grad_node, grad_agg)
    grad_nodes_part, grad_aggs = lax.map(node_back, (zvalues, flat_cot, grad_queries))

    def tile_back(inputs):
        grad_agg, picked_ids, tile_bits = inputs
        grad_parts = jnp.einsum('bkij,bil->bkjl', tile_bits.astype(jnp.float32), grad_agg.reshape(NBD, BLK, L).astype(jnp.float32), precision=lax.Precision.HIGHEST)
        grad_src = jax.ops.segment_sum(grad_parts.reshape(NBD * KT, BLK, L), picked_ids.reshape(-1).astype(jnp.int32), num_segments=5 * NBD).reshape(5, NN, L)
        return (grad_src[0], grad_src[1:].astype(jnp.bfloat16))
    own_part, outbound = lax.map(tile_back, (grad_aggs, flat_src, flat_mask))
    own_part = own_part.reshape(N_PX, N_PY, NN, L)
    outbound = outbound.reshape(N_PX, N_PY, 4, NN, L).astype(jnp.float32)
    zero_row = jnp.zeros((1, N_PY, NN, L), jnp.float32)
    zero_col = jnp.zeros((N_PX, 1, NN, L), jnp.float32)
    from_next_px = jnp.concatenate([outbound[1:, :, 0], zero_row], axis=0)
    from_prev_px = jnp.concatenate([zero_row, outbound[:-1, :, 1]], axis=0)
    from_next_py = jnp.concatenate([outbound[:, 1:, 2], zero_col], axis=1)
    from_prev_py = jnp.concatenate([zero_col, outbound[:, :-1, 3]], axis=1)
    grad_msg = (own_part + from_next_px + from_prev_px + from_next_py + from_prev_py).astype(jnp.bfloat16)

    def edge_back(inputs):
        latent, grad_msg_rows, grad_node = inputs
        pre_act = dense(latent, w_e1)
        grad_pre = (dense(grad_msg_rows, w_e2.T) * silu_slope(pre_act)).astype(jnp.bfloat16)
        return (grad_node + dense(grad_pre, w_e1.T)).astype(jnp.bfloat16)
    grad_nodes = lax.map(edge_back, (flat_nodes, grad_msg.reshape(DEV, NN, L), grad_nodes_part))
    return (grad_nodes.reshape(N_PX, N_PY, NN, L), grad_tokens)
```

```python
import math

import jax
import jax.numpy as jnp
from jax import lax
from jax.sharding import PartitionSpec as P


def with_halo(block, sides, width):
    for axis, dim in sides:
        count = lax.axis_size(axis)
        forward = [(i, i + 1) for i in range(count - 1)]
        backward = [(target, source) for source, target in forward]
        low = lax.ppermute(
            lax.slice_in_dim(block, block.shape[dim] - width, None, axis=dim), axis, forward
        )
        high = lax.ppermute(lax.slice_in_dim(block, 0, width, axis=dim), axis, backward)
        block = jnp.concatenate([low, block, high], axis=dim)
    return block


def passed_along(value, axis, steps):
    count = lax.axis_size(axis)
    leading, last = (max(0, -steps), min(count, count - steps))
    return lax.ppermute(value, axis, [(source, source + steps) for source in range(leading, last)])


def dense(left, right):
    return jnp.dot(left, right, preferred_element_type=jnp.float32)


def silu_slope(values):
    sigma = jax.nn.sigmoid(values)
    return sigma * (1.0 + values * (1.0 - sigma))


def on_device(
    nodes, tile_src, tile_mask, tokens, tok_count, w_e1, w_e2, w_n1, w_n2, w_q, w_kv, w_o, cotangent
):
    latent = nodes[0, 0]
    node_rows = latent.shape[0]
    latent_width = latent.shape[1]
    block_count = tile_src.shape[2]
    tile_count = tile_src.shape[3]
    blk_rows = tile_mask.shape[-1]
    rows_px = lax.axis_size("px")
    rows_py = lax.axis_size("py")
    devices = rows_px * rows_py
    score_scale = 1.0 / math.sqrt(latent_width)
    pre_act = dense(latent, w_e1)
    activation = jax.nn.silu(pre_act).astype(jnp.bfloat16)
    message = dense(activation, w_e2).astype(jnp.bfloat16)
    sources = jnp.stack(
        [
            message,
            passed_along(message, "px", 1),
            passed_along(message, "px", -1),
            passed_along(message, "py", 1),
            passed_along(message, "py", -1),
        ]
    )
    picked_ids = tile_src[0, 0]
    tile_bf16 = tile_mask[0, 0].astype(jnp.bfloat16)
    picked = sources.reshape(5 * block_count, blk_rows, latent_width)[picked_ids]
    gathered = jnp.einsum("bkij,bkjl->bil", tile_bf16, picked, preferred_element_type=jnp.float32)
    gathered = gathered.reshape(node_rows, latent_width).astype(jnp.bfloat16)
    zvalue = dense(latent, w_n1[:latent_width]) + dense(gathered, w_n1[latent_width:])
    hidden = jax.nn.silu(zvalue).astype(jnp.bfloat16)
    updated = (latent.astype(jnp.float32) + dense(hidden, w_n2)).astype(jnp.bfloat16)
    queries = dense(updated, w_q).astype(jnp.bfloat16)
    own_tokens = tokens[0]
    slot_count = own_tokens.shape[0] // devices
    token_groups = own_tokens.reshape(devices, slot_count, latent_width)
    arrived_tokens = lax.all_to_all(
        token_groups, ("px", "py"), split_axis=0, concat_axis=0, tiled=True
    )
    arrived_tokens = arrived_tokens.reshape(devices * slot_count, latent_width)
    arrived = dense(arrived_tokens, w_kv).astype(jnp.bfloat16)
    key_rows = arrived[:, :latent_width]
    value_rows = arrived[:, latent_width:]
    live_keys = (jnp.arange(slot_count)[None, :] < tok_count[:, 0][:, None]).reshape(-1)
    scores = (
        jnp.einsum("nl,kl->nk", queries, key_rows, preferred_element_type=jnp.float32) * score_scale
    )
    scores = jnp.where(live_keys[None, :], scores, -jnp.inf)
    highest = jnp.max(scores, axis=1, keepdims=True)
    expo_terms = jnp.exp(scores - highest)
    probability = expo_terms / jnp.sum(expo_terms, axis=1, keepdims=True)
    prob_low = probability.astype(jnp.bfloat16)
    grad_out = dense(cotangent[0, 0], w_o.T).astype(jnp.bfloat16)
    grad_prob = jnp.einsum("nl,kl->nk", grad_out, value_rows, preferred_element_type=jnp.float32)
    grad_vals = jnp.einsum("nk,nl->kl", prob_low, grad_out, preferred_element_type=jnp.float32)
    spread = jnp.sum(probability * grad_prob, axis=1, keepdims=True)
    grad_score = (probability * (grad_prob - spread) * score_scale).astype(jnp.bfloat16)
    grad_query = dense(grad_score, key_rows).astype(jnp.bfloat16)
    grad_keys = jnp.einsum("nk,nl->kl", grad_score, queries, preferred_element_type=jnp.float32)
    grad_kv = jnp.concatenate([grad_keys, grad_vals], axis=1).astype(jnp.bfloat16)
    grad_slots = dense(grad_kv, w_kv.T).astype(jnp.bfloat16)
    returned = lax.all_to_all(
        grad_slots.reshape(devices, slot_count, latent_width),
        ("px", "py"),
        split_axis=0,
        concat_axis=0,
        tiled=True,
    )
    grad_tokens = returned.reshape(devices * slot_count, latent_width)
    grad_update = cotangent[0, 0].astype(jnp.float32) + dense(grad_query, w_q.T)
    update_low = grad_update.astype(jnp.bfloat16)
    grad_z = (dense(update_low, w_n2.T) * silu_slope(zvalue)).astype(jnp.bfloat16)
    grad_agg = dense(grad_z, w_n1[latent_width:].T).astype(jnp.bfloat16)
    grad_node = grad_update + dense(grad_z, w_n1[:latent_width].T)
    grad_parts = jnp.einsum(
        "bkij,bil->bkjl",
        tile_bf16,
        grad_agg.reshape(block_count, blk_rows, latent_width),
        preferred_element_type=jnp.float32,
    )
    grad_src = jax.ops.segment_sum(
        grad_parts.reshape(block_count * tile_count, blk_rows, latent_width),
        picked_ids.reshape(-1),
        num_segments=5 * block_count,
    )
    grad_src = grad_src.reshape(5, node_rows, latent_width)
    outbound = grad_src[1:].astype(jnp.bfloat16)
    collected = grad_src[0]
    for member, offset in ((0, -1), (1, 1)):
        collected = collected + passed_along(outbound[member], "px", offset).astype(jnp.float32)
    for member, offset in ((2, -1), (3, 1)):
        collected = collected + passed_along(outbound[member], "py", offset).astype(jnp.float32)
    grad_msg = collected.astype(jnp.bfloat16)
    grad_pre = (dense(grad_msg, w_e2.T) * silu_slope(pre_act)).astype(jnp.bfloat16)
    grad_nodes = (grad_node + dense(grad_pre, w_e1.T)).astype(jnp.bfloat16)
    return (grad_nodes[None, None], grad_tokens[None])


def solution(mesh):
    return jax.shard_map(
        on_device,
        mesh=mesh,
        in_specs=(
            P("px", "py", None, None),
            P("px", "py", None, None),
            P("px", "py", None, None, None, None),
            P(("px", "py"), None, None),
            P(None, ("px", "py")),
            P(),
            P(),
            P(),
            P(),
            P(),
            P(),
            P(),
            P("px", "py", None, None),
        ),
        out_specs=(P("px", "py", None, None), P(("px", "py"), None, None)),
        check_vma=False,
    )
```

```python
import math

import jax
import jax.numpy as jnp
from jax import lax
from jax.sharding import PartitionSpec as P


def with_halo(block, sides, width):
    for axis, dim in sides:
        count = lax.axis_size(axis)
        forward = [(i, i + 1) for i in range(count - 1)]
        backward = [(target, source) for source, target in forward]
        low = lax.ppermute(
            lax.slice_in_dim(block, block.shape[dim] - width, None, axis=dim), axis, forward
        )
        high = lax.ppermute(lax.slice_in_dim(block, 0, width, axis=dim), axis, backward)
        block = jnp.concatenate([low, block, high], axis=dim)
    return block


def passed_along(value, axis, steps):
    count = lax.axis_size(axis)
    leading, last = (max(0, -steps), min(count, count - steps))
    return lax.ppermute(value, axis, [(source, source + steps) for source in range(leading, last)])


def exchange_slots(groups, inner, outer):
    staged = jnp.swapaxes(groups, 0, 1)
    staged = lax.all_to_all(staged, inner, split_axis=0, concat_axis=0, tiled=True)
    staged = jnp.swapaxes(staged, 0, 1)
    return lax.all_to_all(staged, outer, split_axis=0, concat_axis=0, tiled=True)


def dense(left, right):
    return jnp.dot(left, right, preferred_element_type=jnp.float32)


def silu_slope(values):
    sigma = jax.nn.sigmoid(values)
    return sigma * (1.0 + values * (1.0 - sigma))


def on_device(
    nodes, tile_src, tile_mask, tokens, tok_count, w_e1, w_e2, w_n1, w_n2, w_q, w_kv, w_o, cotangent
):
    latent = nodes[0, 0]
    node_rows = latent.shape[0]
    latent_width = latent.shape[1]
    block_count = tile_src.shape[2]
    tile_count = tile_src.shape[3]
    blk_rows = tile_mask.shape[-1]
    rows_px = lax.axis_size("px")
    rows_py = lax.axis_size("py")
    devices = rows_px * rows_py
    score_scale = 1.0 / math.sqrt(latent_width)
    pre_act = dense(latent, w_e1)
    activation = jax.nn.silu(pre_act).astype(jnp.bfloat16)
    message = dense(activation, w_e2).astype(jnp.bfloat16)
    sources = jnp.stack(
        [
            message,
            passed_along(message, "px", 1),
            passed_along(message, "px", -1),
            passed_along(message, "py", 1),
            passed_along(message, "py", -1),
        ]
    )
    picked_ids = tile_src[0, 0]
    tile_bf16 = tile_mask[0, 0].astype(jnp.bfloat16)
    picked = sources.reshape(5 * block_count, blk_rows, latent_width)[picked_ids]
    gathered = jnp.einsum("bkij,bkjl->bil", tile_bf16, picked, preferred_element_type=jnp.float32)
    gathered = gathered.reshape(node_rows, latent_width).astype(jnp.bfloat16)
    zvalue = dense(latent, w_n1[:latent_width]) + dense(gathered, w_n1[latent_width:])
    hidden = jax.nn.silu(zvalue).astype(jnp.bfloat16)
    updated = (latent.astype(jnp.float32) + dense(hidden, w_n2)).astype(jnp.bfloat16)
    queries = dense(updated, w_q).astype(jnp.bfloat16)
    own_tokens = tokens[0]
    slot_count = own_tokens.shape[0] // devices
    token_groups = own_tokens.reshape(rows_px, rows_py, slot_count, latent_width)
    arrived_tokens = exchange_slots(token_groups, "py", "px")
    arrived_tokens = arrived_tokens.reshape(devices * slot_count, latent_width)
    arrived = dense(arrived_tokens, w_kv).astype(jnp.bfloat16)
    key_rows = arrived[:, :latent_width]
    value_rows = arrived[:, latent_width:]
    live_keys = (jnp.arange(slot_count)[None, :] < tok_count[:, 0][:, None]).reshape(-1)
    scores = (
        jnp.einsum("nl,kl->nk", queries, key_rows, preferred_element_type=jnp.float32) * score_scale
    )
    scores = jnp.where(live_keys[None, :], scores, -jnp.inf)
    highest = jnp.max(scores, axis=1, keepdims=True)
    expo_terms = jnp.exp(scores - highest)
    probability = expo_terms / jnp.sum(expo_terms, axis=1, keepdims=True)
    prob_low = probability.astype(jnp.bfloat16)
    grad_out = dense(cotangent[0, 0], w_o.T).astype(jnp.bfloat16)
    grad_prob = jnp.einsum("nl,kl->nk", grad_out, value_rows, preferred_element_type=jnp.float32)
    grad_vals = jnp.einsum("nk,nl->kl", prob_low, grad_out, preferred_element_type=jnp.float32)
    spread = jnp.sum(probability * grad_prob, axis=1, keepdims=True)
    grad_score = (probability * (grad_prob - spread) * score_scale).astype(jnp.bfloat16)
    grad_query = dense(grad_score, key_rows).astype(jnp.bfloat16)
    grad_keys = jnp.einsum("nk,nl->kl", grad_score, queries, preferred_element_type=jnp.float32)
    grad_kv = jnp.concatenate([grad_keys, grad_vals], axis=1).astype(jnp.bfloat16)
    grad_slots = dense(grad_kv, w_kv.T).astype(jnp.bfloat16)
    returned = exchange_slots(
        grad_slots.reshape(rows_px, rows_py, slot_count, latent_width), "py", "px"
    )
    grad_tokens = returned.reshape(devices * slot_count, latent_width)
    grad_update = cotangent[0, 0].astype(jnp.float32) + dense(grad_query, w_q.T)
    update_low = grad_update.astype(jnp.bfloat16)
    grad_z = (dense(update_low, w_n2.T) * silu_slope(zvalue)).astype(jnp.bfloat16)
    grad_agg = dense(grad_z, w_n1[latent_width:].T).astype(jnp.bfloat16)
    grad_node = grad_update + dense(grad_z, w_n1[:latent_width].T)
    grad_parts = jnp.einsum(
        "bkij,bil->bkjl",
        tile_bf16,
        grad_agg.reshape(block_count, blk_rows, latent_width),
        preferred_element_type=jnp.float32,
    )
    grad_src = jax.ops.segment_sum(
        grad_parts.reshape(block_count * tile_count, blk_rows, latent_width),
        picked_ids.reshape(-1),
        num_segments=5 * block_count,
    )
    grad_src = grad_src.reshape(5, node_rows, latent_width)
    outbound = grad_src[1:].astype(jnp.bfloat16)
    collected = grad_src[0]
    for member, offset in ((0, -1), (1, 1)):
        collected = collected + passed_along(outbound[member], "px", offset).astype(jnp.float32)
    for member, offset in ((2, -1), (3, 1)):
        collected = collected + passed_along(outbound[member], "py", offset).astype(jnp.float32)
    grad_msg = collected.astype(jnp.bfloat16)
    grad_pre = (dense(grad_msg, w_e2.T) * silu_slope(pre_act)).astype(jnp.bfloat16)
    grad_nodes = (grad_node + dense(grad_pre, w_e1.T)).astype(jnp.bfloat16)
    return (grad_nodes[None, None], grad_tokens[None])


def solution(mesh):
    return jax.shard_map(
        on_device,
        mesh=mesh,
        in_specs=(
            P("px", "py", None, None),
            P("px", "py", None, None),
            P("px", "py", None, None, None, None),
            P(("px", "py"), None, None),
            P(None, ("px", "py")),
            P(),
            P(),
            P(),
            P(),
            P(),
            P(),
            P(),
            P("px", "py", None, None),
        ),
        out_specs=(P("px", "py", None, None), P(("px", "py"), None, None)),
        check_vma=False,
    )
```

```python
import math

import jax
import jax.numpy as jnp
from jax import lax
from jax.experimental import pallas as pl
from jax.experimental.pallas import tpu as pltpu
from jax.sharding import PartitionSpec as P


def with_halo(block, sides, width):
    for axis, dim in sides:
        count = lax.axis_size(axis)
        forward = [(i, i + 1) for i in range(count - 1)]
        backward = [(target, source) for source, target in forward]
        low = lax.ppermute(
            lax.slice_in_dim(block, block.shape[dim] - width, None, axis=dim), axis, forward
        )
        high = lax.ppermute(lax.slice_in_dim(block, 0, width, axis=dim), axis, backward)
        block = jnp.concatenate([low, block, high], axis=dim)
    return block


def passed_along(value, axis, steps):
    count = lax.axis_size(axis)
    leading, last = (max(0, -steps), min(count, count - steps))
    return lax.ppermute(value, axis, [(source, source + steps) for source in range(leading, last)])


def gather_kernel(src_ids, mask_ref, own, up, down, left, right, out_ref):
    b = pl.program_id(0)
    tiles = mask_ref.shape[1]
    per_side = own.shape[0]
    total = jnp.zeros(out_ref.shape, jnp.float32)
    for k in range(tiles):
        picked = src_ids[b * tiles + k]
        side = picked // per_side
        block = picked % per_side
        bits = mask_ref[0, k].astype(jnp.float32).astype(jnp.bfloat16)
        rows = own[block]
        for index, ref in enumerate((up, down, left, right)):
            rows = jnp.where(side == index + 1, ref[block], rows)
        total = total + jnp.dot(bits, rows, preferred_element_type=jnp.float32)
    out_ref[...] = total.astype(out_ref.dtype)


def tile_gather(src_ids, tile_mask, sources):
    blocks, tiles, blk, _ = tile_mask.shape
    width = sources[0].shape[-1]
    whole = pl.BlockSpec((blocks, blk, width), lambda b, ids: (0, 0, 0))
    return pl.pallas_call(
        gather_kernel,
        grid_spec=pltpu.PrefetchScalarGridSpec(
            num_scalar_prefetch=1,
            grid=(blocks,),
            in_specs=[pl.BlockSpec((1, tiles, blk, blk), lambda b, ids: (b, 0, 0, 0))]
            + [whole] * len(sources),
            out_specs=pl.BlockSpec((blk, width), lambda b, ids: (b, 0)),
        ),
        out_shape=jax.ShapeDtypeStruct((blocks * blk, width), jnp.bfloat16),
    )(src_ids, tile_mask, *sources)


def scatter_kernel(src_ids, mask_ref, grad_ref, own_ref, out_ref, total):
    b = pl.program_id(0)
    tiles = mask_ref.shape[1]
    per_side = own_ref.shape[0]

    @pl.when(b == 0)
    def _():
        total[...] = jnp.zeros(total.shape, jnp.float32)

    grad_rows = grad_ref[...]
    for k in range(tiles):
        picked = src_ids[b * tiles + k]
        bits = mask_ref[0, k].astype(jnp.float32).T.astype(jnp.bfloat16)
        total[picked] += jnp.dot(bits, grad_rows, preferred_element_type=jnp.float32)

    @pl.when(b == pl.num_programs(0) - 1)
    def _():
        own_ref[...] = total[0:per_side]
        for side in range(out_ref.shape[0]):
            start = (side + 1) * per_side
            out_ref[side] = total[start : start + per_side].astype(out_ref.dtype)


def tile_scatter(src_ids, tile_mask, grad_agg, sides):
    blocks, tiles, blk, _ = tile_mask.shape
    width = grad_agg.shape[-1]
    return pl.pallas_call(
        scatter_kernel,
        grid_spec=pltpu.PrefetchScalarGridSpec(
            num_scalar_prefetch=1,
            grid=(blocks,),
            in_specs=[
                pl.BlockSpec((1, tiles, blk, blk), lambda b, ids: (b, 0, 0, 0)),
                pl.BlockSpec((blk, width), lambda b, ids: (b, 0)),
            ],
            out_specs=[
                pl.BlockSpec((blocks, blk, width), lambda b, ids: (0, 0, 0)),
                pl.BlockSpec((sides - 1, blocks, blk, width), lambda b, ids: (0, 0, 0, 0)),
            ],
            scratch_shapes=[pltpu.VMEM((sides * blocks, blk, width), jnp.float32)],
        ),
        out_shape=(
            jax.ShapeDtypeStruct((blocks, blk, width), jnp.float32),
            jax.ShapeDtypeStruct((sides - 1, blocks, blk, width), jnp.bfloat16),
        ),
        compiler_params=pltpu.CompilerParams(dimension_semantics=("arbitrary",)),
    )(src_ids, tile_mask, grad_agg)


def dense(left, right):
    return jnp.dot(left, right, preferred_element_type=jnp.float32)


def silu_slope(values):
    sigma = jax.nn.sigmoid(values)
    return sigma * (1.0 + values * (1.0 - sigma))


def on_device(
    nodes, tile_src, tile_mask, tokens, tok_count, w_e1, w_e2, w_n1, w_n2, w_q, w_kv, w_o, cotangent
):
    latent = nodes[0, 0]
    node_rows = latent.shape[0]
    latent_width = latent.shape[1]
    block_count = tile_src.shape[2]
    tile_count = tile_src.shape[3]
    blk_rows = tile_mask.shape[-1]
    rows_px = lax.axis_size("px")
    rows_py = lax.axis_size("py")
    devices = rows_px * rows_py
    score_scale = 1.0 / math.sqrt(latent_width)
    pre_act = dense(latent, w_e1)
    activation = jax.nn.silu(pre_act).astype(jnp.bfloat16)
    message = dense(activation, w_e2).astype(jnp.bfloat16)
    sources = [
        message,
        passed_along(message, "px", 1),
        passed_along(message, "px", -1),
        passed_along(message, "py", 1),
        passed_along(message, "py", -1),
    ]
    src_ids = tile_src[0, 0].reshape(-1)
    gathered = tile_gather(
        src_ids,
        tile_mask[0, 0],
        [part.reshape(block_count, blk_rows, latent_width) for part in sources],
    )
    zvalue = dense(latent, w_n1[:latent_width]) + dense(gathered, w_n1[latent_width:])
    hidden = jax.nn.silu(zvalue).astype(jnp.bfloat16)
    updated = (latent.astype(jnp.float32) + dense(hidden, w_n2)).astype(jnp.bfloat16)
    queries = dense(updated, w_q).astype(jnp.bfloat16)
    own_tokens = tokens[0]
    slot_count = own_tokens.shape[0] // devices
    token_groups = own_tokens.reshape(devices, slot_count, latent_width)
    arrived_tokens = lax.all_to_all(
        token_groups, ("px", "py"), split_axis=0, concat_axis=0, tiled=True
    )
    arrived_tokens = arrived_tokens.reshape(devices * slot_count, latent_width)
    arrived = dense(arrived_tokens, w_kv).astype(jnp.bfloat16)
    key_rows = arrived[:, :latent_width]
    value_rows = arrived[:, latent_width:]
    live_keys = (jnp.arange(slot_count)[None, :] < tok_count[:, 0][:, None]).reshape(-1)
    scores = (
        jnp.einsum("nl,kl->nk", queries, key_rows, preferred_element_type=jnp.float32) * score_scale
    )
    scores = jnp.where(live_keys[None, :], scores, -jnp.inf)
    highest = jnp.max(scores, axis=1, keepdims=True)
    expo_terms = jnp.exp(scores - highest)
    probability = expo_terms / jnp.sum(expo_terms, axis=1, keepdims=True)
    prob_low = probability.astype(jnp.bfloat16)
    grad_out = dense(cotangent[0, 0], w_o.T).astype(jnp.bfloat16)
    grad_prob = jnp.einsum("nl,kl->nk", grad_out, value_rows, preferred_element_type=jnp.float32)
    grad_vals = jnp.einsum("nk,nl->kl", prob_low, grad_out, preferred_element_type=jnp.float32)
    spread = jnp.sum(probability * grad_prob, axis=1, keepdims=True)
    grad_score = (probability * (grad_prob - spread) * score_scale).astype(jnp.bfloat16)
    grad_query = dense(grad_score, key_rows).astype(jnp.bfloat16)
    grad_keys = jnp.einsum("nk,nl->kl", grad_score, queries, preferred_element_type=jnp.float32)
    grad_kv = jnp.concatenate([grad_keys, grad_vals], axis=1).astype(jnp.bfloat16)
    grad_slots = dense(grad_kv, w_kv.T).astype(jnp.bfloat16)
    returned = lax.all_to_all(
        grad_slots.reshape(devices, slot_count, latent_width),
        ("px", "py"),
        split_axis=0,
        concat_axis=0,
        tiled=True,
    )
    grad_tokens = returned.reshape(devices * slot_count, latent_width)
    grad_update = cotangent[0, 0].astype(jnp.float32) + dense(grad_query, w_q.T)
    update_low = grad_update.astype(jnp.bfloat16)
    grad_z = (dense(update_low, w_n2.T) * silu_slope(zvalue)).astype(jnp.bfloat16)
    grad_agg = dense(grad_z, w_n1[latent_width:].T).astype(jnp.bfloat16)
    grad_node = grad_update + dense(grad_z, w_n1[:latent_width].T)
    own_part, outbound = tile_scatter(src_ids, tile_mask[0, 0], grad_agg, len(sources))
    outbound = outbound.reshape(len(sources) - 1, node_rows, latent_width)
    collected = own_part.reshape(node_rows, latent_width)
    for member, offset in ((0, -1), (1, 1)):
        collected = collected + passed_along(outbound[member], "px", offset).astype(jnp.float32)
    for member, offset in ((2, -1), (3, 1)):
        collected = collected + passed_along(outbound[member], "py", offset).astype(jnp.float32)
    grad_msg = collected.astype(jnp.bfloat16)
    grad_pre = (dense(grad_msg, w_e2.T) * silu_slope(pre_act)).astype(jnp.bfloat16)
    grad_nodes = (grad_node + dense(grad_pre, w_e1.T)).astype(jnp.bfloat16)
    return (grad_nodes[None, None], grad_tokens[None])


def solution(mesh):
    return jax.shard_map(
        on_device,
        mesh=mesh,
        in_specs=(
            P("px", "py", None, None),
            P("px", "py", None, None),
            P("px", "py", None, None, None, None),
            P(("px", "py"), None, None),
            P(None, ("px", "py")),
            P(),
            P(),
            P(),
            P(),
            P(),
            P(),
            P(),
            P("px", "py", None, None),
        ),
        out_specs=(P("px", "py", None, None), P(("px", "py"), None, None)),
        check_vma=False,
    )
```

```python
import functools
import math

import jax
import jax.numpy as jnp
from jax import lax
from jax.experimental import pallas as pl
from jax.experimental.pallas import tpu as pltpu
from jax.sharding import PartitionSpec as P


def with_halo(block, sides, width):
    for axis, dim in sides:
        count = lax.axis_size(axis)
        forward = [(i, i + 1) for i in range(count - 1)]
        backward = [(target, source) for source, target in forward]
        low = lax.ppermute(
            lax.slice_in_dim(block, block.shape[dim] - width, None, axis=dim), axis, forward
        )
        high = lax.ppermute(lax.slice_in_dim(block, 0, width, axis=dim), axis, backward)
        block = jnp.concatenate([low, block, high], axis=dim)
    return block


def passed_along(value, axis, steps):
    count = lax.axis_size(axis)
    leading, last = (max(0, -steps), min(count, count - steps))
    return lax.ppermute(value, axis, [(source, source + steps) for source in range(leading, last)])


def gather_kernel(src_ids, mask_ref, own, up, down, left, right, out_ref):
    b = pl.program_id(0)
    tiles = mask_ref.shape[1]
    per_side = own.shape[0]
    total = jnp.zeros(out_ref.shape, jnp.float32)
    for k in range(tiles):
        picked = src_ids[b * tiles + k]
        side = picked // per_side
        block = picked % per_side
        bits = mask_ref[0, k].astype(jnp.float32).astype(jnp.bfloat16)
        rows = own[block]
        for index, ref in enumerate((up, down, left, right)):
            rows = jnp.where(side == index + 1, ref[block], rows)
        total = total + jnp.dot(bits, rows, preferred_element_type=jnp.float32)
    out_ref[...] = total.astype(out_ref.dtype)


def tile_gather(src_ids, tile_mask, sources):
    blocks, tiles, blk, _ = tile_mask.shape
    width = sources[0].shape[-1]
    whole = pl.BlockSpec((blocks, blk, width), lambda b, ids: (0, 0, 0))
    return pl.pallas_call(
        gather_kernel,
        grid_spec=pltpu.PrefetchScalarGridSpec(
            num_scalar_prefetch=1,
            grid=(blocks,),
            in_specs=[pl.BlockSpec((1, tiles, blk, blk), lambda b, ids: (b, 0, 0, 0))]
            + [whole] * len(sources),
            out_specs=pl.BlockSpec((blk, width), lambda b, ids: (b, 0)),
        ),
        out_shape=jax.ShapeDtypeStruct((blocks * blk, width), jnp.bfloat16),
    )(src_ids, tile_mask, *sources)


def scatter_kernel(src_ids, mask_ref, grad_ref, own_ref, out_ref, total):
    b = pl.program_id(0)
    tiles = mask_ref.shape[1]
    per_side = own_ref.shape[0]

    @pl.when(b == 0)
    def _():
        total[...] = jnp.zeros(total.shape, jnp.float32)

    grad_rows = grad_ref[...]
    for k in range(tiles):
        picked = src_ids[b * tiles + k]
        bits = mask_ref[0, k].astype(jnp.float32).T.astype(jnp.bfloat16)
        total[picked] += jnp.dot(bits, grad_rows, preferred_element_type=jnp.float32)

    @pl.when(b == pl.num_programs(0) - 1)
    def _():
        own_ref[...] = total[0:per_side]
        for side in range(out_ref.shape[0]):
            start = (side + 1) * per_side
            out_ref[side] = total[start : start + per_side].astype(out_ref.dtype)


def tile_scatter(src_ids, tile_mask, grad_agg, sides):
    blocks, tiles, blk, _ = tile_mask.shape
    width = grad_agg.shape[-1]
    return pl.pallas_call(
        scatter_kernel,
        grid_spec=pltpu.PrefetchScalarGridSpec(
            num_scalar_prefetch=1,
            grid=(blocks,),
            in_specs=[
                pl.BlockSpec((1, tiles, blk, blk), lambda b, ids: (b, 0, 0, 0)),
                pl.BlockSpec((blk, width), lambda b, ids: (b, 0)),
            ],
            out_specs=[
                pl.BlockSpec((blocks, blk, width), lambda b, ids: (0, 0, 0)),
                pl.BlockSpec((sides - 1, blocks, blk, width), lambda b, ids: (0, 0, 0, 0)),
            ],
            scratch_shapes=[pltpu.VMEM((sides * blocks, blk, width), jnp.float32)],
        ),
        out_shape=(
            jax.ShapeDtypeStruct((blocks, blk, width), jnp.float32),
            jax.ShapeDtypeStruct((sides - 1, blocks, blk, width), jnp.bfloat16),
        ),
        compiler_params=pltpu.CompilerParams(dimension_semantics=("arbitrary",)),
    )(src_ids, tile_mask, grad_agg)


def attend_kernel(scale, live_ref, q_ref, go_ref, kv_ref, gq_ref, gkv_ref, gk_acc, gv_acc):
    step = pl.program_id(0)
    width = q_ref.shape[1]

    @pl.when(step == 0)
    def _():
        gk_acc[...] = jnp.zeros(gk_acc.shape, jnp.float32)
        gv_acc[...] = jnp.zeros(gv_acc.shape, jnp.float32)

    queries = q_ref[...]
    grad_out = go_ref[...]
    keys = kv_ref[:, 0:width]
    values = kv_ref[:, width : 2 * width]
    nt = (((1,), (1,)), ((), ()))
    tn = (((0,), (0,)), ((), ()))
    scores = lax.dot_general(queries, keys, nt, preferred_element_type=jnp.float32) * scale
    scores = jnp.where(live_ref[...] > 0, scores, -jnp.inf)
    highest = jnp.max(scores, axis=1, keepdims=True)
    expo_terms = jnp.exp(scores - highest)
    probability = expo_terms / jnp.sum(expo_terms, axis=1, keepdims=True)
    prob_low = probability.astype(jnp.bfloat16)
    grad_prob = lax.dot_general(grad_out, values, nt, preferred_element_type=jnp.float32)
    spread = jnp.sum(probability * grad_prob, axis=1, keepdims=True)
    grad_score = (probability * (grad_prob - spread) * scale).astype(jnp.bfloat16)
    gq_ref[...] = jnp.dot(grad_score, keys, preferred_element_type=jnp.float32).astype(gq_ref.dtype)
    gk_acc[...] += lax.dot_general(grad_score, queries, tn, preferred_element_type=jnp.float32)
    gv_acc[...] += lax.dot_general(prob_low, grad_out, tn, preferred_element_type=jnp.float32)

    @pl.when(step == pl.num_programs(0) - 1)
    def _():
        gkv_ref[:, 0:width] = gk_acc[...].astype(gkv_ref.dtype)
        gkv_ref[:, width : 2 * width] = gv_acc[...].astype(gkv_ref.dtype)


def attend_back(live, queries, grad_out, keyvals, scale, rows_per_step=256):
    rows, width = queries.shape
    slots = keyvals.shape[0]
    steps = rows // rows_per_step
    row_block = pl.BlockSpec((rows_per_step, width), lambda i: (i, 0))
    return pl.pallas_call(
        functools.partial(attend_kernel, scale),
        grid=(steps,),
        in_specs=[
            pl.BlockSpec((1, slots), lambda i: (0, 0)),
            row_block,
            row_block,
            pl.BlockSpec((slots, 2 * width), lambda i: (0, 0)),
        ],
        out_specs=[row_block, pl.BlockSpec((slots, 2 * width), lambda i: (0, 0))],
        out_shape=(
            jax.ShapeDtypeStruct((rows, width), jnp.bfloat16),
            jax.ShapeDtypeStruct((slots, 2 * width), jnp.bfloat16),
        ),
        scratch_shapes=[
            pltpu.VMEM((slots, width), jnp.float32),
            pltpu.VMEM((slots, width), jnp.float32),
        ],
        compiler_params=pltpu.CompilerParams(dimension_semantics=("arbitrary",)),
        cost_estimate=pl.CostEstimate(
            flops=10 * rows * slots * width,
            transcendentals=rows * slots,
            bytes_accessed=2 * (3 * rows * width + 4 * slots * width),
        ),
    )(live, queries, grad_out, keyvals)


def dense(left, right):
    return jnp.dot(left, right, preferred_element_type=jnp.float32)


def silu_slope(values):
    sigma = jax.nn.sigmoid(values)
    return sigma * (1.0 + values * (1.0 - sigma))


def on_device(
    nodes, tile_src, tile_mask, tokens, tok_count, w_e1, w_e2, w_n1, w_n2, w_q, w_kv, w_o, cotangent
):
    latent = nodes[0, 0]
    node_rows = latent.shape[0]
    latent_width = latent.shape[1]
    block_count = tile_src.shape[2]
    tile_count = tile_src.shape[3]
    blk_rows = tile_mask.shape[-1]
    rows_px = lax.axis_size("px")
    rows_py = lax.axis_size("py")
    devices = rows_px * rows_py
    score_scale = 1.0 / math.sqrt(latent_width)
    pre_act = dense(latent, w_e1)
    activation = jax.nn.silu(pre_act).astype(jnp.bfloat16)
    message = dense(activation, w_e2).astype(jnp.bfloat16)
    sources = [
        message,
        passed_along(message, "px", 1),
        passed_along(message, "px", -1),
        passed_along(message, "py", 1),
        passed_along(message, "py", -1),
    ]
    src_ids = tile_src[0, 0].reshape(-1)
    gathered = tile_gather(
        src_ids,
        tile_mask[0, 0],
        [part.reshape(block_count, blk_rows, latent_width) for part in sources],
    )
    zvalue = dense(latent, w_n1[:latent_width]) + dense(gathered, w_n1[latent_width:])
    hidden = jax.nn.silu(zvalue).astype(jnp.bfloat16)
    updated = (latent.astype(jnp.float32) + dense(hidden, w_n2)).astype(jnp.bfloat16)
    queries = dense(updated, w_q).astype(jnp.bfloat16)
    own_tokens = tokens[0]
    slot_count = own_tokens.shape[0] // devices
    token_groups = own_tokens.reshape(devices, slot_count, latent_width)
    arrived_tokens = lax.all_to_all(
        token_groups, ("px", "py"), split_axis=0, concat_axis=0, tiled=True
    )
    arrived_tokens = arrived_tokens.reshape(devices * slot_count, latent_width)
    arrived = dense(arrived_tokens, w_kv).astype(jnp.bfloat16)
    live_keys = (jnp.arange(slot_count)[None, :] < tok_count[:, 0][:, None]).reshape(1, -1)
    grad_out = dense(cotangent[0, 0], w_o.T).astype(jnp.bfloat16)
    grad_query, grad_kv = attend_back(
        live_keys.astype(jnp.float32), queries, grad_out, arrived, score_scale
    )
    grad_slots = dense(grad_kv, w_kv.T).astype(jnp.bfloat16)
    returned = lax.all_to_all(
        grad_slots.reshape(devices, slot_count, latent_width),
        ("px", "py"),
        split_axis=0,
        concat_axis=0,
        tiled=True,
    )
    grad_tokens = returned.reshape(devices * slot_count, latent_width)
    grad_update = cotangent[0, 0].astype(jnp.float32) + dense(grad_query, w_q.T)
    update_low = grad_update.astype(jnp.bfloat16)
    grad_z = (dense(update_low, w_n2.T) * silu_slope(zvalue)).astype(jnp.bfloat16)
    grad_agg = dense(grad_z, w_n1[latent_width:].T).astype(jnp.bfloat16)
    grad_node = grad_update + dense(grad_z, w_n1[:latent_width].T)
    own_part, outbound = tile_scatter(src_ids, tile_mask[0, 0], grad_agg, len(sources))
    outbound = outbound.reshape(len(sources) - 1, node_rows, latent_width)
    collected = own_part.reshape(node_rows, latent_width)
    for member, offset in ((0, -1), (1, 1)):
        collected = collected + passed_along(outbound[member], "px", offset).astype(jnp.float32)
    for member, offset in ((2, -1), (3, 1)):
        collected = collected + passed_along(outbound[member], "py", offset).astype(jnp.float32)
    grad_msg = collected.astype(jnp.bfloat16)
    grad_pre = (dense(grad_msg, w_e2.T) * silu_slope(pre_act)).astype(jnp.bfloat16)
    grad_nodes = (grad_node + dense(grad_pre, w_e1.T)).astype(jnp.bfloat16)
    return (grad_nodes[None, None], grad_tokens[None])


def solution(mesh):
    return jax.shard_map(
        on_device,
        mesh=mesh,
        in_specs=(
            P("px", "py", None, None),
            P("px", "py", None, None),
            P("px", "py", None, None, None, None),
            P(("px", "py"), None, None),
            P(None, ("px", "py")),
            P(),
            P(),
            P(),
            P(),
            P(),
            P(),
            P(),
            P("px", "py", None, None),
        ),
        out_specs=(P("px", "py", None, None), P(("px", "py"), None, None)),
        check_vma=False,
    )
```

```python
import functools
import math

import jax
import jax.numpy as jnp
from jax import lax
from jax.experimental import pallas as pl
from jax.experimental.pallas import tpu as pltpu
from jax.sharding import PartitionSpec as P


def with_halo(block, sides, width):
    for axis, dim in sides:
        count = lax.axis_size(axis)
        forward = [(i, i + 1) for i in range(count - 1)]
        backward = [(target, source) for source, target in forward]
        low = lax.ppermute(
            lax.slice_in_dim(block, block.shape[dim] - width, None, axis=dim), axis, forward
        )
        high = lax.ppermute(lax.slice_in_dim(block, 0, width, axis=dim), axis, backward)
        block = jnp.concatenate([low, block, high], axis=dim)
    return block


def passed_along(value, axis, steps):
    count = lax.axis_size(axis)
    leading, last = (max(0, -steps), min(count, count - steps))
    return lax.ppermute(value, axis, [(source, source + steps) for source in range(leading, last)])


def gather_kernel(group, src_ids, mask_ref, own, up, down, left, right, out_ref, rhs):
    step = pl.program_id(0)
    tiles = mask_ref.shape[1]
    blk = mask_ref.shape[2]
    per_side = own.shape[0]
    for g in range(group):
        for k in range(tiles):
            picked = src_ids[(step * group + g) * tiles + k]
            side = picked // per_side
            block = picked % per_side
            for index, ref in enumerate((own, up, down, left, right)):

                @pl.when(side == index)
                def _():
                    rhs[k * blk : (k + 1) * blk, :] = ref[block]

        bits = jnp.concatenate(
            [mask_ref[g, k].astype(jnp.float32).astype(jnp.bfloat16) for k in range(tiles)], axis=1
        )
        total = jnp.dot(bits, rhs[...], preferred_element_type=jnp.float32)
        out_ref[g * blk : (g + 1) * blk, :] = total.astype(out_ref.dtype)


def tile_gather(src_ids, tile_mask, sources, group=4):
    blocks, tiles, blk, _ = tile_mask.shape
    width = sources[0].shape[-1]
    whole = pl.BlockSpec((blocks, blk, width), lambda i, ids: (0, 0, 0))
    return pl.pallas_call(
        functools.partial(gather_kernel, group),
        grid_spec=pltpu.PrefetchScalarGridSpec(
            num_scalar_prefetch=1,
            grid=(blocks // group,),
            in_specs=[pl.BlockSpec((group, tiles, blk, blk), lambda i, ids: (i, 0, 0, 0))]
            + [whole] * len(sources),
            out_specs=pl.BlockSpec((group * blk, width), lambda i, ids: (i, 0)),
            scratch_shapes=[pltpu.VMEM((tiles * blk, width), jnp.bfloat16)],
        ),
        out_shape=jax.ShapeDtypeStruct((blocks * blk, width), jnp.bfloat16),
        compiler_params=pltpu.CompilerParams(dimension_semantics=("arbitrary",)),
    )(src_ids, tile_mask, *sources)


def scatter_kernel(group, src_ids, mask_ref, grad_ref, own_ref, out_ref, total):
    step = pl.program_id(0)
    tiles = mask_ref.shape[1]
    blk = mask_ref.shape[2]
    per_side = own_ref.shape[0]
    tn = (((0,), (0,)), ((), ()))

    @pl.when(step == 0)
    def _():
        total[...] = jnp.zeros(total.shape, jnp.float32)

    for g in range(group):
        bits = jnp.concatenate(
            [mask_ref[g, k].astype(jnp.float32).astype(jnp.bfloat16) for k in range(tiles)], axis=1
        )
        grad_rows = grad_ref[g * blk : (g + 1) * blk, :]
        parts = lax.dot_general(bits, grad_rows, tn, preferred_element_type=jnp.float32)
        for k in range(tiles):
            picked = src_ids[(step * group + g) * tiles + k]
            total[picked] += parts[k * blk : (k + 1) * blk]

    @pl.when(step == pl.num_programs(0) - 1)
    def _():
        own_ref[...] = total[0:per_side]
        for side in range(out_ref.shape[0]):
            start = (side + 1) * per_side
            out_ref[side] = total[start : start + per_side].astype(out_ref.dtype)


def tile_scatter(src_ids, tile_mask, grad_agg, sides, group=4):
    blocks, tiles, blk, _ = tile_mask.shape
    width = grad_agg.shape[-1]
    return pl.pallas_call(
        functools.partial(scatter_kernel, group),
        grid_spec=pltpu.PrefetchScalarGridSpec(
            num_scalar_prefetch=1,
            grid=(blocks // group,),
            in_specs=[
                pl.BlockSpec((group, tiles, blk, blk), lambda i, ids: (i, 0, 0, 0)),
                pl.BlockSpec((group * blk, width), lambda i, ids: (i, 0)),
            ],
            out_specs=[
                pl.BlockSpec((blocks, blk, width), lambda i, ids: (0, 0, 0)),
                pl.BlockSpec((sides - 1, blocks, blk, width), lambda i, ids: (0, 0, 0, 0)),
            ],
            scratch_shapes=[pltpu.VMEM((sides * blocks, blk, width), jnp.float32)],
        ),
        out_shape=(
            jax.ShapeDtypeStruct((blocks, blk, width), jnp.float32),
            jax.ShapeDtypeStruct((sides - 1, blocks, blk, width), jnp.bfloat16),
        ),
        compiler_params=pltpu.CompilerParams(dimension_semantics=("arbitrary",)),
    )(src_ids, tile_mask, grad_agg)


def attend_kernel(scale, live_ref, q_ref, go_ref, kv_ref, gq_ref, gkv_ref, gk_acc, gv_acc):
    step = pl.program_id(0)
    width = q_ref.shape[1]

    @pl.when(step == 0)
    def _():
        gk_acc[...] = jnp.zeros(gk_acc.shape, jnp.float32)
        gv_acc[...] = jnp.zeros(gv_acc.shape, jnp.float32)

    queries = q_ref[...]
    grad_out = go_ref[...]
    keys = kv_ref[:, 0:width]
    values = kv_ref[:, width : 2 * width]
    nt = (((1,), (1,)), ((), ()))
    tn = (((0,), (0,)), ((), ()))
    scores = lax.dot_general(queries, keys, nt, preferred_element_type=jnp.float32) * scale
    scores = jnp.where(live_ref[...] > 0, scores, -jnp.inf)
    highest = jnp.max(scores, axis=1, keepdims=True)
    expo_terms = jnp.exp(scores - highest)
    probability = expo_terms / jnp.sum(expo_terms, axis=1, keepdims=True)
    prob_low = probability.astype(jnp.bfloat16)
    grad_prob = lax.dot_general(grad_out, values, nt, preferred_element_type=jnp.float32)
    spread = jnp.sum(probability * grad_prob, axis=1, keepdims=True)
    grad_score = (probability * (grad_prob - spread) * scale).astype(jnp.bfloat16)
    gq_ref[...] = jnp.dot(grad_score, keys, preferred_element_type=jnp.float32).astype(gq_ref.dtype)
    gk_acc[...] += lax.dot_general(grad_score, queries, tn, preferred_element_type=jnp.float32)
    gv_acc[...] += lax.dot_general(prob_low, grad_out, tn, preferred_element_type=jnp.float32)

    @pl.when(step == pl.num_programs(0) - 1)
    def _():
        gkv_ref[:, 0:width] = gk_acc[...].astype(gkv_ref.dtype)
        gkv_ref[:, width : 2 * width] = gv_acc[...].astype(gkv_ref.dtype)


def attend_back(live, queries, grad_out, keyvals, scale, rows_per_step=256):
    rows, width = queries.shape
    slots = keyvals.shape[0]
    steps = rows // rows_per_step
    row_block = pl.BlockSpec((rows_per_step, width), lambda i: (i, 0))
    return pl.pallas_call(
        functools.partial(attend_kernel, scale),
        grid=(steps,),
        in_specs=[
            pl.BlockSpec((1, slots), lambda i: (0, 0)),
            row_block,
            row_block,
            pl.BlockSpec((slots, 2 * width), lambda i: (0, 0)),
        ],
        out_specs=[row_block, pl.BlockSpec((slots, 2 * width), lambda i: (0, 0))],
        out_shape=(
            jax.ShapeDtypeStruct((rows, width), jnp.bfloat16),
            jax.ShapeDtypeStruct((slots, 2 * width), jnp.bfloat16),
        ),
        scratch_shapes=[
            pltpu.VMEM((slots, width), jnp.float32),
            pltpu.VMEM((slots, width), jnp.float32),
        ],
        compiler_params=pltpu.CompilerParams(dimension_semantics=("arbitrary",)),
        cost_estimate=pl.CostEstimate(
            flops=10 * rows * slots * width,
            transcendentals=rows * slots,
            bytes_accessed=2 * (3 * rows * width + 4 * slots * width),
        ),
    )(live, queries, grad_out, keyvals)


def dense(left, right):
    return jnp.dot(left, right, preferred_element_type=jnp.float32)


def silu_slope(values):
    sigma = jax.nn.sigmoid(values)
    return sigma * (1.0 + values * (1.0 - sigma))


def on_device(
    nodes, tile_src, tile_mask, tokens, tok_count, w_e1, w_e2, w_n1, w_n2, w_q, w_kv, w_o, cotangent
):
    latent = nodes[0, 0]
    node_rows = latent.shape[0]
    latent_width = latent.shape[1]
    block_count = tile_src.shape[2]
    tile_count = tile_src.shape[3]
    blk_rows = tile_mask.shape[-1]
    rows_px = lax.axis_size("px")
    rows_py = lax.axis_size("py")
    devices = rows_px * rows_py
    score_scale = 1.0 / math.sqrt(latent_width)
    pre_act = dense(latent, w_e1)
    activation = jax.nn.silu(pre_act).astype(jnp.bfloat16)
    message = dense(activation, w_e2).astype(jnp.bfloat16)
    sources = [
        message,
        passed_along(message, "px", 1),
        passed_along(message, "px", -1),
        passed_along(message, "py", 1),
        passed_along(message, "py", -1),
    ]
    src_ids = tile_src[0, 0].reshape(-1)
    gathered = tile_gather(
        src_ids,
        tile_mask[0, 0],
        [part.reshape(block_count, blk_rows, latent_width) for part in sources],
    )
    zvalue = dense(latent, w_n1[:latent_width]) + dense(gathered, w_n1[latent_width:])
    hidden = jax.nn.silu(zvalue).astype(jnp.bfloat16)
    updated = (latent.astype(jnp.float32) + dense(hidden, w_n2)).astype(jnp.bfloat16)
    queries = dense(updated, w_q).astype(jnp.bfloat16)
    own_tokens = tokens[0]
    slot_count = own_tokens.shape[0] // devices
    token_groups = own_tokens.reshape(devices, slot_count, latent_width)
    arrived_tokens = lax.all_to_all(
        token_groups, ("px", "py"), split_axis=0, concat_axis=0, tiled=True
    )
    arrived_tokens = arrived_tokens.reshape(devices * slot_count, latent_width)
    arrived = dense(arrived_tokens, w_kv).astype(jnp.bfloat16)
    live_keys = (jnp.arange(slot_count)[None, :] < tok_count[:, 0][:, None]).reshape(1, -1)
    grad_out = dense(cotangent[0, 0], w_o.T).astype(jnp.bfloat16)
    grad_query, grad_kv = attend_back(
        live_keys.astype(jnp.float32), queries, grad_out, arrived, score_scale
    )
    grad_slots = dense(grad_kv, w_kv.T).astype(jnp.bfloat16)
    returned = lax.all_to_all(
        grad_slots.reshape(devices, slot_count, latent_width),
        ("px", "py"),
        split_axis=0,
        concat_axis=0,
        tiled=True,
    )
    grad_tokens = returned.reshape(devices * slot_count, latent_width)
    grad_update = cotangent[0, 0].astype(jnp.float32) + dense(grad_query, w_q.T)
    update_low = grad_update.astype(jnp.bfloat16)
    grad_z = (dense(update_low, w_n2.T) * silu_slope(zvalue)).astype(jnp.bfloat16)
    grad_agg = dense(grad_z, w_n1[latent_width:].T).astype(jnp.bfloat16)
    grad_node = grad_update + dense(grad_z, w_n1[:latent_width].T)
    own_part, outbound = tile_scatter(src_ids, tile_mask[0, 0], grad_agg, len(sources))
    outbound = outbound.reshape(len(sources) - 1, node_rows, latent_width)
    collected = own_part.reshape(node_rows, latent_width)
    for member, offset in ((0, -1), (1, 1)):
        collected = collected + passed_along(outbound[member], "px", offset).astype(jnp.float32)
    for member, offset in ((2, -1), (3, 1)):
        collected = collected + passed_along(outbound[member], "py", offset).astype(jnp.float32)
    grad_msg = collected.astype(jnp.bfloat16)
    grad_pre = (dense(grad_msg, w_e2.T) * silu_slope(pre_act)).astype(jnp.bfloat16)
    grad_nodes = (grad_node + dense(grad_pre, w_e1.T)).astype(jnp.bfloat16)
    return (grad_nodes[None, None], grad_tokens[None])


def solution(mesh):
    return jax.shard_map(
        on_device,
        mesh=mesh,
        in_specs=(
            P("px", "py", None, None),
            P("px", "py", None, None),
            P("px", "py", None, None, None, None),
            P(("px", "py"), None, None),
            P(None, ("px", "py")),
            P(),
            P(),
            P(),
            P(),
            P(),
            P(),
            P(),
            P("px", "py", None, None),
        ),
        out_specs=(P("px", "py", None, None), P(("px", "py"), None, None)),
        check_vma=False,
    )
```

```python
import functools
import math

import jax
import jax.numpy as jnp
from jax import lax
from jax.experimental import pallas as pl
from jax.experimental.pallas import tpu as pltpu
from jax.sharding import PartitionSpec as P


def with_halo(block, sides, width):
    for axis, dim in sides:
        count = lax.axis_size(axis)
        forward = [(i, i + 1) for i in range(count - 1)]
        backward = [(target, source) for source, target in forward]
        low = lax.ppermute(
            lax.slice_in_dim(block, block.shape[dim] - width, None, axis=dim), axis, forward
        )
        high = lax.ppermute(lax.slice_in_dim(block, 0, width, axis=dim), axis, backward)
        block = jnp.concatenate([low, block, high], axis=dim)
    return block


def passed_along(value, axis, steps):
    count = lax.axis_size(axis)
    leading, last = (max(0, -steps), min(count, count - steps))
    return lax.ppermute(value, axis, [(source, source + steps) for source in range(leading, last)])


def gather_kernel(group, src_ids, mask_ref, own, up, down, left, right, out_ref, rhs):
    step = pl.program_id(0)
    tiles = mask_ref.shape[1]
    blk = mask_ref.shape[2]
    per_side = own.shape[0]
    for g in range(group):
        for k in range(tiles):
            picked = src_ids[(step * group + g) * tiles + k]
            side = picked // per_side
            block = picked % per_side
            for index, ref in enumerate((own, up, down, left, right)):

                @pl.when(side == index)
                def _():
                    rhs[k * blk : (k + 1) * blk, :] = ref[block]

        bits = jnp.concatenate(
            [mask_ref[g, k].astype(jnp.float32).astype(jnp.bfloat16) for k in range(tiles)], axis=1
        )
        total = jnp.dot(bits, rhs[...], preferred_element_type=jnp.float32)
        out_ref[g * blk : (g + 1) * blk, :] = total.astype(out_ref.dtype)


def tile_gather(src_ids, tile_mask, sources, group=4):
    blocks, tiles, blk, _ = tile_mask.shape
    width = sources[0].shape[-1]
    whole = pl.BlockSpec((blocks, blk, width), lambda i, ids: (0, 0, 0))
    return pl.pallas_call(
        functools.partial(gather_kernel, group),
        grid_spec=pltpu.PrefetchScalarGridSpec(
            num_scalar_prefetch=1,
            grid=(blocks // group,),
            in_specs=[pl.BlockSpec((group, tiles, blk, blk), lambda i, ids: (i, 0, 0, 0))]
            + [whole] * len(sources),
            out_specs=pl.BlockSpec((group * blk, width), lambda i, ids: (i, 0)),
            scratch_shapes=[pltpu.VMEM((tiles * blk, width), jnp.bfloat16)],
        ),
        out_shape=jax.ShapeDtypeStruct((blocks * blk, width), jnp.bfloat16),
        compiler_params=pltpu.CompilerParams(dimension_semantics=("arbitrary",)),
    )(src_ids, tile_mask, *sources)


def scatter_kernel(group, src_ids, mask_ref, grad_ref, own_ref, out_ref, total):
    step = pl.program_id(0)
    tiles = mask_ref.shape[1]
    blk = mask_ref.shape[2]
    per_side = own_ref.shape[0]
    tn = (((0,), (0,)), ((), ()))

    @pl.when(step == 0)
    def _():
        total[...] = jnp.zeros(total.shape, jnp.float32)

    for g in range(group):
        bits = jnp.concatenate(
            [mask_ref[g, k].astype(jnp.float32).astype(jnp.bfloat16) for k in range(tiles)], axis=1
        )
        grad_rows = grad_ref[g * blk : (g + 1) * blk, :]
        parts = lax.dot_general(bits, grad_rows, tn, preferred_element_type=jnp.float32)
        for k in range(tiles):
            picked = src_ids[(step * group + g) * tiles + k]
            total[picked] += parts[k * blk : (k + 1) * blk]

    @pl.when(step == pl.num_programs(0) - 1)
    def _():
        own_ref[...] = total[0:per_side]
        for side in range(out_ref.shape[0]):
            start = (side + 1) * per_side
            out_ref[side] = total[start : start + per_side].astype(out_ref.dtype)


def tile_scatter(src_ids, tile_mask, grad_agg, sides, group=4):
    blocks, tiles, blk, _ = tile_mask.shape
    width = grad_agg.shape[-1]
    return pl.pallas_call(
        functools.partial(scatter_kernel, group),
        grid_spec=pltpu.PrefetchScalarGridSpec(
            num_scalar_prefetch=1,
            grid=(blocks // group,),
            in_specs=[
                pl.BlockSpec((group, tiles, blk, blk), lambda i, ids: (i, 0, 0, 0)),
                pl.BlockSpec((group * blk, width), lambda i, ids: (i, 0)),
            ],
            out_specs=[
                pl.BlockSpec((blocks, blk, width), lambda i, ids: (0, 0, 0)),
                pl.BlockSpec((sides - 1, blocks, blk, width), lambda i, ids: (0, 0, 0, 0)),
            ],
            scratch_shapes=[pltpu.VMEM((sides * blocks, blk, width), jnp.float32)],
        ),
        out_shape=(
            jax.ShapeDtypeStruct((blocks, blk, width), jnp.float32),
            jax.ShapeDtypeStruct((sides - 1, blocks, blk, width), jnp.bfloat16),
        ),
        compiler_params=pltpu.CompilerParams(dimension_semantics=("arbitrary",)),
    )(src_ids, tile_mask, grad_agg)


def attend_kernel(scale, live_ref, q_ref, go_ref, kv_ref, gq_ref, gkv_ref, gk_acc, gv_acc):
    step = pl.program_id(0)
    width = q_ref.shape[1]

    @pl.when(step == 0)
    def _():
        gk_acc[...] = jnp.zeros(gk_acc.shape, jnp.float32)
        gv_acc[...] = jnp.zeros(gv_acc.shape, jnp.float32)

    queries = q_ref[...]
    grad_out = go_ref[...]
    keys = kv_ref[:, 0:width]
    values = kv_ref[:, width : 2 * width]
    nt = (((1,), (1,)), ((), ()))
    tn = (((0,), (0,)), ((), ()))
    scores = lax.dot_general(queries, keys, nt, preferred_element_type=jnp.float32) * scale
    scores = jnp.where(live_ref[...] > 0, scores, -jnp.inf)
    highest = jnp.max(scores, axis=1, keepdims=True)
    expo_terms = jnp.exp(scores - highest)
    probability = expo_terms / jnp.sum(expo_terms, axis=1, keepdims=True)
    prob_low = probability.astype(jnp.bfloat16)
    grad_prob = lax.dot_general(grad_out, values, nt, preferred_element_type=jnp.float32)
    spread = jnp.sum(probability * grad_prob, axis=1, keepdims=True)
    grad_score = (probability * (grad_prob - spread) * scale).astype(jnp.bfloat16)
    gq_ref[...] = jnp.dot(grad_score, keys, preferred_element_type=jnp.float32).astype(gq_ref.dtype)
    gk_acc[...] += lax.dot_general(grad_score, queries, tn, preferred_element_type=jnp.float32)
    gv_acc[...] += lax.dot_general(prob_low, grad_out, tn, preferred_element_type=jnp.float32)

    @pl.when(step == pl.num_programs(0) - 1)
    def _():
        gkv_ref[:, 0:width] = gk_acc[...].astype(gkv_ref.dtype)
        gkv_ref[:, width : 2 * width] = gv_acc[...].astype(gkv_ref.dtype)


def attend_back(live, queries, grad_out, keyvals, scale, rows_per_step=256):
    rows, width = queries.shape
    slots = keyvals.shape[0]
    steps = rows // rows_per_step
    row_block = pl.BlockSpec((rows_per_step, width), lambda i: (i, 0))
    return pl.pallas_call(
        functools.partial(attend_kernel, scale),
        grid=(steps,),
        in_specs=[
            pl.BlockSpec((1, slots), lambda i: (0, 0)),
            row_block,
            row_block,
            pl.BlockSpec((slots, 2 * width), lambda i: (0, 0)),
        ],
        out_specs=[row_block, pl.BlockSpec((slots, 2 * width), lambda i: (0, 0))],
        out_shape=(
            jax.ShapeDtypeStruct((rows, width), jnp.bfloat16),
            jax.ShapeDtypeStruct((slots, 2 * width), jnp.bfloat16),
        ),
        scratch_shapes=[
            pltpu.VMEM((slots, width), jnp.float32),
            pltpu.VMEM((slots, width), jnp.float32),
        ],
        compiler_params=pltpu.CompilerParams(dimension_semantics=("arbitrary",)),
        cost_estimate=pl.CostEstimate(
            flops=10 * rows * slots * width,
            transcendentals=rows * slots,
            bytes_accessed=2 * (3 * rows * width + 4 * slots * width),
        ),
    )(live, queries, grad_out, keyvals)


def slope_of(values):
    sigma = 1.0 / (1.0 + jnp.exp(-values))
    return sigma * (1.0 + values * (1.0 - sigma))


def edge_back_kernel(lat_ref, own_ref, a_ref, b_ref, c_ref, d_ref, gn_ref, w1_ref, w2_ref, out_ref):
    nt = (((1,), (1,)), ((), ()))
    collected = own_ref[...]
    for ref in (a_ref, b_ref, c_ref, d_ref):
        collected = collected + ref[...].astype(jnp.float32)
    grad_msg = collected.astype(jnp.bfloat16)
    pre_act = jnp.dot(lat_ref[...], w1_ref[...], preferred_element_type=jnp.float32)
    grad_pre = lax.dot_general(grad_msg, w2_ref[...], nt, preferred_element_type=jnp.float32)
    grad_pre = (grad_pre * slope_of(pre_act)).astype(jnp.bfloat16)
    total = gn_ref[...] + lax.dot_general(grad_pre, w1_ref[...], nt, preferred_element_type=jnp.float32)
    out_ref[...] = total.astype(out_ref.dtype)


def edge_back(latent, own_part, received, grad_node, w_e1, w_e2, rows_per_step=512):
    rows, width = latent.shape
    row_block = pl.BlockSpec((rows_per_step, width), lambda i: (i, 0))
    weight = pl.BlockSpec(w_e1.shape, lambda i: (0, 0))
    return pl.pallas_call(
        edge_back_kernel,
        grid=(rows // rows_per_step,),
        in_specs=[row_block] * (3 + len(received)) + [weight, weight],
        out_specs=row_block,
        out_shape=jax.ShapeDtypeStruct((rows, width), jnp.bfloat16),
        cost_estimate=pl.CostEstimate(
            flops=6 * rows * width * width,
            transcendentals=rows * width,
            bytes_accessed=rows * width * (2 + 4 + 2 * len(received) + 4 + 2),
        ),
    )(latent, own_part, *received, grad_node, w_e1, w_e2)


def dense(left, right):
    return jnp.dot(left, right, preferred_element_type=jnp.float32)


def silu_slope(values):
    sigma = jax.nn.sigmoid(values)
    return sigma * (1.0 + values * (1.0 - sigma))


def on_device(
    nodes, tile_src, tile_mask, tokens, tok_count, w_e1, w_e2, w_n1, w_n2, w_q, w_kv, w_o, cotangent
):
    latent = nodes[0, 0]
    node_rows = latent.shape[0]
    latent_width = latent.shape[1]
    block_count = tile_src.shape[2]
    tile_count = tile_src.shape[3]
    blk_rows = tile_mask.shape[-1]
    rows_px = lax.axis_size("px")
    rows_py = lax.axis_size("py")
    devices = rows_px * rows_py
    score_scale = 1.0 / math.sqrt(latent_width)
    pre_act = dense(latent, w_e1)
    activation = jax.nn.silu(pre_act).astype(jnp.bfloat16)
    message = dense(activation, w_e2).astype(jnp.bfloat16)
    sources = [
        message,
        passed_along(message, "px", 1),
        passed_along(message, "px", -1),
        passed_along(message, "py", 1),
        passed_along(message, "py", -1),
    ]
    src_ids = tile_src[0, 0].reshape(-1)
    gathered = tile_gather(
        src_ids,
        tile_mask[0, 0],
        [part.reshape(block_count, blk_rows, latent_width) for part in sources],
    )
    zvalue = dense(latent, w_n1[:latent_width]) + dense(gathered, w_n1[latent_width:])
    hidden = jax.nn.silu(zvalue).astype(jnp.bfloat16)
    updated = (latent.astype(jnp.float32) + dense(hidden, w_n2)).astype(jnp.bfloat16)
    queries = dense(updated, w_q).astype(jnp.bfloat16)
    own_tokens = tokens[0]
    slot_count = own_tokens.shape[0] // devices
    token_groups = own_tokens.reshape(devices, slot_count, latent_width)
    arrived_tokens = lax.all_to_all(
        token_groups, ("px", "py"), split_axis=0, concat_axis=0, tiled=True
    )
    arrived_tokens = arrived_tokens.reshape(devices * slot_count, latent_width)
    arrived = dense(arrived_tokens, w_kv).astype(jnp.bfloat16)
    live_keys = (jnp.arange(slot_count)[None, :] < tok_count[:, 0][:, None]).reshape(1, -1)
    grad_out = dense(cotangent[0, 0], w_o.T).astype(jnp.bfloat16)
    grad_query, grad_kv = attend_back(
        live_keys.astype(jnp.float32), queries, grad_out, arrived, score_scale
    )
    grad_slots = dense(grad_kv, w_kv.T).astype(jnp.bfloat16)
    returned = lax.all_to_all(
        grad_slots.reshape(devices, slot_count, latent_width),
        ("px", "py"),
        split_axis=0,
        concat_axis=0,
        tiled=True,
    )
    grad_tokens = returned.reshape(devices * slot_count, latent_width)
    grad_update = cotangent[0, 0].astype(jnp.float32) + dense(grad_query, w_q.T)
    update_low = grad_update.astype(jnp.bfloat16)
    grad_z = (dense(update_low, w_n2.T) * silu_slope(zvalue)).astype(jnp.bfloat16)
    grad_agg = dense(grad_z, w_n1[latent_width:].T).astype(jnp.bfloat16)
    grad_node = grad_update + dense(grad_z, w_n1[:latent_width].T)
    own_part, outbound = tile_scatter(src_ids, tile_mask[0, 0], grad_agg, len(sources))
    outbound = outbound.reshape(len(sources) - 1, node_rows, latent_width)
    received = [
        passed_along(outbound[0], "px", -1),
        passed_along(outbound[1], "px", 1),
        passed_along(outbound[2], "py", -1),
        passed_along(outbound[3], "py", 1),
    ]
    grad_nodes = edge_back(
        latent, own_part.reshape(node_rows, latent_width), received, grad_node, w_e1, w_e2
    )
    return (grad_nodes[None, None], grad_tokens[None])


def solution(mesh):
    return jax.shard_map(
        on_device,
        mesh=mesh,
        in_specs=(
            P("px", "py", None, None),
            P("px", "py", None, None),
            P("px", "py", None, None, None, None),
            P(("px", "py"), None, None),
            P(None, ("px", "py")),
            P(),
            P(),
            P(),
            P(),
            P(),
            P(),
            P(),
            P("px", "py", None, None),
        ),
        out_specs=(P("px", "py", None, None), P(("px", "py"), None, None)),
        check_vma=False,
    )
```

```python
import functools
import math

import jax
import jax.numpy as jnp
from jax import lax
from jax.experimental import pallas as pl
from jax.experimental.pallas import tpu as pltpu
from jax.sharding import PartitionSpec as P


def with_halo(block, sides, width):
    for axis, dim in sides:
        count = lax.axis_size(axis)
        forward = [(i, i + 1) for i in range(count - 1)]
        backward = [(target, source) for source, target in forward]
        low = lax.ppermute(
            lax.slice_in_dim(block, block.shape[dim] - width, None, axis=dim), axis, forward
        )
        high = lax.ppermute(lax.slice_in_dim(block, 0, width, axis=dim), axis, backward)
        block = jnp.concatenate([low, block, high], axis=dim)
    return block


def passed_along(value, axis, steps):
    count = lax.axis_size(axis)
    leading, last = (max(0, -steps), min(count, count - steps))
    return lax.ppermute(value, axis, [(source, source + steps) for source in range(leading, last)])


def gather_kernel(group, src_ids, mask_ref, own, up, down, left, right, out_ref, rhs):
    step = pl.program_id(0)
    tiles = mask_ref.shape[1]
    blk = mask_ref.shape[2]
    per_side = own.shape[0]
    for g in range(group):
        for k in range(tiles):
            picked = src_ids[(step * group + g) * tiles + k]
            side = picked // per_side
            block = picked % per_side
            for index, ref in enumerate((own, up, down, left, right)):

                @pl.when(side == index)
                def _():
                    rhs[k * blk : (k + 1) * blk, :] = ref[block]

        bits = jnp.concatenate(
            [mask_ref[g, k].astype(jnp.float32).astype(jnp.bfloat16) for k in range(tiles)], axis=1
        )
        total = jnp.dot(bits, rhs[...], preferred_element_type=jnp.float32)
        out_ref[g * blk : (g + 1) * blk, :] = total.astype(out_ref.dtype)


def tile_gather(src_ids, tile_mask, sources, group=4):
    blocks, tiles, blk, _ = tile_mask.shape
    width = sources[0].shape[-1]
    whole = pl.BlockSpec((blocks, blk, width), lambda i, ids: (0, 0, 0))
    return pl.pallas_call(
        functools.partial(gather_kernel, group),
        grid_spec=pltpu.PrefetchScalarGridSpec(
            num_scalar_prefetch=1,
            grid=(blocks // group,),
            in_specs=[pl.BlockSpec((group, tiles, blk, blk), lambda i, ids: (i, 0, 0, 0))]
            + [whole] * len(sources),
            out_specs=pl.BlockSpec((group * blk, width), lambda i, ids: (i, 0)),
            scratch_shapes=[pltpu.VMEM((tiles * blk, width), jnp.bfloat16)],
        ),
        out_shape=jax.ShapeDtypeStruct((blocks * blk, width), jnp.bfloat16),
        compiler_params=pltpu.CompilerParams(dimension_semantics=("arbitrary",)),
    )(src_ids, tile_mask, *sources)


def scatter_kernel(group, src_ids, mask_ref, grad_ref, own_ref, *rest):
    side_refs, total = rest[:-1], rest[-1]
    step = pl.program_id(0)
    tiles = mask_ref.shape[1]
    blk = mask_ref.shape[2]
    per_side = own_ref.shape[0]
    tn = (((0,), (0,)), ((), ()))

    @pl.when(step == 0)
    def _():
        total[...] = jnp.zeros(total.shape, jnp.float32)

    for g in range(group):
        bits = jnp.concatenate(
            [mask_ref[g, k].astype(jnp.float32).astype(jnp.bfloat16) for k in range(tiles)], axis=1
        )
        grad_rows = grad_ref[g * blk : (g + 1) * blk, :]
        parts = lax.dot_general(bits, grad_rows, tn, preferred_element_type=jnp.float32)
        for k in range(tiles):
            picked = src_ids[(step * group + g) * tiles + k]
            total[picked] += parts[k * blk : (k + 1) * blk]

    @pl.when(step == pl.num_programs(0) - 1)
    def _():
        own_ref[...] = total[0:per_side]
        for side, out_ref in enumerate(side_refs):
            start = (side + 1) * per_side
            out_ref[...] = total[start : start + per_side].astype(out_ref.dtype)


def tile_scatter(src_ids, tile_mask, grad_agg, sides, group=4):
    blocks, tiles, blk, _ = tile_mask.shape
    width = grad_agg.shape[-1]
    return pl.pallas_call(
        functools.partial(scatter_kernel, group),
        grid_spec=pltpu.PrefetchScalarGridSpec(
            num_scalar_prefetch=1,
            grid=(blocks // group,),
            in_specs=[
                pl.BlockSpec((group, tiles, blk, blk), lambda i, ids: (i, 0, 0, 0)),
                pl.BlockSpec((group * blk, width), lambda i, ids: (i, 0)),
            ],
            out_specs=[pl.BlockSpec((blocks, blk, width), lambda i, ids: (0, 0, 0))] * sides,
            scratch_shapes=[pltpu.VMEM((sides * blocks, blk, width), jnp.float32)],
        ),
        out_shape=[jax.ShapeDtypeStruct((blocks, blk, width), jnp.float32)]
        + [jax.ShapeDtypeStruct((blocks, blk, width), jnp.bfloat16)] * (sides - 1),
        compiler_params=pltpu.CompilerParams(dimension_semantics=("arbitrary",)),
    )(src_ids, tile_mask, grad_agg)


def attend_kernel(scale, live_ref, q_ref, go_ref, kv_ref, gq_ref, gkv_ref, gk_acc, gv_acc):
    step = pl.program_id(0)
    width = q_ref.shape[1]

    @pl.when(step == 0)
    def _():
        gk_acc[...] = jnp.zeros(gk_acc.shape, jnp.float32)
        gv_acc[...] = jnp.zeros(gv_acc.shape, jnp.float32)

    queries = q_ref[...]
    grad_out = go_ref[...]
    keys = kv_ref[:, 0:width]
    values = kv_ref[:, width : 2 * width]
    nt = (((1,), (1,)), ((), ()))
    tn = (((0,), (0,)), ((), ()))
    scores = lax.dot_general(queries, keys, nt, preferred_element_type=jnp.float32) * scale
    scores = jnp.where(live_ref[...] > 0, scores, -jnp.inf)
    highest = jnp.max(scores, axis=1, keepdims=True)
    expo_terms = jnp.exp(scores - highest)
    probability = expo_terms / jnp.sum(expo_terms, axis=1, keepdims=True)
    prob_low = probability.astype(jnp.bfloat16)
    grad_prob = lax.dot_general(grad_out, values, nt, preferred_element_type=jnp.float32)
    spread = jnp.sum(probability * grad_prob, axis=1, keepdims=True)
    grad_score = (probability * (grad_prob - spread) * scale).astype(jnp.bfloat16)
    gq_ref[...] = jnp.dot(grad_score, keys, preferred_element_type=jnp.float32).astype(gq_ref.dtype)
    gk_acc[...] += lax.dot_general(grad_score, queries, tn, preferred_element_type=jnp.float32)
    gv_acc[...] += lax.dot_general(prob_low, grad_out, tn, preferred_element_type=jnp.float32)

    @pl.when(step == pl.num_programs(0) - 1)
    def _():
        gkv_ref[:, 0:width] = gk_acc[...].astype(gkv_ref.dtype)
        gkv_ref[:, width : 2 * width] = gv_acc[...].astype(gkv_ref.dtype)


def attend_back(live, queries, grad_out, keyvals, scale, rows_per_step=256):
    rows, width = queries.shape
    slots = keyvals.shape[0]
    steps = rows // rows_per_step
    row_block = pl.BlockSpec((rows_per_step, width), lambda i: (i, 0))
    return pl.pallas_call(
        functools.partial(attend_kernel, scale),
        grid=(steps,),
        in_specs=[
            pl.BlockSpec((1, slots), lambda i: (0, 0)),
            row_block,
            row_block,
            pl.BlockSpec((slots, 2 * width), lambda i: (0, 0)),
        ],
        out_specs=[row_block, pl.BlockSpec((slots, 2 * width), lambda i: (0, 0))],
        out_shape=(
            jax.ShapeDtypeStruct((rows, width), jnp.bfloat16),
            jax.ShapeDtypeStruct((slots, 2 * width), jnp.bfloat16),
        ),
        scratch_shapes=[
            pltpu.VMEM((slots, width), jnp.float32),
            pltpu.VMEM((slots, width), jnp.float32),
        ],
        compiler_params=pltpu.CompilerParams(dimension_semantics=("arbitrary",)),
        cost_estimate=pl.CostEstimate(
            flops=10 * rows * slots * width,
            transcendentals=rows * slots,
            bytes_accessed=2 * (3 * rows * width + 4 * slots * width),
        ),
    )(live, queries, grad_out, keyvals)


def slope_of(values):
    sigma = 1.0 / (1.0 + jnp.exp(-values))
    return sigma * (1.0 + values * (1.0 - sigma))


def edge_back_kernel(lat_ref, own_ref, a_ref, b_ref, c_ref, d_ref, gn_ref, w1_ref, w2_ref, out_ref):
    nt = (((1,), (1,)), ((), ()))
    collected = own_ref[...]
    for ref in (a_ref, b_ref, c_ref, d_ref):
        collected = collected + ref[...].astype(jnp.float32)
    grad_msg = collected.astype(jnp.bfloat16)
    pre_act = jnp.dot(lat_ref[...], w1_ref[...], preferred_element_type=jnp.float32)
    grad_pre = lax.dot_general(grad_msg, w2_ref[...], nt, preferred_element_type=jnp.float32)
    grad_pre = (grad_pre * slope_of(pre_act)).astype(jnp.bfloat16)
    total = gn_ref[...] + lax.dot_general(grad_pre, w1_ref[...], nt, preferred_element_type=jnp.float32)
    out_ref[...] = total.astype(out_ref.dtype)


def edge_back(latent, own_part, received, grad_node, w_e1, w_e2, rows_per_step=512):
    rows, width = latent.shape
    row_block = pl.BlockSpec((rows_per_step, width), lambda i: (i, 0))
    weight = pl.BlockSpec(w_e1.shape, lambda i: (0, 0))
    return pl.pallas_call(
        edge_back_kernel,
        grid=(rows // rows_per_step,),
        in_specs=[row_block] * (3 + len(received)) + [weight, weight],
        out_specs=row_block,
        out_shape=jax.ShapeDtypeStruct((rows, width), jnp.bfloat16),
        cost_estimate=pl.CostEstimate(
            flops=6 * rows * width * width,
            transcendentals=rows * width,
            bytes_accessed=rows * width * (2 + 4 + 2 * len(received) + 4 + 2),
        ),
    )(latent, own_part, *received, grad_node, w_e1, w_e2)


def dense(left, right):
    return jnp.dot(left, right, preferred_element_type=jnp.float32)


def silu_slope(values):
    sigma = jax.nn.sigmoid(values)
    return sigma * (1.0 + values * (1.0 - sigma))


def on_device(
    nodes, tile_src, tile_mask, tokens, tok_count, w_e1, w_e2, w_n1, w_n2, w_q, w_kv, w_o, cotangent
):
    latent = nodes[0, 0]
    node_rows = latent.shape[0]
    latent_width = latent.shape[1]
    block_count = tile_src.shape[2]
    tile_count = tile_src.shape[3]
    blk_rows = tile_mask.shape[-1]
    rows_px = lax.axis_size("px")
    rows_py = lax.axis_size("py")
    devices = rows_px * rows_py
    score_scale = 1.0 / math.sqrt(latent_width)
    pre_act = dense(latent, w_e1)
    activation = jax.nn.silu(pre_act).astype(jnp.bfloat16)
    message = dense(activation, w_e2).astype(jnp.bfloat16)
    sources = [
        message,
        passed_along(message, "px", 1),
        passed_along(message, "px", -1),
        passed_along(message, "py", 1),
        passed_along(message, "py", -1),
    ]
    src_ids = tile_src[0, 0].reshape(-1)
    gathered = tile_gather(
        src_ids,
        tile_mask[0, 0],
        [part.reshape(block_count, blk_rows, latent_width) for part in sources],
    )
    zvalue = dense(latent, w_n1[:latent_width]) + dense(gathered, w_n1[latent_width:])
    hidden = jax.nn.silu(zvalue).astype(jnp.bfloat16)
    updated = (latent.astype(jnp.float32) + dense(hidden, w_n2)).astype(jnp.bfloat16)
    queries = dense(updated, w_q).astype(jnp.bfloat16)
    own_tokens = tokens[0]
    slot_count = own_tokens.shape[0] // devices
    token_groups = own_tokens.reshape(devices, slot_count, latent_width)
    arrived_tokens = lax.all_to_all(
        token_groups, ("px", "py"), split_axis=0, concat_axis=0, tiled=True
    )
    arrived_tokens = arrived_tokens.reshape(devices * slot_count, latent_width)
    arrived = dense(arrived_tokens, w_kv).astype(jnp.bfloat16)
    live_keys = (jnp.arange(slot_count)[None, :] < tok_count[:, 0][:, None]).reshape(1, -1)
    grad_out = dense(cotangent[0, 0], w_o.T).astype(jnp.bfloat16)
    grad_query, grad_kv = attend_back(
        live_keys.astype(jnp.float32), queries, grad_out, arrived, score_scale
    )
    grad_slots = dense(grad_kv, w_kv.T).astype(jnp.bfloat16)
    returned = lax.all_to_all(
        grad_slots.reshape(devices, slot_count, latent_width),
        ("px", "py"),
        split_axis=0,
        concat_axis=0,
        tiled=True,
    )
    grad_tokens = returned.reshape(devices * slot_count, latent_width)
    grad_update = cotangent[0, 0].astype(jnp.float32) + dense(grad_query, w_q.T)
    update_low = grad_update.astype(jnp.bfloat16)
    grad_z = (dense(update_low, w_n2.T) * silu_slope(zvalue)).astype(jnp.bfloat16)
    grad_agg = dense(grad_z, w_n1[latent_width:].T).astype(jnp.bfloat16)
    grad_node = grad_update + dense(grad_z, w_n1[:latent_width].T)
    own_part, *outbound = tile_scatter(src_ids, tile_mask[0, 0], grad_agg, len(sources))
    outbound = [part.reshape(node_rows, latent_width) for part in outbound]
    received = [
        passed_along(outbound[0], "px", -1),
        passed_along(outbound[1], "px", 1),
        passed_along(outbound[2], "py", -1),
        passed_along(outbound[3], "py", 1),
    ]
    grad_nodes = edge_back(
        latent, own_part.reshape(node_rows, latent_width), received, grad_node, w_e1, w_e2
    )
    return (grad_nodes[None, None], grad_tokens[None])


def solution(mesh):
    return jax.shard_map(
        on_device,
        mesh=mesh,
        in_specs=(
            P("px", "py", None, None),
            P("px", "py", None, None),
            P("px", "py", None, None, None, None),
            P(("px", "py"), None, None),
            P(None, ("px", "py")),
            P(),
            P(),
            P(),
            P(),
            P(),
            P(),
            P(),
            P("px", "py", None, None),
        ),
        out_specs=(P("px", "py", None, None), P(("px", "py"), None, None)),
        check_vma=False,
    )
```

```python
import functools
import math

import jax
import jax.numpy as jnp
from jax import lax
from jax.experimental import pallas as pl
from jax.experimental.pallas import tpu as pltpu
from jax.sharding import PartitionSpec as P


def with_halo(block, sides, width):
    for axis, dim in sides:
        count = lax.axis_size(axis)
        forward = [(i, i + 1) for i in range(count - 1)]
        backward = [(target, source) for source, target in forward]
        low = lax.ppermute(
            lax.slice_in_dim(block, block.shape[dim] - width, None, axis=dim), axis, forward
        )
        high = lax.ppermute(lax.slice_in_dim(block, 0, width, axis=dim), axis, backward)
        block = jnp.concatenate([low, block, high], axis=dim)
    return block


def passed_along(value, axis, steps):
    count = lax.axis_size(axis)
    leading, last = (max(0, -steps), min(count, count - steps))
    return lax.ppermute(value, axis, [(source, source + steps) for source in range(leading, last)])


def gather_kernel(group, src_ids, mask_ref, own, up, down, left, right, out_ref, rhs):
    step = pl.program_id(0)
    tiles = mask_ref.shape[1]
    blk = mask_ref.shape[2]
    per_side = own.shape[0]
    for g in range(group):
        for k in range(tiles):
            picked = src_ids[(step * group + g) * tiles + k]
            side = picked // per_side
            block = picked % per_side
            for index, ref in enumerate((own, up, down, left, right)):

                @pl.when(side == index)
                def _():
                    rhs[k * blk : (k + 1) * blk, :] = ref[block]

        bits = jnp.concatenate(
            [mask_ref[g, k].astype(jnp.float32).astype(jnp.bfloat16) for k in range(tiles)], axis=1
        )
        total = jnp.dot(bits, rhs[...], preferred_element_type=jnp.float32)
        out_ref[g * blk : (g + 1) * blk, :] = total.astype(out_ref.dtype)


def tile_gather(src_ids, tile_mask, sources, group=4):
    blocks, tiles, blk, _ = tile_mask.shape
    width = sources[0].shape[-1]
    whole = pl.BlockSpec((blocks, blk, width), lambda i, ids: (0, 0, 0))
    return pl.pallas_call(
        functools.partial(gather_kernel, group),
        grid_spec=pltpu.PrefetchScalarGridSpec(
            num_scalar_prefetch=1,
            grid=(blocks // group,),
            in_specs=[pl.BlockSpec((group, tiles, blk, blk), lambda i, ids: (i, 0, 0, 0))]
            + [whole] * len(sources),
            out_specs=pl.BlockSpec((group * blk, width), lambda i, ids: (i, 0)),
            scratch_shapes=[pltpu.VMEM((tiles * blk, width), jnp.bfloat16)],
        ),
        out_shape=jax.ShapeDtypeStruct((blocks * blk, width), jnp.bfloat16),
        compiler_params=pltpu.CompilerParams(dimension_semantics=("arbitrary",)),
    )(src_ids, tile_mask, *sources)


def scatter_kernel(group, src_ids, mask_ref, gq_ref, cot_ref, z_ref, wq_ref, wn2_ref, wn1_ref, gn_ref, own_ref, *rest):
    side_refs, total = rest[:-1], rest[-1]
    step = pl.program_id(0)
    tiles = mask_ref.shape[1]
    blk = mask_ref.shape[2]
    per_side = own_ref.shape[0]
    width = gq_ref.shape[1]
    tn = (((0,), (0,)), ((), ()))
    nt = (((1,), (1,)), ((), ()))
    grad_update = cot_ref[...].astype(jnp.float32) + lax.dot_general(
        gq_ref[...], wq_ref[...], nt, preferred_element_type=jnp.float32
    )
    update_low = grad_update.astype(jnp.bfloat16)
    grad_z = lax.dot_general(update_low, wn2_ref[...], nt, preferred_element_type=jnp.float32)
    grad_z = (grad_z * slope_of(z_ref[...])).astype(jnp.bfloat16)
    grad_agg = lax.dot_general(
        grad_z, wn1_ref[width : 2 * width, :], nt, preferred_element_type=jnp.float32
    ).astype(jnp.bfloat16)
    gn_ref[...] = grad_update + lax.dot_general(
        grad_z, wn1_ref[0:width, :], nt, preferred_element_type=jnp.float32
    )

    @pl.when(step == 0)
    def _():
        total[...] = jnp.zeros(total.shape, jnp.float32)

    for g in range(group):
        bits = jnp.concatenate(
            [mask_ref[g, k].astype(jnp.float32).astype(jnp.bfloat16) for k in range(tiles)], axis=1
        )
        grad_rows = grad_agg[g * blk : (g + 1) * blk, :]
        parts = lax.dot_general(bits, grad_rows, tn, preferred_element_type=jnp.float32)
        for k in range(tiles):
            picked = src_ids[(step * group + g) * tiles + k]
            total[picked] += parts[k * blk : (k + 1) * blk]

    @pl.when(step == pl.num_programs(0) - 1)
    def _():
        own_ref[...] = total[0:per_side]
        for side, out_ref in enumerate(side_refs):
            start = (side + 1) * per_side
            out_ref[...] = total[start : start + per_side].astype(out_ref.dtype)


def tile_scatter(src_ids, tile_mask, grad_query, cot, zvalue, w_q, w_n2, w_n1, sides, group=4):
    blocks, tiles, blk, _ = tile_mask.shape
    width = grad_query.shape[-1]
    rows = pl.BlockSpec((group * blk, width), lambda i, ids: (i, 0))
    return pl.pallas_call(
        functools.partial(scatter_kernel, group),
        grid_spec=pltpu.PrefetchScalarGridSpec(
            num_scalar_prefetch=1,
            grid=(blocks // group,),
            in_specs=[
                pl.BlockSpec((group, tiles, blk, blk), lambda i, ids: (i, 0, 0, 0)),
                rows,
                rows,
                rows,
                pl.BlockSpec(w_q.shape, lambda i, ids: (0, 0)),
                pl.BlockSpec(w_n2.shape, lambda i, ids: (0, 0)),
                pl.BlockSpec(w_n1.shape, lambda i, ids: (0, 0)),
            ],
            out_specs=[rows]
            + [pl.BlockSpec((blocks, blk, width), lambda i, ids: (0, 0, 0))] * sides,
            scratch_shapes=[pltpu.VMEM((sides * blocks, blk, width), jnp.float32)],
        ),
        out_shape=[jax.ShapeDtypeStruct((blocks * blk, width), jnp.float32)]
        + [jax.ShapeDtypeStruct((blocks, blk, width), jnp.float32)]
        + [jax.ShapeDtypeStruct((blocks, blk, width), jnp.bfloat16)] * (sides - 1),
        compiler_params=pltpu.CompilerParams(dimension_semantics=("arbitrary",)),
    )(src_ids, tile_mask, grad_query, cot, zvalue, w_q, w_n2, w_n1)


def attend_kernel(scale, live_ref, q_ref, go_ref, kv_ref, wkv_ref, gq_ref, slots_ref, gk_acc, gv_acc):
    step = pl.program_id(0)
    width = q_ref.shape[1]

    @pl.when(step == 0)
    def _():
        gk_acc[...] = jnp.zeros(gk_acc.shape, jnp.float32)
        gv_acc[...] = jnp.zeros(gv_acc.shape, jnp.float32)

    queries = q_ref[...]
    grad_out = go_ref[...]
    keys = kv_ref[:, 0:width]
    values = kv_ref[:, width : 2 * width]
    nt = (((1,), (1,)), ((), ()))
    tn = (((0,), (0,)), ((), ()))
    scores = lax.dot_general(queries, keys, nt, preferred_element_type=jnp.float32) * scale
    scores = jnp.where(live_ref[...] > 0, scores, -jnp.inf)
    highest = jnp.max(scores, axis=1, keepdims=True)
    expo_terms = jnp.exp(scores - highest)
    probability = expo_terms / jnp.sum(expo_terms, axis=1, keepdims=True)
    prob_low = probability.astype(jnp.bfloat16)
    grad_prob = lax.dot_general(grad_out, values, nt, preferred_element_type=jnp.float32)
    spread = jnp.sum(probability * grad_prob, axis=1, keepdims=True)
    grad_score = (probability * (grad_prob - spread) * scale).astype(jnp.bfloat16)
    gq_ref[...] = jnp.dot(grad_score, keys, preferred_element_type=jnp.float32).astype(gq_ref.dtype)
    gk_acc[...] += lax.dot_general(grad_score, queries, tn, preferred_element_type=jnp.float32)
    gv_acc[...] += lax.dot_general(prob_low, grad_out, tn, preferred_element_type=jnp.float32)

    @pl.when(step == pl.num_programs(0) - 1)
    def _():
        grad_keys = gk_acc[...].astype(jnp.bfloat16)
        grad_vals = gv_acc[...].astype(jnp.bfloat16)
        slots = lax.dot_general(grad_keys, wkv_ref[:, 0:width], nt, preferred_element_type=jnp.float32)
        slots += lax.dot_general(grad_vals, wkv_ref[:, width : 2 * width], nt, preferred_element_type=jnp.float32)
        slots_ref[...] = slots.astype(slots_ref.dtype)


def attend_back(live, queries, grad_out, keyvals, w_kv, scale, rows_per_step=256):
    rows, width = queries.shape
    slots = keyvals.shape[0]
    steps = rows // rows_per_step
    row_block = pl.BlockSpec((rows_per_step, width), lambda i: (i, 0))
    return pl.pallas_call(
        functools.partial(attend_kernel, scale),
        grid=(steps,),
        in_specs=[
            pl.BlockSpec((1, slots), lambda i: (0, 0)),
            row_block,
            row_block,
            pl.BlockSpec((slots, 2 * width), lambda i: (0, 0)),
            pl.BlockSpec(w_kv.shape, lambda i: (0, 0)),
        ],
        out_specs=[row_block, pl.BlockSpec((slots, width), lambda i: (0, 0))],
        out_shape=(
            jax.ShapeDtypeStruct((rows, width), jnp.bfloat16),
            jax.ShapeDtypeStruct((slots, width), jnp.bfloat16),
        ),
        scratch_shapes=[
            pltpu.VMEM((slots, width), jnp.float32),
            pltpu.VMEM((slots, width), jnp.float32),
        ],
        compiler_params=pltpu.CompilerParams(dimension_semantics=("arbitrary",)),
        cost_estimate=pl.CostEstimate(
            flops=10 * rows * slots * width,
            transcendentals=rows * slots,
            bytes_accessed=2 * (3 * rows * width + 4 * slots * width),
        ),
    )(live, queries, grad_out, keyvals, w_kv)


def slope_of(values):
    sigma = 1.0 / (1.0 + jnp.exp(-values))
    return sigma * (1.0 + values * (1.0 - sigma))


def edge_back_kernel(lat_ref, own_ref, a_ref, b_ref, c_ref, d_ref, gn_ref, w1_ref, w2_ref, out_ref):
    nt = (((1,), (1,)), ((), ()))
    collected = own_ref[...]
    for ref in (a_ref, b_ref, c_ref, d_ref):
        collected = collected + ref[...].astype(jnp.float32)
    grad_msg = collected.astype(jnp.bfloat16)
    pre_act = jnp.dot(lat_ref[...], w1_ref[...], preferred_element_type=jnp.float32)
    grad_pre = lax.dot_general(grad_msg, w2_ref[...], nt, preferred_element_type=jnp.float32)
    grad_pre = (grad_pre * slope_of(pre_act)).astype(jnp.bfloat16)
    total = gn_ref[...] + lax.dot_general(grad_pre, w1_ref[...], nt, preferred_element_type=jnp.float32)
    out_ref[...] = total.astype(out_ref.dtype)


def edge_back(latent, own_part, received, grad_node, w_e1, w_e2, rows_per_step=512):
    rows, width = latent.shape
    row_block = pl.BlockSpec((rows_per_step, width), lambda i: (i, 0))
    weight = pl.BlockSpec(w_e1.shape, lambda i: (0, 0))
    return pl.pallas_call(
        edge_back_kernel,
        grid=(rows // rows_per_step,),
        in_specs=[row_block] * (3 + len(received)) + [weight, weight],
        out_specs=row_block,
        out_shape=jax.ShapeDtypeStruct((rows, width), jnp.bfloat16),
        cost_estimate=pl.CostEstimate(
            flops=6 * rows * width * width,
            transcendentals=rows * width,
            bytes_accessed=rows * width * (2 + 4 + 2 * len(received) + 4 + 2),
        ),
    )(latent, own_part, *received, grad_node, w_e1, w_e2)


def dense(left, right):
    return jnp.dot(left, right, preferred_element_type=jnp.float32)


def silu_slope(values):
    sigma = jax.nn.sigmoid(values)
    return sigma * (1.0 + values * (1.0 - sigma))


def on_device(
    nodes, tile_src, tile_mask, tokens, tok_count, w_e1, w_e2, w_n1, w_n2, w_q, w_kv, w_o, cotangent
):
    latent = nodes[0, 0]
    node_rows = latent.shape[0]
    latent_width = latent.shape[1]
    block_count = tile_src.shape[2]
    tile_count = tile_src.shape[3]
    blk_rows = tile_mask.shape[-1]
    rows_px = lax.axis_size("px")
    rows_py = lax.axis_size("py")
    devices = rows_px * rows_py
    score_scale = 1.0 / math.sqrt(latent_width)
    pre_act = dense(latent, w_e1)
    activation = jax.nn.silu(pre_act).astype(jnp.bfloat16)
    message = dense(activation, w_e2).astype(jnp.bfloat16)
    sources = [
        message,
        passed_along(message, "px", 1),
        passed_along(message, "px", -1),
        passed_along(message, "py", 1),
        passed_along(message, "py", -1),
    ]
    src_ids = tile_src[0, 0].reshape(-1)
    gathered = tile_gather(
        src_ids,
        tile_mask[0, 0],
        [part.reshape(block_count, blk_rows, latent_width) for part in sources],
    )
    zvalue = dense(latent, w_n1[:latent_width]) + dense(gathered, w_n1[latent_width:])
    hidden = jax.nn.silu(zvalue).astype(jnp.bfloat16)
    updated = (latent.astype(jnp.float32) + dense(hidden, w_n2)).astype(jnp.bfloat16)
    queries = dense(updated, w_q).astype(jnp.bfloat16)
    own_tokens = tokens[0]
    slot_count = own_tokens.shape[0] // devices
    token_groups = own_tokens.reshape(devices, slot_count, latent_width)
    arrived_tokens = lax.all_to_all(
        token_groups, ("px", "py"), split_axis=0, concat_axis=0, tiled=True
    )
    arrived_tokens = arrived_tokens.reshape(devices * slot_count, latent_width)
    arrived = dense(arrived_tokens, w_kv).astype(jnp.bfloat16)
    live_keys = (jnp.arange(slot_count)[None, :] < tok_count[:, 0][:, None]).reshape(1, -1)
    grad_out = dense(cotangent[0, 0], w_o.T).astype(jnp.bfloat16)
    grad_query, grad_slots = attend_back(
        live_keys.astype(jnp.float32), queries, grad_out, arrived, w_kv, score_scale
    )
    returned = lax.all_to_all(
        grad_slots.reshape(devices, slot_count, latent_width),
        ("px", "py"),
        split_axis=0,
        concat_axis=0,
        tiled=True,
    )
    grad_tokens = returned.reshape(devices * slot_count, latent_width)
    grad_node, own_part, *outbound = tile_scatter(
        src_ids, tile_mask[0, 0], grad_query, cotangent[0, 0], zvalue, w_q, w_n2, w_n1, len(sources)
    )
    outbound = [part.reshape(node_rows, latent_width) for part in outbound]
    received = [
        passed_along(outbound[0], "px", -1),
        passed_along(outbound[1], "px", 1),
        passed_along(outbound[2], "py", -1),
        passed_along(outbound[3], "py", 1),
    ]
    grad_nodes = edge_back(
        latent, own_part.reshape(node_rows, latent_width), received, grad_node, w_e1, w_e2
    )
    return (grad_nodes[None, None], grad_tokens[None])


def solution(mesh):
    return jax.shard_map(
        on_device,
        mesh=mesh,
        in_specs=(
            P("px", "py", None, None),
            P("px", "py", None, None),
            P("px", "py", None, None, None, None),
            P(("px", "py"), None, None),
            P(None, ("px", "py")),
            P(),
            P(),
            P(),
            P(),
            P(),
            P(),
            P(),
            P("px", "py", None, None),
        ),
        out_specs=(P("px", "py", None, None), P(("px", "py"), None, None)),
        check_vma=False,
    )
```

```python
import functools
import math

import jax
import jax.numpy as jnp
from jax import lax
from jax.experimental import pallas as pl
from jax.experimental.pallas import tpu as pltpu
from jax.sharding import PartitionSpec as P


def with_halo(block, sides, width):
    for axis, dim in sides:
        count = lax.axis_size(axis)
        forward = [(i, i + 1) for i in range(count - 1)]
        backward = [(target, source) for source, target in forward]
        low = lax.ppermute(
            lax.slice_in_dim(block, block.shape[dim] - width, None, axis=dim), axis, forward
        )
        high = lax.ppermute(lax.slice_in_dim(block, 0, width, axis=dim), axis, backward)
        block = jnp.concatenate([low, block, high], axis=dim)
    return block


def passed_along(value, axis, steps):
    count = lax.axis_size(axis)
    leading, last = (max(0, -steps), min(count, count - steps))
    return lax.ppermute(value, axis, [(source, source + steps) for source in range(leading, last)])


def gather_kernel(
    group, src_ids, mask_ref, own, up, down, left, right, lat_ref, wn1_ref, wn2_ref, wq_ref,
    z_ref, q_ref, rhs, gath
):
    step = pl.program_id(0)
    tiles = mask_ref.shape[1]
    blk = mask_ref.shape[2]
    per_side = own.shape[0]
    for g in range(group):
        for k in range(tiles):
            picked = src_ids[(step * group + g) * tiles + k]
            side = picked // per_side
            block = picked % per_side
            for index, ref in enumerate((own, up, down, left, right)):

                @pl.when(side == index)
                def _():
                    rhs[k * blk : (k + 1) * blk, :] = ref[block]

        bits = jnp.concatenate(
            [mask_ref[g, k].astype(jnp.float32).astype(jnp.bfloat16) for k in range(tiles)], axis=1
        )
        total = jnp.dot(bits, rhs[...], preferred_element_type=jnp.float32)
        gath[g * blk : (g + 1) * blk, :] = total.astype(gath.dtype)
    width = lat_ref.shape[1]
    latent = lat_ref[...]
    zvalue = jnp.dot(latent, wn1_ref[0:width, :], preferred_element_type=jnp.float32)
    zvalue += jnp.dot(gath[...], wn1_ref[width : 2 * width, :], preferred_element_type=jnp.float32)
    z_ref[...] = zvalue
    hidden = (zvalue / (1.0 + jnp.exp(-zvalue))).astype(jnp.bfloat16)
    updated = latent.astype(jnp.float32) + jnp.dot(hidden, wn2_ref[...], preferred_element_type=jnp.float32)
    queries = jnp.dot(updated.astype(jnp.bfloat16), wq_ref[...], preferred_element_type=jnp.float32)
    q_ref[...] = queries.astype(q_ref.dtype)


def tile_gather(src_ids, tile_mask, sources, latent, w_n1, w_n2, w_q, group=4):
    blocks, tiles, blk, _ = tile_mask.shape
    width = sources[0].shape[-1]
    whole = pl.BlockSpec((blocks, blk, width), lambda i, ids: (0, 0, 0))
    rows = pl.BlockSpec((group * blk, width), lambda i, ids: (i, 0))
    return pl.pallas_call(
        functools.partial(gather_kernel, group),
        grid_spec=pltpu.PrefetchScalarGridSpec(
            num_scalar_prefetch=1,
            grid=(blocks // group,),
            in_specs=[pl.BlockSpec((group, tiles, blk, blk), lambda i, ids: (i, 0, 0, 0))]
            + [whole] * len(sources)
            + [rows]
            + [pl.BlockSpec(w.shape, lambda i, ids: (0, 0)) for w in (w_n1, w_n2, w_q)],
            out_specs=[rows, rows],
            scratch_shapes=[
                pltpu.VMEM((tiles * blk, width), jnp.bfloat16),
                pltpu.VMEM((group * blk, width), jnp.bfloat16),
            ],
        ),
        out_shape=(
            jax.ShapeDtypeStruct((blocks * blk, width), jnp.float32),
            jax.ShapeDtypeStruct((blocks * blk, width), jnp.bfloat16),
        ),
        compiler_params=pltpu.CompilerParams(dimension_semantics=("arbitrary",)),
    )(src_ids, tile_mask, *sources, latent, w_n1, w_n2, w_q)


def scatter_kernel(group, src_ids, mask_ref, gq_ref, cot_ref, z_ref, wq_ref, wn2_ref, wn1_ref, gn_ref, own_ref, *rest):
    side_refs, total = rest[:-1], rest[-1]
    step = pl.program_id(0)
    tiles = mask_ref.shape[1]
    blk = mask_ref.shape[2]
    per_side = own_ref.shape[0]
    width = gq_ref.shape[1]
    tn = (((0,), (0,)), ((), ()))
    nt = (((1,), (1,)), ((), ()))
    grad_update = cot_ref[...].astype(jnp.float32) + lax.dot_general(
        gq_ref[...], wq_ref[...], nt, preferred_element_type=jnp.float32
    )
    update_low = grad_update.astype(jnp.bfloat16)
    grad_z = lax.dot_general(update_low, wn2_ref[...], nt, preferred_element_type=jnp.float32)
    grad_z = (grad_z * slope_of(z_ref[...])).astype(jnp.bfloat16)
    grad_agg = lax.dot_general(
        grad_z, wn1_ref[width : 2 * width, :], nt, preferred_element_type=jnp.float32
    ).astype(jnp.bfloat16)
    gn_ref[...] = grad_update + lax.dot_general(
        grad_z, wn1_ref[0:width, :], nt, preferred_element_type=jnp.float32
    )

    @pl.when(step == 0)
    def _():
        total[...] = jnp.zeros(total.shape, jnp.float32)

    for g in range(group):
        bits = jnp.concatenate(
            [mask_ref[g, k].astype(jnp.float32).astype(jnp.bfloat16) for k in range(tiles)], axis=1
        )
        grad_rows = grad_agg[g * blk : (g + 1) * blk, :]
        parts = lax.dot_general(bits, grad_rows, tn, preferred_element_type=jnp.float32)
        for k in range(tiles):
            picked = src_ids[(step * group + g) * tiles + k]
            total[picked] += parts[k * blk : (k + 1) * blk]

    @pl.when(step == pl.num_programs(0) - 1)
    def _():
        own_ref[...] = total[0:per_side]
        for side, out_ref in enumerate(side_refs):
            start = (side + 1) * per_side
            out_ref[...] = total[start : start + per_side].astype(out_ref.dtype)


def tile_scatter(src_ids, tile_mask, grad_query, cot, zvalue, w_q, w_n2, w_n1, sides, group=4):
    blocks, tiles, blk, _ = tile_mask.shape
    width = grad_query.shape[-1]
    rows = pl.BlockSpec((group * blk, width), lambda i, ids: (i, 0))
    return pl.pallas_call(
        functools.partial(scatter_kernel, group),
        grid_spec=pltpu.PrefetchScalarGridSpec(
            num_scalar_prefetch=1,
            grid=(blocks // group,),
            in_specs=[
                pl.BlockSpec((group, tiles, blk, blk), lambda i, ids: (i, 0, 0, 0)),
                rows,
                rows,
                rows,
                pl.BlockSpec(w_q.shape, lambda i, ids: (0, 0)),
                pl.BlockSpec(w_n2.shape, lambda i, ids: (0, 0)),
                pl.BlockSpec(w_n1.shape, lambda i, ids: (0, 0)),
            ],
            out_specs=[rows]
            + [pl.BlockSpec((blocks, blk, width), lambda i, ids: (0, 0, 0))] * sides,
            scratch_shapes=[pltpu.VMEM((sides * blocks, blk, width), jnp.float32)],
        ),
        out_shape=[jax.ShapeDtypeStruct((blocks * blk, width), jnp.float32)]
        + [jax.ShapeDtypeStruct((blocks, blk, width), jnp.float32)]
        + [jax.ShapeDtypeStruct((blocks, blk, width), jnp.bfloat16)] * (sides - 1),
        compiler_params=pltpu.CompilerParams(dimension_semantics=("arbitrary",)),
    )(src_ids, tile_mask, grad_query, cot, zvalue, w_q, w_n2, w_n1)


def attend_kernel(scale, live_ref, q_ref, go_ref, kv_ref, wkv_ref, gq_ref, slots_ref, gk_acc, gv_acc):
    step = pl.program_id(0)
    width = q_ref.shape[1]

    @pl.when(step == 0)
    def _():
        gk_acc[...] = jnp.zeros(gk_acc.shape, jnp.float32)
        gv_acc[...] = jnp.zeros(gv_acc.shape, jnp.float32)

    queries = q_ref[...]
    grad_out = go_ref[...]
    keys = kv_ref[:, 0:width]
    values = kv_ref[:, width : 2 * width]
    nt = (((1,), (1,)), ((), ()))
    tn = (((0,), (0,)), ((), ()))
    scores = lax.dot_general(queries, keys, nt, preferred_element_type=jnp.float32) * scale
    scores = jnp.where(live_ref[...] > 0, scores, -jnp.inf)
    highest = jnp.max(scores, axis=1, keepdims=True)
    expo_terms = jnp.exp(scores - highest)
    probability = expo_terms / jnp.sum(expo_terms, axis=1, keepdims=True)
    prob_low = probability.astype(jnp.bfloat16)
    grad_prob = lax.dot_general(grad_out, values, nt, preferred_element_type=jnp.float32)
    spread = jnp.sum(probability * grad_prob, axis=1, keepdims=True)
    grad_score = (probability * (grad_prob - spread) * scale).astype(jnp.bfloat16)
    gq_ref[...] = jnp.dot(grad_score, keys, preferred_element_type=jnp.float32).astype(gq_ref.dtype)
    gk_acc[...] += lax.dot_general(grad_score, queries, tn, preferred_element_type=jnp.float32)
    gv_acc[...] += lax.dot_general(prob_low, grad_out, tn, preferred_element_type=jnp.float32)

    @pl.when(step == pl.num_programs(0) - 1)
    def _():
        grad_keys = gk_acc[...].astype(jnp.bfloat16)
        grad_vals = gv_acc[...].astype(jnp.bfloat16)
        slots = lax.dot_general(grad_keys, wkv_ref[:, 0:width], nt, preferred_element_type=jnp.float32)
        slots += lax.dot_general(grad_vals, wkv_ref[:, width : 2 * width], nt, preferred_element_type=jnp.float32)
        slots_ref[...] = slots.astype(slots_ref.dtype)


def attend_back(live, queries, grad_out, keyvals, w_kv, scale, rows_per_step=256):
    rows, width = queries.shape
    slots = keyvals.shape[0]
    steps = rows // rows_per_step
    row_block = pl.BlockSpec((rows_per_step, width), lambda i: (i, 0))
    return pl.pallas_call(
        functools.partial(attend_kernel, scale),
        grid=(steps,),
        in_specs=[
            pl.BlockSpec((1, slots), lambda i: (0, 0)),
            row_block,
            row_block,
            pl.BlockSpec((slots, 2 * width), lambda i: (0, 0)),
            pl.BlockSpec(w_kv.shape, lambda i: (0, 0)),
        ],
        out_specs=[row_block, pl.BlockSpec((slots, width), lambda i: (0, 0))],
        out_shape=(
            jax.ShapeDtypeStruct((rows, width), jnp.bfloat16),
            jax.ShapeDtypeStruct((slots, width), jnp.bfloat16),
        ),
        scratch_shapes=[
            pltpu.VMEM((slots, width), jnp.float32),
            pltpu.VMEM((slots, width), jnp.float32),
        ],
        compiler_params=pltpu.CompilerParams(dimension_semantics=("arbitrary",)),
        cost_estimate=pl.CostEstimate(
            flops=10 * rows * slots * width,
            transcendentals=rows * slots,
            bytes_accessed=2 * (3 * rows * width + 4 * slots * width),
        ),
    )(live, queries, grad_out, keyvals, w_kv)


def slope_of(values):
    sigma = 1.0 / (1.0 + jnp.exp(-values))
    return sigma * (1.0 + values * (1.0 - sigma))


def edge_back_kernel(lat_ref, own_ref, a_ref, b_ref, c_ref, d_ref, gn_ref, w1_ref, w2_ref, out_ref):
    nt = (((1,), (1,)), ((), ()))
    collected = own_ref[...]
    for ref in (a_ref, b_ref, c_ref, d_ref):
        collected = collected + ref[...].astype(jnp.float32)
    grad_msg = collected.astype(jnp.bfloat16)
    pre_act = jnp.dot(lat_ref[...], w1_ref[...], preferred_element_type=jnp.float32)
    grad_pre = lax.dot_general(grad_msg, w2_ref[...], nt, preferred_element_type=jnp.float32)
    grad_pre = (grad_pre * slope_of(pre_act)).astype(jnp.bfloat16)
    total = gn_ref[...] + lax.dot_general(grad_pre, w1_ref[...], nt, preferred_element_type=jnp.float32)
    out_ref[...] = total.astype(out_ref.dtype)


def edge_back(latent, own_part, received, grad_node, w_e1, w_e2, rows_per_step=512):
    rows, width = latent.shape
    row_block = pl.BlockSpec((rows_per_step, width), lambda i: (i, 0))
    weight = pl.BlockSpec(w_e1.shape, lambda i: (0, 0))
    return pl.pallas_call(
        edge_back_kernel,
        grid=(rows // rows_per_step,),
        in_specs=[row_block] * (3 + len(received)) + [weight, weight],
        out_specs=row_block,
        out_shape=jax.ShapeDtypeStruct((rows, width), jnp.bfloat16),
        cost_estimate=pl.CostEstimate(
            flops=6 * rows * width * width,
            transcendentals=rows * width,
            bytes_accessed=rows * width * (2 + 4 + 2 * len(received) + 4 + 2),
        ),
    )(latent, own_part, *received, grad_node, w_e1, w_e2)


def dense(left, right):
    return jnp.dot(left, right, preferred_element_type=jnp.float32)


def silu_slope(values):
    sigma = jax.nn.sigmoid(values)
    return sigma * (1.0 + values * (1.0 - sigma))


def on_device(
    nodes, tile_src, tile_mask, tokens, tok_count, w_e1, w_e2, w_n1, w_n2, w_q, w_kv, w_o, cotangent
):
    latent = nodes[0, 0]
    node_rows = latent.shape[0]
    latent_width = latent.shape[1]
    block_count = tile_src.shape[2]
    tile_count = tile_src.shape[3]
    blk_rows = tile_mask.shape[-1]
    rows_px = lax.axis_size("px")
    rows_py = lax.axis_size("py")
    devices = rows_px * rows_py
    score_scale = 1.0 / math.sqrt(latent_width)
    pre_act = dense(latent, w_e1)
    activation = jax.nn.silu(pre_act).astype(jnp.bfloat16)
    message = dense(activation, w_e2).astype(jnp.bfloat16)
    sources = [
        message,
        passed_along(message, "px", 1),
        passed_along(message, "px", -1),
        passed_along(message, "py", 1),
        passed_along(message, "py", -1),
    ]
    src_ids = tile_src[0, 0].reshape(-1)
    zvalue, queries = tile_gather(
        src_ids,
        tile_mask[0, 0],
        [part.reshape(block_count, blk_rows, latent_width) for part in sources],
        latent,
        w_n1,
        w_n2,
        w_q,
    )
    own_tokens = tokens[0]
    slot_count = own_tokens.shape[0] // devices
    token_groups = own_tokens.reshape(devices, slot_count, latent_width)
    arrived_tokens = lax.all_to_all(
        token_groups, ("px", "py"), split_axis=0, concat_axis=0, tiled=True
    )
    arrived_tokens = arrived_tokens.reshape(devices * slot_count, latent_width)
    arrived = dense(arrived_tokens, w_kv).astype(jnp.bfloat16)
    live_keys = (jnp.arange(slot_count)[None, :] < tok_count[:, 0][:, None]).reshape(1, -1)
    grad_out = dense(cotangent[0, 0], w_o.T).astype(jnp.bfloat16)
    grad_query, grad_slots = attend_back(
        live_keys.astype(jnp.float32), queries, grad_out, arrived, w_kv, score_scale
    )
    returned = lax.all_to_all(
        grad_slots.reshape(devices, slot_count, latent_width),
        ("px", "py"),
        split_axis=0,
        concat_axis=0,
        tiled=True,
    )
    grad_tokens = returned.reshape(devices * slot_count, latent_width)
    grad_node, own_part, *outbound = tile_scatter(
        src_ids, tile_mask[0, 0], grad_query, cotangent[0, 0], zvalue, w_q, w_n2, w_n1, len(sources)
    )
    outbound = [part.reshape(node_rows, latent_width) for part in outbound]
    received = [
        passed_along(outbound[0], "px", -1),
        passed_along(outbound[1], "px", 1),
        passed_along(outbound[2], "py", -1),
        passed_along(outbound[3], "py", 1),
    ]
    grad_nodes = edge_back(
        latent, own_part.reshape(node_rows, latent_width), received, grad_node, w_e1, w_e2
    )
    return (grad_nodes[None, None], grad_tokens[None])


def solution(mesh):
    return jax.shard_map(
        on_device,
        mesh=mesh,
        in_specs=(
            P("px", "py", None, None),
            P("px", "py", None, None),
            P("px", "py", None, None, None, None),
            P(("px", "py"), None, None),
            P(None, ("px", "py")),
            P(),
            P(),
            P(),
            P(),
            P(),
            P(),
            P(),
            P("px", "py", None, None),
        ),
        out_specs=(P("px", "py", None, None), P(("px", "py"), None, None)),
        check_vma=False,
    )
```

```python
import functools
import math

import jax
import jax.numpy as jnp
from jax import lax
from jax.experimental import pallas as pl
from jax.experimental.pallas import tpu as pltpu
from jax.sharding import PartitionSpec as P


def with_halo(block, sides, width):
    for axis, dim in sides:
        count = lax.axis_size(axis)
        forward = [(i, i + 1) for i in range(count - 1)]
        backward = [(target, source) for source, target in forward]
        low = lax.ppermute(
            lax.slice_in_dim(block, block.shape[dim] - width, None, axis=dim), axis, forward
        )
        high = lax.ppermute(lax.slice_in_dim(block, 0, width, axis=dim), axis, backward)
        block = jnp.concatenate([low, block, high], axis=dim)
    return block


def passed_along(value, axis, steps):
    count = lax.axis_size(axis)
    leading, last = (max(0, -steps), min(count, count - steps))
    return lax.ppermute(value, axis, [(source, source + steps) for source in range(leading, last)])


def gather_kernel(
    group, src_ids, mask_ref, own, up, down, left, right, lat_ref, wn1_ref, wn2_ref, wq_ref,
    z_ref, q_ref, rhs, gath
):
    step = pl.program_id(0)
    tiles = mask_ref.shape[1]
    blk = mask_ref.shape[2]
    per_side = own.shape[0]
    for g in range(group):
        for k in range(tiles):
            picked = src_ids[(step * group + g) * tiles + k]
            side = picked // per_side
            block = picked % per_side
            for index, ref in enumerate((own, up, down, left, right)):

                @pl.when(side == index)
                def _():
                    rhs[k * blk : (k + 1) * blk, :] = ref[block]

        bits = jnp.concatenate(
            [mask_ref[g, k].astype(jnp.float32).astype(jnp.bfloat16) for k in range(tiles)], axis=1
        )
        total = jnp.dot(bits, rhs[...], preferred_element_type=jnp.float32)
        gath[g * blk : (g + 1) * blk, :] = total.astype(gath.dtype)
    width = lat_ref.shape[1]
    latent = lat_ref[...]
    zvalue = jnp.dot(latent, wn1_ref[0:width, :], preferred_element_type=jnp.float32)
    zvalue += jnp.dot(gath[...], wn1_ref[width : 2 * width, :], preferred_element_type=jnp.float32)
    z_ref[...] = zvalue
    hidden = (zvalue / (1.0 + jnp.exp(-zvalue))).astype(jnp.bfloat16)
    updated = latent.astype(jnp.float32) + jnp.dot(hidden, wn2_ref[...], preferred_element_type=jnp.float32)
    queries = jnp.dot(updated.astype(jnp.bfloat16), wq_ref[...], preferred_element_type=jnp.float32)
    q_ref[...] = queries.astype(q_ref.dtype)


def tile_gather(src_ids, tile_mask, sources, latent, w_n1, w_n2, w_q, group=4):
    blocks, tiles, blk, _ = tile_mask.shape
    width = sources[0].shape[-1]
    whole = pl.BlockSpec((blocks, blk, width), lambda i, ids: (0, 0, 0))
    rows = pl.BlockSpec((group * blk, width), lambda i, ids: (i, 0))
    return pl.pallas_call(
        functools.partial(gather_kernel, group),
        grid_spec=pltpu.PrefetchScalarGridSpec(
            num_scalar_prefetch=1,
            grid=(blocks // group,),
            in_specs=[pl.BlockSpec((group, tiles, blk, blk), lambda i, ids: (i, 0, 0, 0))]
            + [whole] * len(sources)
            + [rows]
            + [pl.BlockSpec(w.shape, lambda i, ids: (0, 0)) for w in (w_n1, w_n2, w_q)],
            out_specs=[rows, rows],
            scratch_shapes=[
                pltpu.VMEM((tiles * blk, width), jnp.bfloat16),
                pltpu.VMEM((group * blk, width), jnp.bfloat16),
            ],
        ),
        out_shape=(
            jax.ShapeDtypeStruct((blocks * blk, width), jnp.float32),
            jax.ShapeDtypeStruct((blocks * blk, width), jnp.bfloat16),
        ),
        compiler_params=pltpu.CompilerParams(dimension_semantics=("arbitrary",)),
    )(src_ids, tile_mask, *sources, latent, w_n1, w_n2, w_q)


def scatter_kernel(group, src_ids, mask_ref, gq_ref, cot_ref, z_ref, wq_ref, wn2_ref, wn1_ref, gn_ref, own_ref, *rest):
    side_refs, total = rest[:-1], rest[-1]
    step = pl.program_id(0)
    tiles = mask_ref.shape[1]
    blk = mask_ref.shape[2]
    per_side = own_ref.shape[0]
    width = gq_ref.shape[1]
    tn = (((0,), (0,)), ((), ()))
    nt = (((1,), (1,)), ((), ()))
    grad_update = cot_ref[...].astype(jnp.float32) + lax.dot_general(
        gq_ref[...], wq_ref[...], nt, preferred_element_type=jnp.float32
    )
    update_low = grad_update.astype(jnp.bfloat16)
    grad_z = lax.dot_general(update_low, wn2_ref[...], nt, preferred_element_type=jnp.float32)
    grad_z = (grad_z * slope_of(z_ref[...])).astype(jnp.bfloat16)
    grad_agg = lax.dot_general(
        grad_z, wn1_ref[width : 2 * width, :], nt, preferred_element_type=jnp.float32
    ).astype(jnp.bfloat16)
    gn_ref[...] = grad_update + lax.dot_general(
        grad_z, wn1_ref[0:width, :], nt, preferred_element_type=jnp.float32
    )

    @pl.when(step == 0)
    def _():
        total[...] = jnp.zeros(total.shape, jnp.float32)

    for g in range(group):
        bits = jnp.concatenate(
            [mask_ref[g, k].astype(jnp.float32).astype(jnp.bfloat16) for k in range(tiles)], axis=1
        )
        grad_rows = grad_agg[g * blk : (g + 1) * blk, :]
        parts = lax.dot_general(bits, grad_rows, tn, preferred_element_type=jnp.float32)
        for k in range(tiles):
            picked = src_ids[(step * group + g) * tiles + k]
            total[picked] += parts[k * blk : (k + 1) * blk]

    @pl.when(step == pl.num_programs(0) - 1)
    def _():
        own_ref[...] = total[0:per_side]
        for side, out_ref in enumerate(side_refs):
            start = (side + 1) * per_side
            out_ref[...] = total[start : start + per_side].astype(out_ref.dtype)


def tile_scatter(src_ids, tile_mask, grad_query, cot, zvalue, w_q, w_n2, w_n1, sides, group=4):
    blocks, tiles, blk, _ = tile_mask.shape
    width = grad_query.shape[-1]
    rows = pl.BlockSpec((group * blk, width), lambda i, ids: (i, 0))
    return pl.pallas_call(
        functools.partial(scatter_kernel, group),
        grid_spec=pltpu.PrefetchScalarGridSpec(
            num_scalar_prefetch=1,
            grid=(blocks // group,),
            in_specs=[
                pl.BlockSpec((group, tiles, blk, blk), lambda i, ids: (i, 0, 0, 0)),
                rows,
                rows,
                rows,
                pl.BlockSpec(w_q.shape, lambda i, ids: (0, 0)),
                pl.BlockSpec(w_n2.shape, lambda i, ids: (0, 0)),
                pl.BlockSpec(w_n1.shape, lambda i, ids: (0, 0)),
            ],
            out_specs=[rows]
            + [pl.BlockSpec((blocks, blk, width), lambda i, ids: (0, 0, 0))] * sides,
            scratch_shapes=[pltpu.VMEM((sides * blocks, blk, width), jnp.float32)],
        ),
        out_shape=[jax.ShapeDtypeStruct((blocks * blk, width), jnp.float32)]
        + [jax.ShapeDtypeStruct((blocks, blk, width), jnp.float32)]
        + [jax.ShapeDtypeStruct((blocks, blk, width), jnp.bfloat16)] * (sides - 1),
        compiler_params=pltpu.CompilerParams(dimension_semantics=("arbitrary",)),
    )(src_ids, tile_mask, grad_query, cot, zvalue, w_q, w_n2, w_n1)


def attend_kernel(scale, live_ref, q_ref, go_ref, kv_ref, wkv_ref, gq_ref, slots_ref, gk_acc, gv_acc):
    step = pl.program_id(0)
    width = q_ref.shape[1]

    @pl.when(step == 0)
    def _():
        gk_acc[...] = jnp.zeros(gk_acc.shape, jnp.float32)
        gv_acc[...] = jnp.zeros(gv_acc.shape, jnp.float32)

    queries = q_ref[...]
    grad_out = go_ref[...]
    keys = kv_ref[:, 0:width]
    values = kv_ref[:, width : 2 * width]
    nt = (((1,), (1,)), ((), ()))
    tn = (((0,), (0,)), ((), ()))
    scores = lax.dot_general(queries, keys, nt, preferred_element_type=jnp.float32) * scale
    scores = jnp.where(live_ref[...] > 0, scores, -jnp.inf)
    highest = jnp.max(scores, axis=1, keepdims=True)
    expo_terms = jnp.exp(scores - highest)
    probability = expo_terms / jnp.sum(expo_terms, axis=1, keepdims=True)
    prob_low = probability.astype(jnp.bfloat16)
    grad_prob = lax.dot_general(grad_out, values, nt, preferred_element_type=jnp.float32)
    spread = jnp.sum(probability * grad_prob, axis=1, keepdims=True)
    grad_score = (probability * (grad_prob - spread) * scale).astype(jnp.bfloat16)
    gq_ref[...] = jnp.dot(grad_score, keys, preferred_element_type=jnp.float32).astype(gq_ref.dtype)
    gk_acc[...] += lax.dot_general(grad_score, queries, tn, preferred_element_type=jnp.float32)
    gv_acc[...] += lax.dot_general(prob_low, grad_out, tn, preferred_element_type=jnp.float32)

    @pl.when(step == pl.num_programs(0) - 1)
    def _():
        grad_keys = gk_acc[...].astype(jnp.bfloat16)
        grad_vals = gv_acc[...].astype(jnp.bfloat16)
        slots = lax.dot_general(grad_keys, wkv_ref[:, 0:width], nt, preferred_element_type=jnp.float32)
        slots += lax.dot_general(grad_vals, wkv_ref[:, width : 2 * width], nt, preferred_element_type=jnp.float32)
        slots_ref[...] = slots.astype(slots_ref.dtype)


def attend_back(live, queries, grad_out, keyvals, w_kv, scale, rows_per_step=256):
    rows, width = queries.shape
    slots = keyvals.shape[0]
    steps = rows // rows_per_step
    row_block = pl.BlockSpec((rows_per_step, width), lambda i: (i, 0))
    return pl.pallas_call(
        functools.partial(attend_kernel, scale),
        grid=(steps,),
        in_specs=[
            pl.BlockSpec((1, slots), lambda i: (0, 0)),
            row_block,
            row_block,
            pl.BlockSpec((slots, 2 * width), lambda i: (0, 0)),
            pl.BlockSpec(w_kv.shape, lambda i: (0, 0)),
        ],
        out_specs=[row_block, pl.BlockSpec((slots, width), lambda i: (0, 0))],
        out_shape=(
            jax.ShapeDtypeStruct((rows, width), jnp.bfloat16),
            jax.ShapeDtypeStruct((slots, width), jnp.bfloat16),
        ),
        scratch_shapes=[
            pltpu.VMEM((slots, width), jnp.float32),
            pltpu.VMEM((slots, width), jnp.float32),
        ],
        compiler_params=pltpu.CompilerParams(dimension_semantics=("arbitrary",)),
        cost_estimate=pl.CostEstimate(
            flops=10 * rows * slots * width,
            transcendentals=rows * slots,
            bytes_accessed=2 * (3 * rows * width + 4 * slots * width),
        ),
    )(live, queries, grad_out, keyvals, w_kv)


def slope_of(values):
    sigma = 1.0 / (1.0 + jnp.exp(-values))
    return sigma * (1.0 + values * (1.0 - sigma))


def edge_back_kernel(lat_ref, own_ref, a_ref, b_ref, c_ref, d_ref, gn_ref, w1_ref, w2_ref, out_ref):
    nt = (((1,), (1,)), ((), ()))
    collected = own_ref[...]
    for ref in (a_ref, b_ref, c_ref, d_ref):
        collected = collected + ref[...].astype(jnp.float32)
    grad_msg = collected.astype(jnp.bfloat16)
    pre_act = jnp.dot(lat_ref[...], w1_ref[...], preferred_element_type=jnp.float32)
    grad_pre = lax.dot_general(grad_msg, w2_ref[...], nt, preferred_element_type=jnp.float32)
    grad_pre = (grad_pre * slope_of(pre_act)).astype(jnp.bfloat16)
    total = gn_ref[...] + lax.dot_general(grad_pre, w1_ref[...], nt, preferred_element_type=jnp.float32)
    out_ref[...] = total.astype(out_ref.dtype)


def edge_back(latent, own_part, received, grad_node, w_e1, w_e2, rows_per_step=512):
    rows, width = latent.shape
    row_block = pl.BlockSpec((rows_per_step, width), lambda i: (i, 0))
    weight = pl.BlockSpec(w_e1.shape, lambda i: (0, 0))
    return pl.pallas_call(
        edge_back_kernel,
        grid=(rows // rows_per_step,),
        in_specs=[row_block] * (3 + len(received)) + [weight, weight],
        out_specs=row_block,
        out_shape=jax.ShapeDtypeStruct((rows, width), jnp.bfloat16),
        cost_estimate=pl.CostEstimate(
            flops=6 * rows * width * width,
            transcendentals=rows * width,
            bytes_accessed=rows * width * (2 + 4 + 2 * len(received) + 4 + 2),
        ),
    )(latent, own_part, *received, grad_node, w_e1, w_e2)


def dense(left, right):
    return jnp.dot(left, right, preferred_element_type=jnp.float32)


def silu_slope(values):
    sigma = jax.nn.sigmoid(values)
    return sigma * (1.0 + values * (1.0 - sigma))


def on_device(
    nodes, tile_src, tile_mask, tokens, tok_count, w_e1, w_e2, w_n1, w_n2, w_q, w_kv, w_o, cotangent
):
    latent = nodes[0, 0]
    node_rows = latent.shape[0]
    latent_width = latent.shape[1]
    block_count = tile_src.shape[2]
    tile_count = tile_src.shape[3]
    blk_rows = tile_mask.shape[-1]
    rows_px = lax.axis_size("px")
    rows_py = lax.axis_size("py")
    devices = rows_px * rows_py
    score_scale = 1.0 / math.sqrt(latent_width)
    pre_act = dense(latent, w_e1)
    activation = jax.nn.silu(pre_act).astype(jnp.bfloat16)
    message = dense(activation, w_e2).astype(jnp.bfloat16)
    sources = [
        message,
        passed_along(message, "px", 1),
        passed_along(message, "px", -1),
        passed_along(message, "py", 1),
        passed_along(message, "py", -1),
    ]
    held_tokens, sources[1] = lax.optimization_barrier((tokens, sources[1]))
    src_ids = tile_src[0, 0].reshape(-1)
    zvalue, queries = tile_gather(
        src_ids,
        tile_mask[0, 0],
        [part.reshape(block_count, blk_rows, latent_width) for part in sources],
        latent,
        w_n1,
        w_n2,
        w_q,
    )
    own_tokens = held_tokens[0]
    slot_count = own_tokens.shape[0] // devices
    token_groups = own_tokens.reshape(devices, slot_count, latent_width)
    arrived_tokens = lax.all_to_all(
        token_groups, ("px", "py"), split_axis=0, concat_axis=0, tiled=True
    )
    arrived_tokens = arrived_tokens.reshape(devices * slot_count, latent_width)
    arrived = dense(arrived_tokens, w_kv).astype(jnp.bfloat16)
    live_keys = (jnp.arange(slot_count)[None, :] < tok_count[:, 0][:, None]).reshape(1, -1)
    grad_out = dense(cotangent[0, 0], w_o.T).astype(jnp.bfloat16)
    grad_query, grad_slots = attend_back(
        live_keys.astype(jnp.float32), queries, grad_out, arrived, w_kv, score_scale
    )
    returned = lax.all_to_all(
        grad_slots.reshape(devices, slot_count, latent_width),
        ("px", "py"),
        split_axis=0,
        concat_axis=0,
        tiled=True,
    )
    grad_tokens = returned.reshape(devices * slot_count, latent_width)
    grad_node, own_part, *outbound = tile_scatter(
        src_ids, tile_mask[0, 0], grad_query, cotangent[0, 0], zvalue, w_q, w_n2, w_n1, len(sources)
    )
    outbound = [part.reshape(node_rows, latent_width) for part in outbound]
    received = [
        passed_along(outbound[0], "px", -1),
        passed_along(outbound[1], "px", 1),
        passed_along(outbound[2], "py", -1),
        passed_along(outbound[3], "py", 1),
    ]
    grad_nodes = edge_back(
        latent, own_part.reshape(node_rows, latent_width), received, grad_node, w_e1, w_e2
    )
    return (grad_nodes[None, None], grad_tokens[None])


def solution(mesh):
    return jax.shard_map(
        on_device,
        mesh=mesh,
        in_specs=(
            P("px", "py", None, None),
            P("px", "py", None, None),
            P("px", "py", None, None, None, None),
            P(("px", "py"), None, None),
            P(None, ("px", "py")),
            P(),
            P(),
            P(),
            P(),
            P(),
            P(),
            P(),
            P("px", "py", None, None),
        ),
        out_specs=(P("px", "py", None, None), P(("px", "py"), None, None)),
        check_vma=False,
    )
```

```python
import functools
import math

import jax
import jax.numpy as jnp
from jax import lax
from jax.experimental import pallas as pl
from jax.experimental.pallas import tpu as pltpu
from jax.sharding import PartitionSpec as P


def with_halo(block, sides, width):
    for axis, dim in sides:
        count = lax.axis_size(axis)
        forward = [(i, i + 1) for i in range(count - 1)]
        backward = [(target, source) for source, target in forward]
        low = lax.ppermute(
            lax.slice_in_dim(block, block.shape[dim] - width, None, axis=dim), axis, forward
        )
        high = lax.ppermute(lax.slice_in_dim(block, 0, width, axis=dim), axis, backward)
        block = jnp.concatenate([low, block, high], axis=dim)
    return block


def passed_along(value, axis, steps):
    count = lax.axis_size(axis)
    leading, last = (max(0, -steps), min(count, count - steps))
    return lax.ppermute(value, axis, [(source, source + steps) for source in range(leading, last)])


def gather_kernel(
    group, src_ids, mask_ref, own, up, down, left, right, lat_ref, wn1_ref, wn2_ref, wq_ref,
    z_ref, q_ref, rhs, gath
):
    step = pl.program_id(0)
    tiles = mask_ref.shape[1]
    blk = mask_ref.shape[2]
    per_side = own.shape[0]
    for g in range(group):
        for k in range(tiles):
            picked = src_ids[(step * group + g) * tiles + k]
            side = picked // per_side
            block = picked % per_side
            for index, ref in enumerate((own, up, down, left, right)):

                @pl.when(side == index)
                def _():
                    rhs[k * blk : (k + 1) * blk, :] = ref[block]

        bits = jnp.concatenate(
            [mask_ref[g, k].astype(jnp.float32).astype(jnp.bfloat16) for k in range(tiles)], axis=1
        )
        total = jnp.dot(bits, rhs[...], preferred_element_type=jnp.float32)
        gath[g * blk : (g + 1) * blk, :] = total.astype(gath.dtype)
    width = lat_ref.shape[1]
    latent = lat_ref[...]
    zvalue = jnp.dot(latent, wn1_ref[0:width, :], preferred_element_type=jnp.float32)
    zvalue += jnp.dot(gath[...], wn1_ref[width : 2 * width, :], preferred_element_type=jnp.float32)
    z_ref[...] = zvalue
    hidden = (zvalue / (1.0 + jnp.exp(-zvalue))).astype(jnp.bfloat16)
    updated = latent.astype(jnp.float32) + jnp.dot(hidden, wn2_ref[...], preferred_element_type=jnp.float32)
    queries = jnp.dot(updated.astype(jnp.bfloat16), wq_ref[...], preferred_element_type=jnp.float32)
    q_ref[...] = queries.astype(q_ref.dtype)


def tile_gather(src_ids, tile_mask, sources, latent, w_n1, w_n2, w_q, group=4):
    blocks, tiles, blk, _ = tile_mask.shape
    width = sources[0].shape[-1]
    whole = pl.BlockSpec((blocks, blk, width), lambda i, ids: (0, 0, 0))
    rows = pl.BlockSpec((group * blk, width), lambda i, ids: (i, 0))
    return pl.pallas_call(
        functools.partial(gather_kernel, group),
        grid_spec=pltpu.PrefetchScalarGridSpec(
            num_scalar_prefetch=1,
            grid=(blocks // group,),
            in_specs=[pl.BlockSpec((group, tiles, blk, blk), lambda i, ids: (i, 0, 0, 0))]
            + [whole] * len(sources)
            + [rows]
            + [pl.BlockSpec(w.shape, lambda i, ids: (0, 0)) for w in (w_n1, w_n2, w_q)],
            out_specs=[rows, rows],
            scratch_shapes=[
                pltpu.VMEM((tiles * blk, width), jnp.bfloat16),
                pltpu.VMEM((group * blk, width), jnp.bfloat16),
            ],
        ),
        out_shape=(
            jax.ShapeDtypeStruct((blocks * blk, width), jnp.float32),
            jax.ShapeDtypeStruct((blocks * blk, width), jnp.bfloat16),
        ),
        compiler_params=pltpu.CompilerParams(dimension_semantics=("arbitrary",)),
    )(src_ids, tile_mask, *sources, latent, w_n1, w_n2, w_q)


def scatter_kernel(group, src_ids, mask_ref, gq_ref, cot_ref, z_ref, wq_ref, wn2_ref, wn1_ref, gn_ref, own_ref, *rest):
    side_refs, total = rest[:-1], rest[-1]
    step = pl.program_id(0)
    tiles = mask_ref.shape[1]
    blk = mask_ref.shape[2]
    per_side = own_ref.shape[0]
    width = gq_ref.shape[1]
    tn = (((0,), (0,)), ((), ()))
    nt = (((1,), (1,)), ((), ()))
    grad_update = cot_ref[...].astype(jnp.float32) + lax.dot_general(
        gq_ref[...], wq_ref[...], nt, preferred_element_type=jnp.float32
    )
    update_low = grad_update.astype(jnp.bfloat16)
    grad_z = lax.dot_general(update_low, wn2_ref[...], nt, preferred_element_type=jnp.float32)
    grad_z = (grad_z * slope_of(z_ref[...])).astype(jnp.bfloat16)
    grad_agg = lax.dot_general(
        grad_z, wn1_ref[width : 2 * width, :], nt, preferred_element_type=jnp.float32
    ).astype(jnp.bfloat16)
    gn_ref[...] = grad_update + lax.dot_general(
        grad_z, wn1_ref[0:width, :], nt, preferred_element_type=jnp.float32
    )

    @pl.when(step == 0)
    def _():
        total[...] = jnp.zeros(total.shape, jnp.float32)

    for g in range(group):
        bits = jnp.concatenate(
            [mask_ref[g, k].astype(jnp.float32).astype(jnp.bfloat16) for k in range(tiles)], axis=1
        )
        grad_rows = grad_agg[g * blk : (g + 1) * blk, :]
        parts = lax.dot_general(bits, grad_rows, tn, preferred_element_type=jnp.float32)
        for k in range(tiles):
            picked = src_ids[(step * group + g) * tiles + k]
            total[picked] += parts[k * blk : (k + 1) * blk]

    @pl.when(step == pl.num_programs(0) - 1)
    def _():
        own_ref[...] = total[0:per_side]
        for side, out_ref in enumerate(side_refs):
            start = (side + 1) * per_side
            out_ref[...] = total[start : start + per_side].astype(out_ref.dtype)


def tile_scatter(src_ids, tile_mask, grad_query, cot, zvalue, w_q, w_n2, w_n1, sides, group=4):
    blocks, tiles, blk, _ = tile_mask.shape
    width = grad_query.shape[-1]
    rows = pl.BlockSpec((group * blk, width), lambda i, ids: (i, 0))
    return pl.pallas_call(
        functools.partial(scatter_kernel, group),
        grid_spec=pltpu.PrefetchScalarGridSpec(
            num_scalar_prefetch=1,
            grid=(blocks // group,),
            in_specs=[
                pl.BlockSpec((group, tiles, blk, blk), lambda i, ids: (i, 0, 0, 0)),
                rows,
                rows,
                rows,
                pl.BlockSpec(w_q.shape, lambda i, ids: (0, 0)),
                pl.BlockSpec(w_n2.shape, lambda i, ids: (0, 0)),
                pl.BlockSpec(w_n1.shape, lambda i, ids: (0, 0)),
            ],
            out_specs=[rows]
            + [pl.BlockSpec((blocks, blk, width), lambda i, ids: (0, 0, 0))] * sides,
            scratch_shapes=[pltpu.VMEM((sides * blocks, blk, width), jnp.float32)],
        ),
        out_shape=[jax.ShapeDtypeStruct((blocks * blk, width), jnp.float32)]
        + [jax.ShapeDtypeStruct((blocks, blk, width), jnp.float32)]
        + [jax.ShapeDtypeStruct((blocks, blk, width), jnp.bfloat16)] * (sides - 1),
        compiler_params=pltpu.CompilerParams(dimension_semantics=("arbitrary",)),
    )(src_ids, tile_mask, grad_query, cot, zvalue, w_q, w_n2, w_n1)


def attend_kernel(scale, live_ref, q_ref, go_ref, kv_ref, wkv_ref, gq_ref, slots_ref, gk_acc, gv_acc):
    step = pl.program_id(0)
    width = q_ref.shape[1]

    @pl.when(step == 0)
    def _():
        gk_acc[...] = jnp.zeros(gk_acc.shape, jnp.float32)
        gv_acc[...] = jnp.zeros(gv_acc.shape, jnp.float32)

    queries = q_ref[...]
    grad_out = go_ref[...]
    keys = kv_ref[:, 0:width]
    values = kv_ref[:, width : 2 * width]
    nt = (((1,), (1,)), ((), ()))
    tn = (((0,), (0,)), ((), ()))
    scores = lax.dot_general(queries, keys, nt, preferred_element_type=jnp.float32) * scale
    scores = jnp.where(live_ref[...] > 0, scores, -jnp.inf)
    highest = jnp.max(scores, axis=1, keepdims=True)
    expo_terms = jnp.exp(scores - highest)
    probability = expo_terms / jnp.sum(expo_terms, axis=1, keepdims=True)
    prob_low = probability.astype(jnp.bfloat16)
    grad_prob = lax.dot_general(grad_out, values, nt, preferred_element_type=jnp.float32)
    spread = jnp.sum(probability * grad_prob, axis=1, keepdims=True)
    grad_score = (probability * (grad_prob - spread) * scale).astype(jnp.bfloat16)
    gq_ref[...] = jnp.dot(grad_score, keys, preferred_element_type=jnp.float32).astype(gq_ref.dtype)
    gk_acc[...] += lax.dot_general(grad_score, queries, tn, preferred_element_type=jnp.float32)
    gv_acc[...] += lax.dot_general(prob_low, grad_out, tn, preferred_element_type=jnp.float32)

    @pl.when(step == pl.num_programs(0) - 1)
    def _():
        grad_keys = gk_acc[...].astype(jnp.bfloat16)
        grad_vals = gv_acc[...].astype(jnp.bfloat16)
        slots = lax.dot_general(grad_keys, wkv_ref[:, 0:width], nt, preferred_element_type=jnp.float32)
        slots += lax.dot_general(grad_vals, wkv_ref[:, width : 2 * width], nt, preferred_element_type=jnp.float32)
        slots_ref[...] = slots.astype(slots_ref.dtype)


def attend_back(live, queries, grad_out, keyvals, w_kv, scale, rows_per_step=512):
    rows, width = queries.shape
    slots = keyvals.shape[0]
    steps = rows // rows_per_step
    row_block = pl.BlockSpec((rows_per_step, width), lambda i: (i, 0))
    return pl.pallas_call(
        functools.partial(attend_kernel, scale),
        grid=(steps,),
        in_specs=[
            pl.BlockSpec((1, slots), lambda i: (0, 0)),
            row_block,
            row_block,
            pl.BlockSpec((slots, 2 * width), lambda i: (0, 0)),
            pl.BlockSpec(w_kv.shape, lambda i: (0, 0)),
        ],
        out_specs=[row_block, pl.BlockSpec((slots, width), lambda i: (0, 0))],
        out_shape=(
            jax.ShapeDtypeStruct((rows, width), jnp.bfloat16),
            jax.ShapeDtypeStruct((slots, width), jnp.bfloat16),
        ),
        scratch_shapes=[
            pltpu.VMEM((slots, width), jnp.float32),
            pltpu.VMEM((slots, width), jnp.float32),
        ],
        compiler_params=pltpu.CompilerParams(dimension_semantics=("arbitrary",)),
        cost_estimate=pl.CostEstimate(
            flops=10 * rows * slots * width,
            transcendentals=rows * slots,
            bytes_accessed=2 * (3 * rows * width + 4 * slots * width),
        ),
    )(live, queries, grad_out, keyvals, w_kv)


def slope_of(values):
    sigma = 1.0 / (1.0 + jnp.exp(-values))
    return sigma * (1.0 + values * (1.0 - sigma))


def edge_back_kernel(lat_ref, own_ref, a_ref, b_ref, c_ref, d_ref, gn_ref, w1_ref, w2_ref, out_ref):
    nt = (((1,), (1,)), ((), ()))
    collected = own_ref[...]
    for ref in (a_ref, b_ref, c_ref, d_ref):
        collected = collected + ref[...].astype(jnp.float32)
    grad_msg = collected.astype(jnp.bfloat16)
    pre_act = jnp.dot(lat_ref[...], w1_ref[...], preferred_element_type=jnp.float32)
    grad_pre = lax.dot_general(grad_msg, w2_ref[...], nt, preferred_element_type=jnp.float32)
    grad_pre = (grad_pre * slope_of(pre_act)).astype(jnp.bfloat16)
    total = gn_ref[...] + lax.dot_general(grad_pre, w1_ref[...], nt, preferred_element_type=jnp.float32)
    out_ref[...] = total.astype(out_ref.dtype)


def edge_back(latent, own_part, received, grad_node, w_e1, w_e2, rows_per_step=512):
    rows, width = latent.shape
    row_block = pl.BlockSpec((rows_per_step, width), lambda i: (i, 0))
    weight = pl.BlockSpec(w_e1.shape, lambda i: (0, 0))
    return pl.pallas_call(
        edge_back_kernel,
        grid=(rows // rows_per_step,),
        in_specs=[row_block] * (3 + len(received)) + [weight, weight],
        out_specs=row_block,
        out_shape=jax.ShapeDtypeStruct((rows, width), jnp.bfloat16),
        cost_estimate=pl.CostEstimate(
            flops=6 * rows * width * width,
            transcendentals=rows * width,
            bytes_accessed=rows * width * (2 + 4 + 2 * len(received) + 4 + 2),
        ),
    )(latent, own_part, *received, grad_node, w_e1, w_e2)


def dense(left, right):
    return jnp.dot(left, right, preferred_element_type=jnp.float32)


def silu_slope(values):
    sigma = jax.nn.sigmoid(values)
    return sigma * (1.0 + values * (1.0 - sigma))


def on_device(
    nodes, tile_src, tile_mask, tokens, tok_count, w_e1, w_e2, w_n1, w_n2, w_q, w_kv, w_o, cotangent
):
    latent = nodes[0, 0]
    node_rows = latent.shape[0]
    latent_width = latent.shape[1]
    block_count = tile_src.shape[2]
    tile_count = tile_src.shape[3]
    blk_rows = tile_mask.shape[-1]
    rows_px = lax.axis_size("px")
    rows_py = lax.axis_size("py")
    devices = rows_px * rows_py
    score_scale = 1.0 / math.sqrt(latent_width)
    pre_act = dense(latent, w_e1)
    activation = jax.nn.silu(pre_act).astype(jnp.bfloat16)
    message = dense(activation, w_e2).astype(jnp.bfloat16)
    sources = [
        message,
        passed_along(message, "px", 1),
        passed_along(message, "px", -1),
        passed_along(message, "py", 1),
        passed_along(message, "py", -1),
    ]
    src_ids = tile_src[0, 0].reshape(-1)
    zvalue, queries = tile_gather(
        src_ids,
        tile_mask[0, 0],
        [part.reshape(block_count, blk_rows, latent_width) for part in sources],
        latent,
        w_n1,
        w_n2,
        w_q,
    )
    own_tokens = tokens[0]
    slot_count = own_tokens.shape[0] // devices
    token_groups = own_tokens.reshape(devices, slot_count, latent_width)
    arrived_tokens = lax.all_to_all(
        token_groups, ("px", "py"), split_axis=0, concat_axis=0, tiled=True
    )
    arrived_tokens = arrived_tokens.reshape(devices * slot_count, latent_width)
    arrived = dense(arrived_tokens, w_kv).astype(jnp.bfloat16)
    live_keys = (jnp.arange(slot_count)[None, :] < tok_count[:, 0][:, None]).reshape(1, -1)
    grad_out = dense(cotangent[0, 0], w_o.T).astype(jnp.bfloat16)
    grad_query, grad_slots = attend_back(
        live_keys.astype(jnp.float32), queries, grad_out, arrived, w_kv, score_scale
    )
    returned = lax.all_to_all(
        grad_slots.reshape(devices, slot_count, latent_width),
        ("px", "py"),
        split_axis=0,
        concat_axis=0,
        tiled=True,
    )
    grad_tokens = returned.reshape(devices * slot_count, latent_width)
    grad_node, own_part, *outbound = tile_scatter(
        src_ids, tile_mask[0, 0], grad_query, cotangent[0, 0], zvalue, w_q, w_n2, w_n1, len(sources)
    )
    outbound = [part.reshape(node_rows, latent_width) for part in outbound]
    received = [
        passed_along(outbound[0], "px", -1),
        passed_along(outbound[1], "px", 1),
        passed_along(outbound[2], "py", -1),
        passed_along(outbound[3], "py", 1),
    ]
    grad_nodes = edge_back(
        latent, own_part.reshape(node_rows, latent_width), received, grad_node, w_e1, w_e2
    )
    return (grad_nodes[None, None], grad_tokens[None])


def solution(mesh):
    return jax.shard_map(
        on_device,
        mesh=mesh,
        in_specs=(
            P("px", "py", None, None),
            P("px", "py", None, None),
            P("px", "py", None, None, None, None),
            P(("px", "py"), None, None),
            P(None, ("px", "py")),
            P(),
            P(),
            P(),
            P(),
            P(),
            P(),
            P(),
            P("px", "py", None, None),
        ),
        out_specs=(P("px", "py", None, None), P(("px", "py"), None, None)),
        check_vma=False,
    )
```

```python
import functools
import math

import jax
import jax.numpy as jnp
from jax import lax
from jax.experimental import pallas as pl
from jax.experimental.pallas import tpu as pltpu
from jax.sharding import PartitionSpec as P


def with_halo(block, sides, width):
    for axis, dim in sides:
        count = lax.axis_size(axis)
        forward = [(i, i + 1) for i in range(count - 1)]
        backward = [(target, source) for source, target in forward]
        low = lax.ppermute(
            lax.slice_in_dim(block, block.shape[dim] - width, None, axis=dim), axis, forward
        )
        high = lax.ppermute(lax.slice_in_dim(block, 0, width, axis=dim), axis, backward)
        block = jnp.concatenate([low, block, high], axis=dim)
    return block


def passed_along(value, axis, steps):
    count = lax.axis_size(axis)
    leading, last = (max(0, -steps), min(count, count - steps))
    return lax.ppermute(value, axis, [(source, source + steps) for source in range(leading, last)])


def gather_kernel(
    group, src_ids, mask_ref, own, up, down, left, right, lat_ref, wn1_ref, wn2_ref, wq_ref,
    z_ref, q_ref, rhs, gath
):
    step = pl.program_id(0)
    tiles = mask_ref.shape[1]
    blk = mask_ref.shape[2]
    per_side = own.shape[0]
    for g in range(group):
        for k in range(tiles):
            picked = src_ids[(step * group + g) * tiles + k]
            side = picked // per_side
            block = picked % per_side
            for index, ref in enumerate((own, up, down, left, right)):

                @pl.when(side == index)
                def _():
                    rhs[k * blk : (k + 1) * blk, :] = ref[block]

        bits = jnp.concatenate(
            [mask_ref[g, k].astype(jnp.float32).astype(jnp.bfloat16) for k in range(tiles)], axis=1
        )
        total = jnp.dot(bits, rhs[...], preferred_element_type=jnp.float32)
        gath[g * blk : (g + 1) * blk, :] = total.astype(gath.dtype)
    width = lat_ref.shape[1]
    latent = lat_ref[...]
    zvalue = jnp.dot(latent, wn1_ref[0:width, :], preferred_element_type=jnp.float32)
    zvalue += jnp.dot(gath[...], wn1_ref[width : 2 * width, :], preferred_element_type=jnp.float32)
    z_ref[...] = zvalue
    hidden = (zvalue / (1.0 + jnp.exp(-zvalue))).astype(jnp.bfloat16)
    updated = latent.astype(jnp.float32) + jnp.dot(hidden, wn2_ref[...], preferred_element_type=jnp.float32)
    queries = jnp.dot(updated.astype(jnp.bfloat16), wq_ref[...], preferred_element_type=jnp.float32)
    q_ref[...] = queries.astype(q_ref.dtype)


def tile_gather(src_ids, tile_mask, sources, latent, w_n1, w_n2, w_q, group=4):
    blocks, tiles, blk, _ = tile_mask.shape
    width = sources[0].shape[-1]
    whole = pl.BlockSpec((blocks, blk, width), lambda i, ids: (0, 0, 0))
    rows = pl.BlockSpec((group * blk, width), lambda i, ids: (i, 0))
    return pl.pallas_call(
        functools.partial(gather_kernel, group),
        grid_spec=pltpu.PrefetchScalarGridSpec(
            num_scalar_prefetch=1,
            grid=(blocks // group,),
            in_specs=[pl.BlockSpec((group, tiles, blk, blk), lambda i, ids: (i, 0, 0, 0))]
            + [whole] * len(sources)
            + [rows]
            + [pl.BlockSpec(w.shape, lambda i, ids: (0, 0)) for w in (w_n1, w_n2, w_q)],
            out_specs=[rows, rows],
            scratch_shapes=[
                pltpu.VMEM((tiles * blk, width), jnp.bfloat16),
                pltpu.VMEM((group * blk, width), jnp.bfloat16),
            ],
        ),
        out_shape=(
            jax.ShapeDtypeStruct((blocks * blk, width), jnp.float32),
            jax.ShapeDtypeStruct((blocks * blk, width), jnp.bfloat16),
        ),
        compiler_params=pltpu.CompilerParams(dimension_semantics=("arbitrary",)),
    )(src_ids, tile_mask, *sources, latent, w_n1, w_n2, w_q)


def scatter_kernel(group, src_ids, mask_ref, gq_ref, cot_ref, z_ref, wq_ref, wn2_ref, wn1_ref, gn_ref, own_ref, *rest):
    side_refs, total = rest[:-1], rest[-1]
    step = pl.program_id(0)
    tiles = mask_ref.shape[1]
    blk = mask_ref.shape[2]
    per_side = own_ref.shape[0]
    width = gq_ref.shape[1]
    tn = (((0,), (0,)), ((), ()))
    nt = (((1,), (1,)), ((), ()))
    grad_update = cot_ref[...].astype(jnp.float32) + lax.dot_general(
        gq_ref[...], wq_ref[...], nt, preferred_element_type=jnp.float32
    )
    update_low = grad_update.astype(jnp.bfloat16)
    grad_z = lax.dot_general(update_low, wn2_ref[...], nt, preferred_element_type=jnp.float32)
    grad_z = (grad_z * slope_of(z_ref[...])).astype(jnp.bfloat16)
    grad_agg = lax.dot_general(
        grad_z, wn1_ref[width : 2 * width, :], nt, preferred_element_type=jnp.float32
    ).astype(jnp.bfloat16)
    gn_ref[...] = grad_update + lax.dot_general(
        grad_z, wn1_ref[0:width, :], nt, preferred_element_type=jnp.float32
    )

    @pl.when(step == 0)
    def _():
        total[...] = jnp.zeros(total.shape, jnp.float32)

    for g in range(group):
        bits = jnp.concatenate(
            [mask_ref[g, k].astype(jnp.float32).astype(jnp.bfloat16) for k in range(tiles)], axis=1
        )
        grad_rows = grad_agg[g * blk : (g + 1) * blk, :]
        parts = lax.dot_general(bits, grad_rows, tn, preferred_element_type=jnp.float32)
        for k in range(tiles):
            picked = src_ids[(step * group + g) * tiles + k]
            total[picked] += parts[k * blk : (k + 1) * blk]

    @pl.when(step == pl.num_programs(0) - 1)
    def _():
        own_ref[...] = total[0:per_side]
        for side, out_ref in enumerate(side_refs):
            start = (side + 1) * per_side
            out_ref[...] = total[start : start + per_side].astype(out_ref.dtype)


def tile_scatter(src_ids, tile_mask, grad_query, cot, zvalue, w_q, w_n2, w_n1, sides, group=4):
    blocks, tiles, blk, _ = tile_mask.shape
    width = grad_query.shape[-1]
    rows = pl.BlockSpec((group * blk, width), lambda i, ids: (i, 0))
    return pl.pallas_call(
        functools.partial(scatter_kernel, group),
        grid_spec=pltpu.PrefetchScalarGridSpec(
            num_scalar_prefetch=1,
            grid=(blocks // group,),
            in_specs=[
                pl.BlockSpec((group, tiles, blk, blk), lambda i, ids: (i, 0, 0, 0)),
                rows,
                rows,
                rows,
                pl.BlockSpec(w_q.shape, lambda i, ids: (0, 0)),
                pl.BlockSpec(w_n2.shape, lambda i, ids: (0, 0)),
                pl.BlockSpec(w_n1.shape, lambda i, ids: (0, 0)),
            ],
            out_specs=[rows]
            + [pl.BlockSpec((blocks, blk, width), lambda i, ids: (0, 0, 0))] * sides,
            scratch_shapes=[pltpu.VMEM((sides * blocks, blk, width), jnp.float32)],
        ),
        out_shape=[jax.ShapeDtypeStruct((blocks * blk, width), jnp.float32)]
        + [jax.ShapeDtypeStruct((blocks, blk, width), jnp.float32)]
        + [jax.ShapeDtypeStruct((blocks, blk, width), jnp.bfloat16)] * (sides - 1),
        compiler_params=pltpu.CompilerParams(dimension_semantics=("arbitrary",)),
    )(src_ids, tile_mask, grad_query, cot, zvalue, w_q, w_n2, w_n1)


def attend_kernel(scale, live_ref, q_ref, go_ref, kv_ref, wkv_ref, gq_ref, slots_ref, gk_acc, gv_acc):
    step = pl.program_id(0)
    width = q_ref.shape[1]

    @pl.when(step == 0)
    def _():
        gk_acc[...] = jnp.zeros(gk_acc.shape, jnp.float32)
        gv_acc[...] = jnp.zeros(gv_acc.shape, jnp.float32)

    queries = q_ref[...]
    grad_out = go_ref[...]
    keys = kv_ref[:, 0:width]
    values = kv_ref[:, width : 2 * width]
    nt = (((1,), (1,)), ((), ()))
    tn = (((0,), (0,)), ((), ()))
    scores = lax.dot_general(queries, keys, nt, preferred_element_type=jnp.float32) * scale
    scores = jnp.where(live_ref[...] > 0, scores, -jnp.inf)
    highest = jnp.max(scores, axis=1, keepdims=True)
    expo_terms = jnp.exp(scores - highest)
    probability = expo_terms / jnp.sum(expo_terms, axis=1, keepdims=True)
    prob_low = probability.astype(jnp.bfloat16)
    grad_prob = lax.dot_general(grad_out, values, nt, preferred_element_type=jnp.float32)
    spread = jnp.sum(probability * grad_prob, axis=1, keepdims=True)
    grad_score = (probability * (grad_prob - spread) * scale).astype(jnp.bfloat16)
    gq_ref[...] = jnp.dot(grad_score, keys, preferred_element_type=jnp.float32).astype(gq_ref.dtype)
    gk_acc[...] += lax.dot_general(grad_score, queries, tn, preferred_element_type=jnp.float32)
    gv_acc[...] += lax.dot_general(prob_low, grad_out, tn, preferred_element_type=jnp.float32)

    @pl.when(step == pl.num_programs(0) - 1)
    def _():
        grad_keys = gk_acc[...].astype(jnp.bfloat16)
        grad_vals = gv_acc[...].astype(jnp.bfloat16)
        slots = lax.dot_general(grad_keys, wkv_ref[:, 0:width], nt, preferred_element_type=jnp.float32)
        slots += lax.dot_general(grad_vals, wkv_ref[:, width : 2 * width], nt, preferred_element_type=jnp.float32)
        slots_ref[...] = slots.astype(slots_ref.dtype)


def attend_back(live, queries, grad_out, keyvals, w_kv, scale, rows_per_step=1024):
    rows, width = queries.shape
    slots = keyvals.shape[0]
    steps = rows // rows_per_step
    row_block = pl.BlockSpec((rows_per_step, width), lambda i: (i, 0))
    return pl.pallas_call(
        functools.partial(attend_kernel, scale),
        grid=(steps,),
        in_specs=[
            pl.BlockSpec((1, slots), lambda i: (0, 0)),
            row_block,
            row_block,
            pl.BlockSpec((slots, 2 * width), lambda i: (0, 0)),
            pl.BlockSpec(w_kv.shape, lambda i: (0, 0)),
        ],
        out_specs=[row_block, pl.BlockSpec((slots, width), lambda i: (0, 0))],
        out_shape=(
            jax.ShapeDtypeStruct((rows, width), jnp.bfloat16),
            jax.ShapeDtypeStruct((slots, width), jnp.bfloat16),
        ),
        scratch_shapes=[
            pltpu.VMEM((slots, width), jnp.float32),
            pltpu.VMEM((slots, width), jnp.float32),
        ],
        compiler_params=pltpu.CompilerParams(dimension_semantics=("arbitrary",)),
        cost_estimate=pl.CostEstimate(
            flops=10 * rows * slots * width,
            transcendentals=rows * slots,
            bytes_accessed=2 * (3 * rows * width + 4 * slots * width),
        ),
    )(live, queries, grad_out, keyvals, w_kv)


def slope_of(values):
    sigma = 1.0 / (1.0 + jnp.exp(-values))
    return sigma * (1.0 + values * (1.0 - sigma))


def edge_back_kernel(lat_ref, own_ref, a_ref, b_ref, c_ref, d_ref, gn_ref, w1_ref, w2_ref, out_ref):
    nt = (((1,), (1,)), ((), ()))
    collected = own_ref[...]
    for ref in (a_ref, b_ref, c_ref, d_ref):
        collected = collected + ref[...].astype(jnp.float32)
    grad_msg = collected.astype(jnp.bfloat16)
    pre_act = jnp.dot(lat_ref[...], w1_ref[...], preferred_element_type=jnp.float32)
    grad_pre = lax.dot_general(grad_msg, w2_ref[...], nt, preferred_element_type=jnp.float32)
    grad_pre = (grad_pre * slope_of(pre_act)).astype(jnp.bfloat16)
    total = gn_ref[...] + lax.dot_general(grad_pre, w1_ref[...], nt, preferred_element_type=jnp.float32)
    out_ref[...] = total.astype(out_ref.dtype)


def edge_back(latent, own_part, received, grad_node, w_e1, w_e2, rows_per_step=512):
    rows, width = latent.shape
    row_block = pl.BlockSpec((rows_per_step, width), lambda i: (i, 0))
    weight = pl.BlockSpec(w_e1.shape, lambda i: (0, 0))
    return pl.pallas_call(
        edge_back_kernel,
        grid=(rows // rows_per_step,),
        in_specs=[row_block] * (3 + len(received)) + [weight, weight],
        out_specs=row_block,
        out_shape=jax.ShapeDtypeStruct((rows, width), jnp.bfloat16),
        cost_estimate=pl.CostEstimate(
            flops=6 * rows * width * width,
            transcendentals=rows * width,
            bytes_accessed=rows * width * (2 + 4 + 2 * len(received) + 4 + 2),
        ),
    )(latent, own_part, *received, grad_node, w_e1, w_e2)


def dense(left, right):
    return jnp.dot(left, right, preferred_element_type=jnp.float32)


def silu_slope(values):
    sigma = jax.nn.sigmoid(values)
    return sigma * (1.0 + values * (1.0 - sigma))


def on_device(
    nodes, tile_src, tile_mask, tokens, tok_count, w_e1, w_e2, w_n1, w_n2, w_q, w_kv, w_o, cotangent
):
    latent = nodes[0, 0]
    node_rows = latent.shape[0]
    latent_width = latent.shape[1]
    block_count = tile_src.shape[2]
    tile_count = tile_src.shape[3]
    blk_rows = tile_mask.shape[-1]
    rows_px = lax.axis_size("px")
    rows_py = lax.axis_size("py")
    devices = rows_px * rows_py
    score_scale = 1.0 / math.sqrt(latent_width)
    pre_act = dense(latent, w_e1)
    activation = jax.nn.silu(pre_act).astype(jnp.bfloat16)
    message = dense(activation, w_e2).astype(jnp.bfloat16)
    sources = [
        message,
        passed_along(message, "px", 1),
        passed_along(message, "px", -1),
        passed_along(message, "py", 1),
        passed_along(message, "py", -1),
    ]
    src_ids = tile_src[0, 0].reshape(-1)
    zvalue, queries = tile_gather(
        src_ids,
        tile_mask[0, 0],
        [part.reshape(block_count, blk_rows, latent_width) for part in sources],
        latent,
        w_n1,
        w_n2,
        w_q,
    )
    own_tokens = tokens[0]
    slot_count = own_tokens.shape[0] // devices
    token_groups = own_tokens.reshape(devices, slot_count, latent_width)
    arrived_tokens = lax.all_to_all(
        token_groups, ("px", "py"), split_axis=0, concat_axis=0, tiled=True
    )
    arrived_tokens = arrived_tokens.reshape(devices * slot_count, latent_width)
    arrived = dense(arrived_tokens, w_kv).astype(jnp.bfloat16)
    live_keys = (jnp.arange(slot_count)[None, :] < tok_count[:, 0][:, None]).reshape(1, -1)
    grad_out = dense(cotangent[0, 0], w_o.T).astype(jnp.bfloat16)
    grad_query, grad_slots = attend_back(
        live_keys.astype(jnp.float32), queries, grad_out, arrived, w_kv, score_scale
    )
    returned = lax.all_to_all(
        grad_slots.reshape(devices, slot_count, latent_width),
        ("px", "py"),
        split_axis=0,
        concat_axis=0,
        tiled=True,
    )
    grad_tokens = returned.reshape(devices * slot_count, latent_width)
    grad_node, own_part, *outbound = tile_scatter(
        src_ids, tile_mask[0, 0], grad_query, cotangent[0, 0], zvalue, w_q, w_n2, w_n1, len(sources)
    )
    outbound = [part.reshape(node_rows, latent_width) for part in outbound]
    received = [
        passed_along(outbound[0], "px", -1),
        passed_along(outbound[1], "px", 1),
        passed_along(outbound[2], "py", -1),
        passed_along(outbound[3], "py", 1),
    ]
    grad_nodes = edge_back(
        latent, own_part.reshape(node_rows, latent_width), received, grad_node, w_e1, w_e2
    )
    return (grad_nodes[None, None], grad_tokens[None])


def solution(mesh):
    return jax.shard_map(
        on_device,
        mesh=mesh,
        in_specs=(
            P("px", "py", None, None),
            P("px", "py", None, None),
            P("px", "py", None, None, None, None),
            P(("px", "py"), None, None),
            P(None, ("px", "py")),
            P(),
            P(),
            P(),
            P(),
            P(),
            P(),
            P(),
            P("px", "py", None, None),
        ),
        out_specs=(P("px", "py", None, None), P(("px", "py"), None, None)),
        check_vma=False,
    )
```

```python
import functools
import math

import jax
import jax.numpy as jnp
from jax import lax
from jax.experimental import pallas as pl
from jax.experimental.pallas import tpu as pltpu
from jax.sharding import PartitionSpec as P


def with_halo(block, sides, width):
    for axis, dim in sides:
        count = lax.axis_size(axis)
        forward = [(i, i + 1) for i in range(count - 1)]
        backward = [(target, source) for source, target in forward]
        low = lax.ppermute(
            lax.slice_in_dim(block, block.shape[dim] - width, None, axis=dim), axis, forward
        )
        high = lax.ppermute(lax.slice_in_dim(block, 0, width, axis=dim), axis, backward)
        block = jnp.concatenate([low, block, high], axis=dim)
    return block


def passed_along(value, axis, steps):
    count = lax.axis_size(axis)
    leading, last = (max(0, -steps), min(count, count - steps))
    return lax.ppermute(value, axis, [(source, source + steps) for source in range(leading, last)])


def gather_kernel(
    group, src_ids, mask_ref, own, up, down, left, right, lat_ref, wn1_ref, wn2_ref, wq_ref,
    z_ref, q_ref, rhs, gath
):
    step = pl.program_id(0)
    tiles = mask_ref.shape[1]
    blk = mask_ref.shape[2]
    per_side = own.shape[0]
    for g in range(group):
        for k in range(tiles):
            picked = src_ids[(step * group + g) * tiles + k]
            side = picked // per_side
            block = picked % per_side
            for index, ref in enumerate((own, up, down, left, right)):

                @pl.when(side == index)
                def _():
                    rhs[k * blk : (k + 1) * blk, :] = ref[block]

        bits = jnp.concatenate(
            [mask_ref[g, k].astype(jnp.float32).astype(jnp.bfloat16) for k in range(tiles)], axis=1
        )
        total = jnp.dot(bits, rhs[...], preferred_element_type=jnp.float32)
        gath[g * blk : (g + 1) * blk, :] = total.astype(gath.dtype)
    width = lat_ref.shape[1]
    latent = lat_ref[...]
    zvalue = jnp.dot(latent, wn1_ref[0:width, :], preferred_element_type=jnp.float32)
    zvalue += jnp.dot(gath[...], wn1_ref[width : 2 * width, :], preferred_element_type=jnp.float32)
    z_ref[...] = zvalue
    hidden = (zvalue / (1.0 + jnp.exp(-zvalue))).astype(jnp.bfloat16)
    updated = latent.astype(jnp.float32) + jnp.dot(hidden, wn2_ref[...], preferred_element_type=jnp.float32)
    queries = jnp.dot(updated.astype(jnp.bfloat16), wq_ref[...], preferred_element_type=jnp.float32)
    q_ref[...] = queries.astype(q_ref.dtype)


def tile_gather(src_ids, tile_mask, sources, latent, w_n1, w_n2, w_q, group=4):
    blocks, tiles, blk, _ = tile_mask.shape
    width = sources[0].shape[-1]
    whole = pl.BlockSpec((blocks, blk, width), lambda i, ids: (0, 0, 0))
    rows = pl.BlockSpec((group * blk, width), lambda i, ids: (i, 0))
    return pl.pallas_call(
        functools.partial(gather_kernel, group),
        grid_spec=pltpu.PrefetchScalarGridSpec(
            num_scalar_prefetch=1,
            grid=(blocks // group,),
            in_specs=[pl.BlockSpec((group, tiles, blk, blk), lambda i, ids: (i, 0, 0, 0))]
            + [whole] * len(sources)
            + [rows]
            + [pl.BlockSpec(w.shape, lambda i, ids: (0, 0)) for w in (w_n1, w_n2, w_q)],
            out_specs=[rows, rows],
            scratch_shapes=[
                pltpu.VMEM((tiles * blk, width), jnp.bfloat16),
                pltpu.VMEM((group * blk, width), jnp.bfloat16),
            ],
        ),
        out_shape=(
            jax.ShapeDtypeStruct((blocks * blk, width), jnp.float32),
            jax.ShapeDtypeStruct((blocks * blk, width), jnp.bfloat16),
        ),
        compiler_params=pltpu.CompilerParams(dimension_semantics=("arbitrary",)),
    )(src_ids, tile_mask, *sources, latent, w_n1, w_n2, w_q)


def scatter_kernel(group, src_ids, mask_ref, gq_ref, cot_ref, z_ref, wq_ref, wn2_ref, wn1_ref, gn_ref, own_ref, *rest):
    side_refs, total = rest[:-1], rest[-1]
    step = pl.program_id(0)
    tiles = mask_ref.shape[1]
    blk = mask_ref.shape[2]
    per_side = own_ref.shape[0]
    width = gq_ref.shape[1]
    tn = (((0,), (0,)), ((), ()))
    nt = (((1,), (1,)), ((), ()))
    grad_update = cot_ref[...].astype(jnp.float32) + lax.dot_general(
        gq_ref[...], wq_ref[...], nt, preferred_element_type=jnp.float32
    )
    update_low = grad_update.astype(jnp.bfloat16)
    grad_z = lax.dot_general(update_low, wn2_ref[...], nt, preferred_element_type=jnp.float32)
    grad_z = (grad_z * slope_of(z_ref[...])).astype(jnp.bfloat16)
    grad_agg = lax.dot_general(
        grad_z, wn1_ref[width : 2 * width, :], nt, preferred_element_type=jnp.float32
    ).astype(jnp.bfloat16)
    gn_ref[...] = grad_update + lax.dot_general(
        grad_z, wn1_ref[0:width, :], nt, preferred_element_type=jnp.float32
    )

    @pl.when(step == 0)
    def _():
        total[...] = jnp.zeros(total.shape, jnp.float32)

    for g in range(group):
        bits = jnp.concatenate(
            [mask_ref[g, k].astype(jnp.float32).astype(jnp.bfloat16) for k in range(tiles)], axis=1
        )
        grad_rows = grad_agg[g * blk : (g + 1) * blk, :]
        parts = lax.dot_general(bits, grad_rows, tn, preferred_element_type=jnp.float32)
        for k in range(tiles):
            picked = src_ids[(step * group + g) * tiles + k]
            total[picked] += parts[k * blk : (k + 1) * blk]

    @pl.when(step == pl.num_programs(0) - 1)
    def _():
        own_ref[...] = total[0:per_side]
        for side, out_ref in enumerate(side_refs):
            start = (side + 1) * per_side
            out_ref[...] = total[start : start + per_side].astype(out_ref.dtype)


def tile_scatter(src_ids, tile_mask, grad_query, cot, zvalue, w_q, w_n2, w_n1, sides, group=4):
    blocks, tiles, blk, _ = tile_mask.shape
    width = grad_query.shape[-1]
    rows = pl.BlockSpec((group * blk, width), lambda i, ids: (i, 0))
    return pl.pallas_call(
        functools.partial(scatter_kernel, group),
        grid_spec=pltpu.PrefetchScalarGridSpec(
            num_scalar_prefetch=1,
            grid=(blocks // group,),
            in_specs=[
                pl.BlockSpec((group, tiles, blk, blk), lambda i, ids: (i, 0, 0, 0)),
                rows,
                rows,
                rows,
                pl.BlockSpec(w_q.shape, lambda i, ids: (0, 0)),
                pl.BlockSpec(w_n2.shape, lambda i, ids: (0, 0)),
                pl.BlockSpec(w_n1.shape, lambda i, ids: (0, 0)),
            ],
            out_specs=[rows]
            + [pl.BlockSpec((blocks, blk, width), lambda i, ids: (0, 0, 0))] * sides,
            scratch_shapes=[pltpu.VMEM((sides * blocks, blk, width), jnp.float32)],
        ),
        out_shape=[jax.ShapeDtypeStruct((blocks * blk, width), jnp.float32)]
        + [jax.ShapeDtypeStruct((blocks, blk, width), jnp.float32)]
        + [jax.ShapeDtypeStruct((blocks, blk, width), jnp.bfloat16)] * (sides - 1),
        compiler_params=pltpu.CompilerParams(dimension_semantics=("arbitrary",)),
    )(src_ids, tile_mask, grad_query, cot, zvalue, w_q, w_n2, w_n1)


def attend_kernel(scale, live_ref, q_ref, go_ref, kv_ref, wkv_ref, gq_ref, slots_ref, gk_acc, gv_acc):
    step = pl.program_id(0)
    width = q_ref.shape[1]

    @pl.when(step == 0)
    def _():
        gk_acc[...] = jnp.zeros(gk_acc.shape, jnp.float32)
        gv_acc[...] = jnp.zeros(gv_acc.shape, jnp.float32)

    queries = q_ref[...]
    grad_out = go_ref[...]
    keys = kv_ref[:, 0:width]
    values = kv_ref[:, width : 2 * width]
    nt = (((1,), (1,)), ((), ()))
    tn = (((0,), (0,)), ((), ()))
    scores = lax.dot_general(queries, keys, nt, preferred_element_type=jnp.float32) * scale
    scores = jnp.where(live_ref[...] > 0, scores, -jnp.inf)
    highest = jnp.max(scores, axis=1, keepdims=True)
    expo_terms = jnp.exp(scores - highest)
    probability = expo_terms / jnp.sum(expo_terms, axis=1, keepdims=True)
    prob_low = probability.astype(jnp.bfloat16)
    grad_prob = lax.dot_general(grad_out, values, nt, preferred_element_type=jnp.float32)
    spread = jnp.sum(probability * grad_prob, axis=1, keepdims=True)
    grad_score = (probability * (grad_prob - spread) * scale).astype(jnp.bfloat16)
    gq_ref[...] = jnp.dot(grad_score, keys, preferred_element_type=jnp.float32).astype(gq_ref.dtype)
    gk_acc[...] += lax.dot_general(grad_score, queries, tn, preferred_element_type=jnp.float32)
    gv_acc[...] += lax.dot_general(prob_low, grad_out, tn, preferred_element_type=jnp.float32)

    @pl.when(step == pl.num_programs(0) - 1)
    def _():
        grad_keys = gk_acc[...].astype(jnp.bfloat16)
        grad_vals = gv_acc[...].astype(jnp.bfloat16)
        slots = lax.dot_general(grad_keys, wkv_ref[:, 0:width], nt, preferred_element_type=jnp.float32)
        slots += lax.dot_general(grad_vals, wkv_ref[:, width : 2 * width], nt, preferred_element_type=jnp.float32)
        slots_ref[...] = slots.astype(slots_ref.dtype)


def attend_back(live, queries, grad_out, keyvals, w_kv, scale, rows_per_step=1024):
    rows, width = queries.shape
    slots = keyvals.shape[0]
    steps = rows // rows_per_step
    row_block = pl.BlockSpec((rows_per_step, width), lambda i: (i, 0))
    return pl.pallas_call(
        functools.partial(attend_kernel, scale),
        grid=(steps,),
        in_specs=[
            pl.BlockSpec((1, slots), lambda i: (0, 0)),
            row_block,
            row_block,
            pl.BlockSpec((slots, 2 * width), lambda i: (0, 0)),
            pl.BlockSpec(w_kv.shape, lambda i: (0, 0)),
        ],
        out_specs=[row_block, pl.BlockSpec((slots, width), lambda i: (0, 0))],
        out_shape=(
            jax.ShapeDtypeStruct((rows, width), jnp.bfloat16),
            jax.ShapeDtypeStruct((slots, width), jnp.bfloat16),
        ),
        scratch_shapes=[
            pltpu.VMEM((slots, width), jnp.float32),
            pltpu.VMEM((slots, width), jnp.float32),
        ],
        compiler_params=pltpu.CompilerParams(dimension_semantics=("arbitrary",)),
        cost_estimate=pl.CostEstimate(
            flops=10 * rows * slots * width,
            transcendentals=rows * slots,
            bytes_accessed=2 * (3 * rows * width + 4 * slots * width),
        ),
    )(live, queries, grad_out, keyvals, w_kv)


def slope_of(values):
    sigma = 1.0 / (1.0 + jnp.exp(-values))
    return sigma * (1.0 + values * (1.0 - sigma))


def edge_back_kernel(slope_ref, own_ref, a_ref, b_ref, c_ref, d_ref, gn_ref, w1_ref, w2_ref, out_ref):
    nt = (((1,), (1,)), ((), ()))
    collected = own_ref[...]
    for ref in (a_ref, b_ref, c_ref, d_ref):
        collected = collected + ref[...].astype(jnp.float32)
    grad_msg = collected.astype(jnp.bfloat16)
    grad_pre = lax.dot_general(grad_msg, w2_ref[...], nt, preferred_element_type=jnp.float32)
    grad_pre = (grad_pre * slope_ref[...]).astype(jnp.bfloat16)
    total = gn_ref[...] + lax.dot_general(grad_pre, w1_ref[...], nt, preferred_element_type=jnp.float32)
    out_ref[...] = total.astype(out_ref.dtype)


def edge_back(edge_slope, own_part, received, grad_node, w_e1, w_e2, rows_per_step=512):
    rows, width = edge_slope.shape
    row_block = pl.BlockSpec((rows_per_step, width), lambda i: (i, 0))
    weight = pl.BlockSpec(w_e1.shape, lambda i: (0, 0))
    return pl.pallas_call(
        edge_back_kernel,
        grid=(rows // rows_per_step,),
        in_specs=[row_block] * (3 + len(received)) + [weight, weight],
        out_specs=row_block,
        out_shape=jax.ShapeDtypeStruct((rows, width), jnp.bfloat16),
        cost_estimate=pl.CostEstimate(
            flops=6 * rows * width * width,
            transcendentals=rows * width,
            bytes_accessed=rows * width * (4 + 4 + 2 * len(received) + 4 + 2),
        ),
    )(edge_slope, own_part, *received, grad_node, w_e1, w_e2)


def dense(left, right):
    return jnp.dot(left, right, preferred_element_type=jnp.float32)


def silu_slope(values):
    sigma = jax.nn.sigmoid(values)
    return sigma * (1.0 + values * (1.0 - sigma))


def on_device(
    nodes, tile_src, tile_mask, tokens, tok_count, w_e1, w_e2, w_n1, w_n2, w_q, w_kv, w_o, cotangent
):
    latent = nodes[0, 0]
    node_rows = latent.shape[0]
    latent_width = latent.shape[1]
    block_count = tile_src.shape[2]
    tile_count = tile_src.shape[3]
    blk_rows = tile_mask.shape[-1]
    rows_px = lax.axis_size("px")
    rows_py = lax.axis_size("py")
    devices = rows_px * rows_py
    score_scale = 1.0 / math.sqrt(latent_width)
    pre_act = dense(latent, w_e1)
    activation = jax.nn.silu(pre_act).astype(jnp.bfloat16)
    message = dense(activation, w_e2).astype(jnp.bfloat16)
    sources = [
        message,
        passed_along(message, "px", 1),
        passed_along(message, "px", -1),
        passed_along(message, "py", 1),
        passed_along(message, "py", -1),
    ]
    src_ids = tile_src[0, 0].reshape(-1)
    zvalue, queries = tile_gather(
        src_ids,
        tile_mask[0, 0],
        [part.reshape(block_count, blk_rows, latent_width) for part in sources],
        latent,
        w_n1,
        w_n2,
        w_q,
    )
    own_tokens = tokens[0]
    slot_count = own_tokens.shape[0] // devices
    token_groups = own_tokens.reshape(devices, slot_count, latent_width)
    arrived_tokens = lax.all_to_all(
        token_groups, ("px", "py"), split_axis=0, concat_axis=0, tiled=True
    )
    arrived_tokens = arrived_tokens.reshape(devices * slot_count, latent_width)
    arrived = dense(arrived_tokens, w_kv).astype(jnp.bfloat16)
    live_keys = (jnp.arange(slot_count)[None, :] < tok_count[:, 0][:, None]).reshape(1, -1)
    grad_out = dense(cotangent[0, 0], w_o.T).astype(jnp.bfloat16)
    grad_query, grad_slots = attend_back(
        live_keys.astype(jnp.float32), queries, grad_out, arrived, w_kv, score_scale
    )
    returned = lax.all_to_all(
        grad_slots.reshape(devices, slot_count, latent_width),
        ("px", "py"),
        split_axis=0,
        concat_axis=0,
        tiled=True,
    )
    grad_tokens = returned.reshape(devices * slot_count, latent_width)
    grad_node, own_part, *outbound = tile_scatter(
        src_ids, tile_mask[0, 0], grad_query, cotangent[0, 0], zvalue, w_q, w_n2, w_n1, len(sources)
    )
    outbound = [part.reshape(node_rows, latent_width) for part in outbound]
    received = [
        passed_along(outbound[0], "px", -1),
        passed_along(outbound[1], "px", 1),
        passed_along(outbound[2], "py", -1),
        passed_along(outbound[3], "py", 1),
    ]
    late_pre_act, own_part = lax.optimization_barrier((pre_act, own_part))
    edge_slope = silu_slope(late_pre_act)
    grad_nodes = edge_back(
        edge_slope, own_part.reshape(node_rows, latent_width), received, grad_node, w_e1, w_e2
    )
    return (grad_nodes[None, None], grad_tokens[None])


def solution(mesh):
    return jax.shard_map(
        on_device,
        mesh=mesh,
        in_specs=(
            P("px", "py", None, None),
            P("px", "py", None, None),
            P("px", "py", None, None, None, None),
            P(("px", "py"), None, None),
            P(None, ("px", "py")),
            P(),
            P(),
            P(),
            P(),
            P(),
            P(),
            P(),
            P("px", "py", None, None),
        ),
        out_specs=(P("px", "py", None, None), P(("px", "py"), None, None)),
        check_vma=False,
    )
```

```python
import functools
import math

import jax
import jax.numpy as jnp
from jax import lax
from jax.experimental import pallas as pl
from jax.experimental.pallas import tpu as pltpu
from jax.sharding import PartitionSpec as P


def with_halo(block, sides, width):
    for axis, dim in sides:
        count = lax.axis_size(axis)
        forward = [(i, i + 1) for i in range(count - 1)]
        backward = [(target, source) for source, target in forward]
        low = lax.ppermute(
            lax.slice_in_dim(block, block.shape[dim] - width, None, axis=dim), axis, forward
        )
        high = lax.ppermute(lax.slice_in_dim(block, 0, width, axis=dim), axis, backward)
        block = jnp.concatenate([low, block, high], axis=dim)
    return block


def passed_along(value, axis, steps):
    count = lax.axis_size(axis)
    leading, last = (max(0, -steps), min(count, count - steps))
    return lax.ppermute(value, axis, [(source, source + steps) for source in range(leading, last)])


def gather_kernel(
    group, src_ids, mask_ref, own, up, down, left, right, lat_ref, wn1_ref, wn2_ref, wq_ref,
    z_ref, q_ref, rhs, gath
):
    step = pl.program_id(0)
    tiles = mask_ref.shape[1]
    blk = mask_ref.shape[2]
    per_side = own.shape[0]
    for g in range(group):
        for k in range(tiles):
            picked = src_ids[(step * group + g) * tiles + k]
            side = picked // per_side
            block = picked % per_side
            for index, ref in enumerate((own, up, down, left, right)):

                @pl.when(side == index)
                def _():
                    rhs[k * blk : (k + 1) * blk, :] = ref[block]

        bits = jnp.concatenate(
            [mask_ref[g, k].astype(jnp.float32).astype(jnp.bfloat16) for k in range(tiles)], axis=1
        )
        total = jnp.dot(bits, rhs[...], preferred_element_type=jnp.float32)
        gath[g * blk : (g + 1) * blk, :] = total.astype(gath.dtype)
    width = lat_ref.shape[1]
    latent = lat_ref[...]
    zvalue = jnp.dot(latent, wn1_ref[0:width, :], preferred_element_type=jnp.float32)
    zvalue += jnp.dot(gath[...], wn1_ref[width : 2 * width, :], preferred_element_type=jnp.float32)
    z_ref[...] = zvalue
    hidden = (zvalue / (1.0 + jnp.exp(-zvalue))).astype(jnp.bfloat16)
    updated = latent.astype(jnp.float32) + jnp.dot(hidden, wn2_ref[...], preferred_element_type=jnp.float32)
    queries = jnp.dot(updated.astype(jnp.bfloat16), wq_ref[...], preferred_element_type=jnp.float32)
    q_ref[...] = queries.astype(q_ref.dtype)


def tile_gather(src_ids, tile_mask, sources, latent, w_n1, w_n2, w_q, group=4):
    blocks, tiles, blk, _ = tile_mask.shape
    width = sources[0].shape[-1]
    whole = pl.BlockSpec((blocks, blk, width), lambda i, ids: (0, 0, 0))
    rows = pl.BlockSpec((group * blk, width), lambda i, ids: (i, 0))
    return pl.pallas_call(
        functools.partial(gather_kernel, group),
        grid_spec=pltpu.PrefetchScalarGridSpec(
            num_scalar_prefetch=1,
            grid=(blocks // group,),
            in_specs=[pl.BlockSpec((group, tiles, blk, blk), lambda i, ids: (i, 0, 0, 0))]
            + [whole] * len(sources)
            + [rows]
            + [pl.BlockSpec(w.shape, lambda i, ids: (0, 0)) for w in (w_n1, w_n2, w_q)],
            out_specs=[rows, rows],
            scratch_shapes=[
                pltpu.VMEM((tiles * blk, width), jnp.bfloat16),
                pltpu.VMEM((group * blk, width), jnp.bfloat16),
            ],
        ),
        out_shape=(
            jax.ShapeDtypeStruct((blocks * blk, width), jnp.float32),
            jax.ShapeDtypeStruct((blocks * blk, width), jnp.bfloat16),
        ),
        compiler_params=pltpu.CompilerParams(dimension_semantics=("arbitrary",)),
    )(src_ids, tile_mask, *sources, latent, w_n1, w_n2, w_q)


def scatter_kernel(group, src_ids, mask_ref, gq_ref, cot_ref, z_ref, wq_ref, wn2_ref, wn1_ref, gn_ref, own_ref, *rest):
    side_refs, total = rest[:-1], rest[-1]
    step = pl.program_id(0)
    tiles = mask_ref.shape[1]
    blk = mask_ref.shape[2]
    per_side = own_ref.shape[0]
    width = gq_ref.shape[1]
    tn = (((0,), (0,)), ((), ()))
    nt = (((1,), (1,)), ((), ()))
    grad_update = cot_ref[...].astype(jnp.float32) + lax.dot_general(
        gq_ref[...], wq_ref[...], nt, preferred_element_type=jnp.float32
    )
    update_low = grad_update.astype(jnp.bfloat16)
    grad_z = lax.dot_general(update_low, wn2_ref[...], nt, preferred_element_type=jnp.float32)
    grad_z = (grad_z * slope_of(z_ref[...])).astype(jnp.bfloat16)
    grad_agg = lax.dot_general(
        grad_z, wn1_ref[width : 2 * width, :], nt, preferred_element_type=jnp.float32
    ).astype(jnp.bfloat16)
    gn_ref[...] = grad_update + lax.dot_general(
        grad_z, wn1_ref[0:width, :], nt, preferred_element_type=jnp.float32
    )

    @pl.when(step == 0)
    def _():
        total[...] = jnp.zeros(total.shape, jnp.float32)

    for g in range(group):
        bits = jnp.concatenate(
            [mask_ref[g, k].astype(jnp.float32).astype(jnp.bfloat16) for k in range(tiles)], axis=1
        )
        grad_rows = grad_agg[g * blk : (g + 1) * blk, :]
        parts = lax.dot_general(bits, grad_rows, tn, preferred_element_type=jnp.float32)
        for k in range(tiles):
            picked = src_ids[(step * group + g) * tiles + k]
            total[picked] += parts[k * blk : (k + 1) * blk]

    @pl.when(step == pl.num_programs(0) - 1)
    def _():
        own_ref[...] = total[0:per_side]
        for side, out_ref in enumerate(side_refs):
            start = (side + 1) * per_side
            out_ref[...] = total[start : start + per_side].astype(out_ref.dtype)


def tile_scatter(src_ids, tile_mask, grad_query, cot, zvalue, w_q, w_n2, w_n1, sides, group=4):
    blocks, tiles, blk, _ = tile_mask.shape
    width = grad_query.shape[-1]
    rows = pl.BlockSpec((group * blk, width), lambda i, ids: (i, 0))
    return pl.pallas_call(
        functools.partial(scatter_kernel, group),
        grid_spec=pltpu.PrefetchScalarGridSpec(
            num_scalar_prefetch=1,
            grid=(blocks // group,),
            in_specs=[
                pl.BlockSpec((group, tiles, blk, blk), lambda i, ids: (i, 0, 0, 0)),
                rows,
                rows,
                rows,
                pl.BlockSpec(w_q.shape, lambda i, ids: (0, 0)),
                pl.BlockSpec(w_n2.shape, lambda i, ids: (0, 0)),
                pl.BlockSpec(w_n1.shape, lambda i, ids: (0, 0)),
            ],
            out_specs=[rows]
            + [pl.BlockSpec((blocks, blk, width), lambda i, ids: (0, 0, 0))] * sides,
            scratch_shapes=[pltpu.VMEM((sides * blocks, blk, width), jnp.float32)],
        ),
        out_shape=[jax.ShapeDtypeStruct((blocks * blk, width), jnp.float32)]
        + [jax.ShapeDtypeStruct((blocks, blk, width), jnp.float32)]
        + [jax.ShapeDtypeStruct((blocks, blk, width), jnp.bfloat16)] * (sides - 1),
        compiler_params=pltpu.CompilerParams(dimension_semantics=("arbitrary",)),
    )(src_ids, tile_mask, grad_query, cot, zvalue, w_q, w_n2, w_n1)


def attend_kernel(scale, live_ref, q_ref, go_ref, kv_ref, wkv_ref, gq_ref, slots_ref, gk_acc, gv_acc):
    step = pl.program_id(0)
    width = q_ref.shape[1]

    @pl.when(step == 0)
    def _():
        gk_acc[...] = jnp.zeros(gk_acc.shape, jnp.float32)
        gv_acc[...] = jnp.zeros(gv_acc.shape, jnp.float32)

    queries = q_ref[...]
    grad_out = go_ref[...]
    keys = kv_ref[:, 0:width]
    values = kv_ref[:, width : 2 * width]
    nt = (((1,), (1,)), ((), ()))
    tn = (((0,), (0,)), ((), ()))
    scores = lax.dot_general(queries, keys, nt, preferred_element_type=jnp.float32) * scale
    scores = jnp.where(live_ref[...] > 0, scores, -jnp.inf)
    highest = jnp.max(scores, axis=1, keepdims=True)
    expo_terms = jnp.exp(scores - highest)
    probability = expo_terms / jnp.sum(expo_terms, axis=1, keepdims=True)
    prob_low = probability.astype(jnp.bfloat16)
    grad_prob = lax.dot_general(grad_out, values, nt, preferred_element_type=jnp.float32)
    spread = jnp.sum(probability * grad_prob, axis=1, keepdims=True)
    grad_score = (probability * (grad_prob - spread) * scale).astype(jnp.bfloat16)
    gq_ref[...] = jnp.dot(grad_score, keys, preferred_element_type=jnp.float32).astype(gq_ref.dtype)
    gk_acc[...] += lax.dot_general(grad_score, queries, tn, preferred_element_type=jnp.float32)
    gv_acc[...] += lax.dot_general(prob_low, grad_out, tn, preferred_element_type=jnp.float32)

    @pl.when(step == pl.num_programs(0) - 1)
    def _():
        grad_keys = gk_acc[...].astype(jnp.bfloat16)
        grad_vals = gv_acc[...].astype(jnp.bfloat16)
        slots = lax.dot_general(grad_keys, wkv_ref[:, 0:width], nt, preferred_element_type=jnp.float32)
        slots += lax.dot_general(grad_vals, wkv_ref[:, width : 2 * width], nt, preferred_element_type=jnp.float32)
        slots_ref[...] = slots.astype(slots_ref.dtype)


def attend_back(live, queries, grad_out, keyvals, w_kv, scale, rows_per_step=1024):
    rows, width = queries.shape
    slots = keyvals.shape[0]
    steps = rows // rows_per_step
    row_block = pl.BlockSpec((rows_per_step, width), lambda i: (i, 0))
    return pl.pallas_call(
        functools.partial(attend_kernel, scale),
        grid=(steps,),
        in_specs=[
            pl.BlockSpec((1, slots), lambda i: (0, 0)),
            row_block,
            row_block,
            pl.BlockSpec((slots, 2 * width), lambda i: (0, 0)),
            pl.BlockSpec(w_kv.shape, lambda i: (0, 0)),
        ],
        out_specs=[row_block, pl.BlockSpec((slots, width), lambda i: (0, 0))],
        out_shape=(
            jax.ShapeDtypeStruct((rows, width), jnp.bfloat16),
            jax.ShapeDtypeStruct((slots, width), jnp.bfloat16),
        ),
        scratch_shapes=[
            pltpu.VMEM((slots, width), jnp.float32),
            pltpu.VMEM((slots, width), jnp.float32),
        ],
        compiler_params=pltpu.CompilerParams(dimension_semantics=("arbitrary",)),
        cost_estimate=pl.CostEstimate(
            flops=10 * rows * slots * width,
            transcendentals=rows * slots,
            bytes_accessed=2 * (3 * rows * width + 4 * slots * width),
        ),
    )(live, queries, grad_out, keyvals, w_kv)


def slope_of(values):
    sigma = 1.0 / (1.0 + jnp.exp(-values))
    return sigma * (1.0 + values * (1.0 - sigma))


def edge_back_kernel(slope_ref, own_ref, a_ref, b_ref, c_ref, d_ref, gn_ref, w1_ref, w2_ref, out_ref):
    nt = (((1,), (1,)), ((), ()))
    collected = own_ref[...]
    for ref in (a_ref, b_ref, c_ref, d_ref):
        collected = collected + ref[...].astype(jnp.float32)
    grad_msg = collected.astype(jnp.bfloat16)
    grad_pre = lax.dot_general(grad_msg, w2_ref[...], nt, preferred_element_type=jnp.float32)
    grad_pre = (grad_pre * slope_ref[...]).astype(jnp.bfloat16)
    total = gn_ref[...] + lax.dot_general(grad_pre, w1_ref[...], nt, preferred_element_type=jnp.float32)
    out_ref[...] = total.astype(out_ref.dtype)


def edge_back(edge_slope, own_part, received, grad_node, w_e1, w_e2, rows_per_step=256):
    rows, width = edge_slope.shape
    row_block = pl.BlockSpec((rows_per_step, width), lambda i: (i, 0))
    weight = pl.BlockSpec(w_e1.shape, lambda i: (0, 0))
    return pl.pallas_call(
        edge_back_kernel,
        grid=(rows // rows_per_step,),
        in_specs=[row_block] * (3 + len(received)) + [weight, weight],
        out_specs=row_block,
        out_shape=jax.ShapeDtypeStruct((rows, width), jnp.bfloat16),
        cost_estimate=pl.CostEstimate(
            flops=6 * rows * width * width,
            transcendentals=rows * width,
            bytes_accessed=rows * width * (4 + 4 + 2 * len(received) + 4 + 2),
        ),
    )(edge_slope, own_part, *received, grad_node, w_e1, w_e2)


def dense(left, right):
    return jnp.dot(left, right, preferred_element_type=jnp.float32)


def silu_slope(values):
    sigma = jax.nn.sigmoid(values)
    return sigma * (1.0 + values * (1.0 - sigma))


def on_device(
    nodes, tile_src, tile_mask, tokens, tok_count, w_e1, w_e2, w_n1, w_n2, w_q, w_kv, w_o, cotangent
):
    latent = nodes[0, 0]
    node_rows = latent.shape[0]
    latent_width = latent.shape[1]
    block_count = tile_src.shape[2]
    tile_count = tile_src.shape[3]
    blk_rows = tile_mask.shape[-1]
    rows_px = lax.axis_size("px")
    rows_py = lax.axis_size("py")
    devices = rows_px * rows_py
    score_scale = 1.0 / math.sqrt(latent_width)
    pre_act = dense(latent, w_e1)
    activation = jax.nn.silu(pre_act).astype(jnp.bfloat16)
    message = dense(activation, w_e2).astype(jnp.bfloat16)
    sources = [
        message,
        passed_along(message, "px", 1),
        passed_along(message, "px", -1),
        passed_along(message, "py", 1),
        passed_along(message, "py", -1),
    ]
    src_ids = tile_src[0, 0].reshape(-1)
    zvalue, queries = tile_gather(
        src_ids,
        tile_mask[0, 0],
        [part.reshape(block_count, blk_rows, latent_width) for part in sources],
        latent,
        w_n1,
        w_n2,
        w_q,
    )
    own_tokens = tokens[0]
    slot_count = own_tokens.shape[0] // devices
    token_groups = own_tokens.reshape(devices, slot_count, latent_width)
    arrived_tokens = lax.all_to_all(
        token_groups, ("px", "py"), split_axis=0, concat_axis=0, tiled=True
    )
    arrived_tokens = arrived_tokens.reshape(devices * slot_count, latent_width)
    arrived = dense(arrived_tokens, w_kv).astype(jnp.bfloat16)
    live_keys = (jnp.arange(slot_count)[None, :] < tok_count[:, 0][:, None]).reshape(1, -1)
    grad_out = dense(cotangent[0, 0], w_o.T).astype(jnp.bfloat16)
    grad_query, grad_slots = attend_back(
        live_keys.astype(jnp.float32), queries, grad_out, arrived, w_kv, score_scale
    )
    returned = lax.all_to_all(
        grad_slots.reshape(devices, slot_count, latent_width),
        ("px", "py"),
        split_axis=0,
        concat_axis=0,
        tiled=True,
    )
    grad_tokens = returned.reshape(devices * slot_count, latent_width)
    grad_node, own_part, *outbound = tile_scatter(
        src_ids, tile_mask[0, 0], grad_query, cotangent[0, 0], zvalue, w_q, w_n2, w_n1, len(sources)
    )
    outbound = [part.reshape(node_rows, latent_width) for part in outbound]
    received = [
        passed_along(outbound[0], "px", -1),
        passed_along(outbound[1], "px", 1),
        passed_along(outbound[2], "py", -1),
        passed_along(outbound[3], "py", 1),
    ]
    late_pre_act, own_part = lax.optimization_barrier((pre_act, own_part))
    edge_slope = silu_slope(late_pre_act)
    grad_nodes = edge_back(
        edge_slope, own_part.reshape(node_rows, latent_width), received, grad_node, w_e1, w_e2
    )
    return (grad_nodes[None, None], grad_tokens[None])


def solution(mesh):
    return jax.shard_map(
        on_device,
        mesh=mesh,
        in_specs=(
            P("px", "py", None, None),
            P("px", "py", None, None),
            P("px", "py", None, None, None, None),
            P(("px", "py"), None, None),
            P(None, ("px", "py")),
            P(),
            P(),
            P(),
            P(),
            P(),
            P(),
            P(),
            P("px", "py", None, None),
        ),
        out_specs=(P("px", "py", None, None), P(("px", "py"), None, None)),
        check_vma=False,
    )
```

```python
import functools
import math

import jax
import jax.numpy as jnp
from jax import lax
from jax.experimental import pallas as pl
from jax.experimental.pallas import tpu as pltpu
from jax.sharding import PartitionSpec as P


def with_halo(block, sides, width):
    for axis, dim in sides:
        count = lax.axis_size(axis)
        forward = [(i, i + 1) for i in range(count - 1)]
        backward = [(target, source) for source, target in forward]
        low = lax.ppermute(
            lax.slice_in_dim(block, block.shape[dim] - width, None, axis=dim), axis, forward
        )
        high = lax.ppermute(lax.slice_in_dim(block, 0, width, axis=dim), axis, backward)
        block = jnp.concatenate([low, block, high], axis=dim)
    return block


def passed_along(value, axis, steps):
    count = lax.axis_size(axis)
    leading, last = (max(0, -steps), min(count, count - steps))
    return lax.ppermute(value, axis, [(source, source + steps) for source in range(leading, last)])


def gather_kernel(
    group, src_ids, mask_ref, own, up, down, left, right, lat_ref, wn1_ref, wn2_ref, wq_ref,
    z_ref, q_ref, rhs, gath
):
    step = pl.program_id(0)
    tiles = mask_ref.shape[1]
    blk = mask_ref.shape[2]
    per_side = own.shape[0]
    for g in range(group):
        for k in range(tiles):
            picked = src_ids[(step * group + g) * tiles + k]
            side = picked // per_side
            block = picked % per_side
            for index, ref in enumerate((own, up, down, left, right)):

                @pl.when(side == index)
                def _():
                    rhs[k * blk : (k + 1) * blk, :] = ref[block]

        bits = jnp.concatenate(
            [mask_ref[g, k].astype(jnp.float32).astype(jnp.bfloat16) for k in range(tiles)], axis=1
        )
        total = jnp.dot(bits, rhs[...], preferred_element_type=jnp.float32)
        gath[g * blk : (g + 1) * blk, :] = total.astype(gath.dtype)
    width = lat_ref.shape[1]
    latent = lat_ref[...]
    zvalue = jnp.dot(latent, wn1_ref[0:width, :], preferred_element_type=jnp.float32)
    zvalue += jnp.dot(gath[...], wn1_ref[width : 2 * width, :], preferred_element_type=jnp.float32)
    z_ref[...] = zvalue
    hidden = (zvalue / (1.0 + jnp.exp(-zvalue))).astype(jnp.bfloat16)
    updated = latent.astype(jnp.float32) + jnp.dot(hidden, wn2_ref[...], preferred_element_type=jnp.float32)
    queries = jnp.dot(updated.astype(jnp.bfloat16), wq_ref[...], preferred_element_type=jnp.float32)
    q_ref[...] = queries.astype(q_ref.dtype)


def tile_gather(src_ids, tile_mask, sources, latent, w_n1, w_n2, w_q, group=4):
    blocks, tiles, blk, _ = tile_mask.shape
    width = sources[0].shape[-1]
    whole = pl.BlockSpec((blocks, blk, width), lambda i, ids: (0, 0, 0))
    rows = pl.BlockSpec((group * blk, width), lambda i, ids: (i, 0))
    return pl.pallas_call(
        functools.partial(gather_kernel, group),
        grid_spec=pltpu.PrefetchScalarGridSpec(
            num_scalar_prefetch=1,
            grid=(blocks // group,),
            in_specs=[pl.BlockSpec((group, tiles, blk, blk), lambda i, ids: (i, 0, 0, 0))]
            + [whole] * len(sources)
            + [rows]
            + [pl.BlockSpec(w.shape, lambda i, ids: (0, 0)) for w in (w_n1, w_n2, w_q)],
            out_specs=[rows, rows],
            scratch_shapes=[
                pltpu.VMEM((tiles * blk, width), jnp.bfloat16),
                pltpu.VMEM((group * blk, width), jnp.bfloat16),
            ],
        ),
        out_shape=(
            jax.ShapeDtypeStruct((blocks * blk, width), jnp.float32),
            jax.ShapeDtypeStruct((blocks * blk, width), jnp.bfloat16),
        ),
        compiler_params=pltpu.CompilerParams(dimension_semantics=("arbitrary",)),
    )(src_ids, tile_mask, *sources, latent, w_n1, w_n2, w_q)


def scatter_kernel(group, src_ids, mask_ref, gq_ref, cot_ref, z_ref, wq_ref, wn2_ref, wn1_ref, gn_ref, own_ref, *rest):
    side_refs, total = rest[:-1], rest[-1]
    step = pl.program_id(0)
    tiles = mask_ref.shape[1]
    blk = mask_ref.shape[2]
    per_side = own_ref.shape[0]
    width = gq_ref.shape[1]
    tn = (((0,), (0,)), ((), ()))
    nt = (((1,), (1,)), ((), ()))
    grad_update = cot_ref[...].astype(jnp.float32) + lax.dot_general(
        gq_ref[...], wq_ref[...], nt, preferred_element_type=jnp.float32
    )
    update_low = grad_update.astype(jnp.bfloat16)
    grad_z = lax.dot_general(update_low, wn2_ref[...], nt, preferred_element_type=jnp.float32)
    grad_z = (grad_z * slope_of(z_ref[...])).astype(jnp.bfloat16)
    grad_agg = lax.dot_general(
        grad_z, wn1_ref[width : 2 * width, :], nt, preferred_element_type=jnp.float32
    ).astype(jnp.bfloat16)
    gn_ref[...] = grad_update + lax.dot_general(
        grad_z, wn1_ref[0:width, :], nt, preferred_element_type=jnp.float32
    )

    @pl.when(step == 0)
    def _():
        total[...] = jnp.zeros(total.shape, jnp.float32)

    for g in range(group):
        bits = jnp.concatenate(
            [mask_ref[g, k].astype(jnp.float32).astype(jnp.bfloat16) for k in range(tiles)], axis=1
        )
        grad_rows = grad_agg[g * blk : (g + 1) * blk, :]
        parts = lax.dot_general(bits, grad_rows, tn, preferred_element_type=jnp.float32)
        for k in range(tiles):
            picked = src_ids[(step * group + g) * tiles + k]
            total[picked] += parts[k * blk : (k + 1) * blk]

    @pl.when(step == pl.num_programs(0) - 1)
    def _():
        own_ref[...] = total[0:per_side]
        for side, out_ref in enumerate(side_refs):
            start = (side + 1) * per_side
            out_ref[...] = total[start : start + per_side].astype(out_ref.dtype)


def tile_scatter(src_ids, tile_mask, grad_query, cot, zvalue, w_q, w_n2, w_n1, sides, group=4):
    blocks, tiles, blk, _ = tile_mask.shape
    width = grad_query.shape[-1]
    rows = pl.BlockSpec((group * blk, width), lambda i, ids: (i, 0))
    return pl.pallas_call(
        functools.partial(scatter_kernel, group),
        grid_spec=pltpu.PrefetchScalarGridSpec(
            num_scalar_prefetch=1,
            grid=(blocks // group,),
            in_specs=[
                pl.BlockSpec((group, tiles, blk, blk), lambda i, ids: (i, 0, 0, 0)),
                rows,
                rows,
                rows,
                pl.BlockSpec(w_q.shape, lambda i, ids: (0, 0)),
                pl.BlockSpec(w_n2.shape, lambda i, ids: (0, 0)),
                pl.BlockSpec(w_n1.shape, lambda i, ids: (0, 0)),
            ],
            out_specs=[rows]
            + [pl.BlockSpec((blocks, blk, width), lambda i, ids: (0, 0, 0))] * sides,
            scratch_shapes=[pltpu.VMEM((sides * blocks, blk, width), jnp.float32)],
        ),
        out_shape=[jax.ShapeDtypeStruct((blocks * blk, width), jnp.float32)]
        + [jax.ShapeDtypeStruct((blocks, blk, width), jnp.float32)]
        + [jax.ShapeDtypeStruct((blocks, blk, width), jnp.bfloat16)] * (sides - 1),
        compiler_params=pltpu.CompilerParams(dimension_semantics=("arbitrary",)),
    )(src_ids, tile_mask, grad_query, cot, zvalue, w_q, w_n2, w_n1)


def attend_kernel(scale, live_ref, q_ref, go_ref, kv_ref, wkv_ref, gq_ref, slots_ref, gk_acc, gv_acc):
    step = pl.program_id(0)
    width = q_ref.shape[1]

    @pl.when(step == 0)
    def _():
        gk_acc[...] = jnp.zeros(gk_acc.shape, jnp.float32)
        gv_acc[...] = jnp.zeros(gv_acc.shape, jnp.float32)

    queries = q_ref[...]
    grad_out = go_ref[...]
    keys = kv_ref[:, 0:width]
    values = kv_ref[:, width : 2 * width]
    nt = (((1,), (1,)), ((), ()))
    tn = (((0,), (0,)), ((), ()))
    scores = lax.dot_general(queries, keys, nt, preferred_element_type=jnp.float32) * scale
    scores = jnp.where(live_ref[...] > 0, scores, -jnp.inf)
    highest = jnp.max(scores, axis=1, keepdims=True)
    expo_terms = jnp.exp(scores - highest)
    probability = expo_terms / jnp.sum(expo_terms, axis=1, keepdims=True)
    prob_low = probability.astype(jnp.bfloat16)
    grad_prob = lax.dot_general(grad_out, values, nt, preferred_element_type=jnp.float32)
    spread = jnp.sum(probability * grad_prob, axis=1, keepdims=True)
    grad_score = (probability * (grad_prob - spread) * scale).astype(jnp.bfloat16)
    gq_ref[...] = jnp.dot(grad_score, keys, preferred_element_type=jnp.float32).astype(gq_ref.dtype)
    gk_acc[...] += lax.dot_general(grad_score, queries, tn, preferred_element_type=jnp.float32)
    gv_acc[...] += lax.dot_general(prob_low, grad_out, tn, preferred_element_type=jnp.float32)

    @pl.when(step == pl.num_programs(0) - 1)
    def _():
        grad_keys = gk_acc[...].astype(jnp.bfloat16)
        grad_vals = gv_acc[...].astype(jnp.bfloat16)
        slots = lax.dot_general(grad_keys, wkv_ref[:, 0:width], nt, preferred_element_type=jnp.float32)
        slots += lax.dot_general(grad_vals, wkv_ref[:, width : 2 * width], nt, preferred_element_type=jnp.float32)
        slots_ref[...] = slots.astype(slots_ref.dtype)


def attend_back(live, queries, grad_out, keyvals, w_kv, scale, rows_per_step=1024):
    rows, width = queries.shape
    slots = keyvals.shape[0]
    steps = rows // rows_per_step
    row_block = pl.BlockSpec((rows_per_step, width), lambda i: (i, 0))
    return pl.pallas_call(
        functools.partial(attend_kernel, scale),
        grid=(steps,),
        in_specs=[
            pl.BlockSpec((1, slots), lambda i: (0, 0)),
            row_block,
            row_block,
            pl.BlockSpec((slots, 2 * width), lambda i: (0, 0)),
            pl.BlockSpec(w_kv.shape, lambda i: (0, 0)),
        ],
        out_specs=[row_block, pl.BlockSpec((slots, width), lambda i: (0, 0))],
        out_shape=(
            jax.ShapeDtypeStruct((rows, width), jnp.bfloat16),
            jax.ShapeDtypeStruct((slots, width), jnp.bfloat16),
        ),
        scratch_shapes=[
            pltpu.VMEM((slots, width), jnp.float32),
            pltpu.VMEM((slots, width), jnp.float32),
        ],
        compiler_params=pltpu.CompilerParams(dimension_semantics=("arbitrary",)),
        cost_estimate=pl.CostEstimate(
            flops=10 * rows * slots * width,
            transcendentals=rows * slots,
            bytes_accessed=2 * (3 * rows * width + 4 * slots * width),
        ),
    )(live, queries, grad_out, keyvals, w_kv)


def slope_of(values):
    sigma = 1.0 / (1.0 + jnp.exp(-values))
    return sigma * (1.0 + values * (1.0 - sigma))


def edge_back_kernel(slope_ref, own_ref, a_ref, b_ref, c_ref, d_ref, gn_ref, w1_ref, w2_ref, out_ref):
    nt = (((1,), (1,)), ((), ()))
    collected = own_ref[...]
    for ref in (a_ref, b_ref, c_ref, d_ref):
        collected = collected + ref[...].astype(jnp.float32)
    grad_msg = collected.astype(jnp.bfloat16)
    grad_pre = lax.dot_general(grad_msg, w2_ref[...], nt, preferred_element_type=jnp.float32)
    grad_pre = (grad_pre * slope_ref[...]).astype(jnp.bfloat16)
    total = gn_ref[...] + lax.dot_general(grad_pre, w1_ref[...], nt, preferred_element_type=jnp.float32)
    out_ref[...] = total.astype(out_ref.dtype)


def edge_back(edge_slope, own_part, received, grad_node, w_e1, w_e2, rows_per_step=1024):
    rows, width = edge_slope.shape
    row_block = pl.BlockSpec((rows_per_step, width), lambda i: (i, 0))
    weight = pl.BlockSpec(w_e1.shape, lambda i: (0, 0))
    return pl.pallas_call(
        edge_back_kernel,
        grid=(rows // rows_per_step,),
        in_specs=[row_block] * (3 + len(received)) + [weight, weight],
        out_specs=row_block,
        out_shape=jax.ShapeDtypeStruct((rows, width), jnp.bfloat16),
        cost_estimate=pl.CostEstimate(
            flops=6 * rows * width * width,
            transcendentals=rows * width,
            bytes_accessed=rows * width * (4 + 4 + 2 * len(received) + 4 + 2),
        ),
    )(edge_slope, own_part, *received, grad_node, w_e1, w_e2)


def dense(left, right):
    return jnp.dot(left, right, preferred_element_type=jnp.float32)


def silu_slope(values):
    sigma = jax.nn.sigmoid(values)
    return sigma * (1.0 + values * (1.0 - sigma))


def on_device(
    nodes, tile_src, tile_mask, tokens, tok_count, w_e1, w_e2, w_n1, w_n2, w_q, w_kv, w_o, cotangent
):
    latent = nodes[0, 0]
    node_rows = latent.shape[0]
    latent_width = latent.shape[1]
    block_count = tile_src.shape[2]
    tile_count = tile_src.shape[3]
    blk_rows = tile_mask.shape[-1]
    rows_px = lax.axis_size("px")
    rows_py = lax.axis_size("py")
    devices = rows_px * rows_py
    score_scale = 1.0 / math.sqrt(latent_width)
    pre_act = dense(latent, w_e1)
    activation = jax.nn.silu(pre_act).astype(jnp.bfloat16)
    message = dense(activation, w_e2).astype(jnp.bfloat16)
    sources = [
        message,
        passed_along(message, "px", 1),
        passed_along(message, "px", -1),
        passed_along(message, "py", 1),
        passed_along(message, "py", -1),
    ]
    src_ids = tile_src[0, 0].reshape(-1)
    zvalue, queries = tile_gather(
        src_ids,
        tile_mask[0, 0],
        [part.reshape(block_count, blk_rows, latent_width) for part in sources],
        latent,
        w_n1,
        w_n2,
        w_q,
    )
    own_tokens = tokens[0]
    slot_count = own_tokens.shape[0] // devices
    token_groups = own_tokens.reshape(devices, slot_count, latent_width)
    arrived_tokens = lax.all_to_all(
        token_groups, ("px", "py"), split_axis=0, concat_axis=0, tiled=True
    )
    arrived_tokens = arrived_tokens.reshape(devices * slot_count, latent_width)
    arrived = dense(arrived_tokens, w_kv).astype(jnp.bfloat16)
    live_keys = (jnp.arange(slot_count)[None, :] < tok_count[:, 0][:, None]).reshape(1, -1)
    grad_out = dense(cotangent[0, 0], w_o.T).astype(jnp.bfloat16)
    grad_query, grad_slots = attend_back(
        live_keys.astype(jnp.float32), queries, grad_out, arrived, w_kv, score_scale
    )
    returned = lax.all_to_all(
        grad_slots.reshape(devices, slot_count, latent_width),
        ("px", "py"),
        split_axis=0,
        concat_axis=0,
        tiled=True,
    )
    grad_tokens = returned.reshape(devices * slot_count, latent_width)
    grad_node, own_part, *outbound = tile_scatter(
        src_ids, tile_mask[0, 0], grad_query, cotangent[0, 0], zvalue, w_q, w_n2, w_n1, len(sources)
    )
    outbound = [part.reshape(node_rows, latent_width) for part in outbound]
    received = [
        passed_along(outbound[0], "px", -1),
        passed_along(outbound[1], "px", 1),
        passed_along(outbound[2], "py", -1),
        passed_along(outbound[3], "py", 1),
    ]
    late_pre_act, own_part = lax.optimization_barrier((pre_act, own_part))
    edge_slope = silu_slope(late_pre_act)
    grad_nodes = edge_back(
        edge_slope, own_part.reshape(node_rows, latent_width), received, grad_node, w_e1, w_e2
    )
    return (grad_nodes[None, None], grad_tokens[None])


def solution(mesh):
    return jax.shard_map(
        on_device,
        mesh=mesh,
        in_specs=(
            P("px", "py", None, None),
            P("px", "py", None, None),
            P("px", "py", None, None, None, None),
            P(("px", "py"), None, None),
            P(None, ("px", "py")),
            P(),
            P(),
            P(),
            P(),
            P(),
            P(),
            P(),
            P("px", "py", None, None),
        ),
        out_specs=(P("px", "py", None, None), P(("px", "py"), None, None)),
        check_vma=False,
    )
```
